32 devices in a mesh: expert: 16 (over z, y, x), shard: 2 (over core).
Axes of the slice: x: 2, y: 2, z: 4, core: 2. Of those that a mesh axis runs over, the one named last changes fastest.
Arguments:
- tokens_in: bfloat16 [4096, 2048], P(('expert', 'shard'))
- cotangent: bfloat16 [4096, 2048], P(('expert', 'shard')), may hold values from -6 to 6
- expert_ids: int32 [4096, 6], P(('expert', 'shard')), may hold values from 0 to 15, all different within a row; in each aligned block of 128 rows (0 to 127, 128 to 255, ...) at most 64 rows name the same one
- attention_gain: bfloat16 [2048], P(('expert', 'shard')), may hold values from 0.5 to 1.5
- query_weight: bfloat16 [2048, 3072], P(('expert', 'shard')), may hold values from -0.25 to 0.25
- latent_down: bfloat16 [2048, 576], P(('expert', 'shard')), may hold values from -0.125 to 0.125
- latent_gain: bfloat16 [512], P(('expert', 'shard')), may hold values from 0.5 to 1.5
- latent_up: bfloat16 [512, 4096], P(('expert', 'shard')), may hold values from -0.25 to 0.25
- output_weight: bfloat16 [2048, 2048], P(None, ('expert', 'shard')), may hold values from -0.375 to 0.375
- feedforward_gain: bfloat16 [2048], P(('expert', 'shard')), may hold values from 0.5 to 1.5
- router_weight: bfloat16 [2048, 16], P(('expert', 'shard')), may hold values from -0.0625 to 0.0625
- shared_inner: bfloat16 [2, 2048, 2816], P(None, ('expert', 'shard')), may hold values from -0.125 to 0.125
- shared_outer: bfloat16 [2816, 2048], P(None, ('expert', 'shard')), may hold values from -0.109375 to 0.109375
- expert_inner: bfloat16 [16, 2, 2048, 1408], P('expert', None, None, 'shard'), may hold values from -0.125 to 0.125
- expert_outer: bfloat16 [16, 1408, 2048], P('expert', 'shard'), may hold values from -3.5 to 3.5
Outputs:
- layer_output: bfloat16 [4096, 2048], P(('expert', 'shard'))
- input_gradient: bfloat16 [4096, 2048], P(('expert', 'shard'))
- attention_gain_delta: float32 [2048], P(('expert', 'shard'))
- query_delta: float32 [2048, 3072], P(('expert', 'shard'))
- latent_down_delta: float32 [2048, 576], P(('expert', 'shard'))
- latent_gain_delta: float32 [512], P(('expert', 'shard'))
- latent_up_delta: float32 [512, 4096], P(('expert', 'shard'))
- output_delta: float32 [2048, 2048], P(None, ('expert', 'shard'))
- feedforward_gain_delta: float32 [2048], P(('expert', 'shard'))
- router_delta: float32 [2048, 16], P(('expert', 'shard'))
- shared_inner_delta: float32 [2, 2048, 2816], P(None, ('expert', 'shard'))
- shared_outer_delta: float32 [2816, 2048], P(None, ('expert', 'shard'))
- expert_inner_delta: float32 [16, 2, 2048, 1408], P('expert', None, None, 'shard')
- expert_outer_delta: float32 [16, 1408, 2048], P('expert', 'shard')
- statistics: float32 [3], replicated
The draws below stay inside these ranges and needn't reach their ends.
Inputs may be any that keep to these rules, and one draw needn't show every extreme that they name: `expert_ids`: each row names 6 different experts. In each aligned block of 128 rows (the rows of one device) no expert is named by more than 64 rows, a bound that some block reaches.
All inputs are finite; a program needn't handle non-finite values.
Results may differ from the reference program's by a relative error of at most 0.02.
Values may be sent and summed in bfloat16 or wider, within the bound.
No kernel may reach another device: no remote copies, remote signals or barrier semaphores. Data moves between devices by JAX's collectives and lax.ppermute only.
A program may use at most 448 MiB of HBM per device.

```python
import math
import jax
import jax.numpy as jnp
import numpy as np
from jax import lax

D = 2048
H = 16
DN = 128
DR = 64
DV = 128
KVR = 512
FF = 1408
SFF = 2816
TOPK = 6
TOK_DEV = 128
CL = 64
EXPERTS = 16
CAP = 64
TOKENS = 4096
N_EXPERT = 16
N_SHARD = 2


def draw_tokens_in(key, part):
    block_index = jnp.arange(TOKENS, dtype=jnp.int32) // TOK_DEV
    blocks = TOKENS // TOK_DEV
    fraction = block_index.astype(jnp.float32) / max(blocks - 1, 1)
    basic_draw = jax.random.normal(key, (TOKENS, D), jnp.float32)
    row_scale = 0.6 + 0.8 * fraction
    return (basic_draw * row_scale[:, None]).astype(jnp.bfloat16)


def shard_levels(rng, dims, split, low, high):
    factor_of = 1.0
    for axis_at, shards_of in split:
        draws = jax.random.uniform(jax.random.fold_in(jax.random.fold_in(rng, 6), axis_at), (shards_of,), jnp.float32, low / len(split), high / len(split))
        factor_of = factor_of * jnp.repeat(jnp.exp(draws), dims[axis_at] // shards_of).reshape((-1,) + (1,) * (len(dims) - 1 - axis_at))
    return factor_of


def assign_block(own_key, own, number, rows, number_of, top, reach, skew):
    ranking = jax.random.permutation(own_key, number_of)
    crowded, usual = load_shares(number_of, rows * top, reach, skew, True), load_shares(number_of, rows * top, reach, skew, False)
    places = jnp.arange(number_of)

    def named(sizes, turn):
        used = int((sizes > 0).sum())
        fixed = max(1, used // 4)
        passed = fixed + (places - fixed + turn * (used - fixed)) % max(1, number_of - fixed)
        return jnp.zeros((number_of,), jnp.int32).at[ranking[jnp.where(places < fixed, places, passed)]].set(jnp.asarray(sizes, jnp.int32))

    sizes = jnp.where(number % 4 == 0, named(crowded, number // 4), named(usual, number - number // 4 - 1))
    mixed = jax.random.permutation(jax.random.fold_in(own, 3), number_of)
    donor, taker = mixed[0:number_of // 2 * 2:2], mixed[1:number_of // 2 * 2:2]
    margin = jnp.minimum(sizes[donor] - 1, reach - sizes[taker]) // 2
    margin = jnp.where((donor == ranking[0]) | (taker == ranking[0]) | (sizes[taker] == 0), 0, jnp.maximum(margin, 0))
    passed = jax.random.randint(jax.random.fold_in(own, 4), (number_of // 2,), 0, 1 << 20) % (margin + 1)
    sizes = sizes.at[donor].add(-passed).at[taker].add(passed)
    items = jnp.searchsorted(jnp.cumsum(sizes), jnp.arange(rows * top), side="right").astype(jnp.int32)
    table = items.reshape(top, rows).T
    table = table[jax.random.permutation(jax.random.fold_in(own, 1), rows)]
    turn = jax.random.randint(jax.random.fold_in(own, 2), (rows, 1), 0, top)
    return jnp.take_along_axis(table, (jnp.arange(top)[None, :] + turn) % top, axis=1)


def load_shares(number_of, total, bound, skew, full):
    portions = [(1 << 20) // math.isqrt(grade ** skew) + 1 for grade in range(1, number_of + 1)]
    largest = bound if full else min(bound, max(-(-total // number_of), total * portions[0] // sum(portions)))
    least = 1 if total - largest >= number_of - 1 else 0
    counts, surplus = [largest] + [least] * (number_of - 1), total - largest - least * (number_of - 1)
    while surplus > 0:
        candidates = [i for i in range(1, number_of) if counts[i] < largest] or [i for i in range(1, number_of) if counts[i] < bound]
        mass, left = sum([portions[i] for i in candidates]), surplus
        for i in candidates:
            extra = min(bound - counts[i], max(1, left * portions[i] // mass), surplus)
            counts[i] = counts[i] + extra
            surplus = surplus - extra
    return np.array(counts)


def normal_values(rng, dims, spread, bound, pieces=(), kind=jnp.bfloat16):
    drawn = spread * jax.random.normal(rng, dims, jnp.float32)
    if pieces:
        drawn = drawn * shard_levels(rng, dims, pieces, -0.22, 0.18)
    return jnp.clip(drawn, -bound, bound).astype(kind)


def setup_inputs(seed: int = 0) -> dict:
    splits = jax.random.split(jax.random.key(seed), 16)
    tokens_in = draw_tokens_in(jax.random.fold_in(splits[15], 71), 0)
    cotangent = normal_values(splits[1], (TOKENS, D), 1.0, 6.0, ((0, 32),))
    expert_ids_keys = jax.random.split(jax.random.fold_in(splits[2], 1), TOKENS // TOK_DEV)
    expert_ids_turns = jax.random.permutation(jax.random.fold_in(splits[2], 3), TOKENS // TOK_DEV)
    expert_ids = jax.vmap(lambda own, number: assign_block(jax.random.fold_in(splits[2], 2), own, number, TOK_DEV, EXPERTS, TOPK, CAP, 2))(expert_ids_keys, expert_ids_turns).reshape((TOKENS, TOPK))
    attention_gain = jnp.clip(1.0 + 0.1 * jax.random.normal(splits[3], (D,), jnp.float32), 0.5, 1.5).astype(jnp.bfloat16)
    query_weight = normal_values(splits[4], (D, H * (DN + DR)), (D // 4) ** -0.5, 0.25, ((0, 32),))
    latent_down = normal_values(splits[5], (D, KVR + DR), D ** -0.5, 0.125, ((0, 32),))
    latent_gain = jnp.clip(1.0 + 0.1 * jax.random.normal(splits[6], (KVR,), jnp.float32), 0.5, 1.5).astype(jnp.bfloat16)
    latent_up = normal_values(splits[7], (KVR, H * (DN + DV)), KVR ** -0.5, 0.25, ((0, 32),))
    output_weight = normal_values(splits[8], (H * DV, D), (H * DV // 8) ** -0.5, 0.375, ((1, 32),))
    feedforward_gain = jnp.clip(1.0 + 0.1 * jax.random.normal(splits[9], (D,), jnp.float32), 0.5, 1.5).astype(jnp.bfloat16)
    router_weight = normal_values(splits[10], (D, EXPERTS), (4 * D) ** -0.5, 0.0625, ((0, 32),))
    shared_inner = normal_values(splits[11], (2, D, SFF), D ** -0.5, 0.125, ((1, 32),))
    shared_outer = normal_values(splits[12], (SFF, D), SFF ** -0.5, 0.109375, ((1, 32),))
    expert_inner = normal_values(splits[13], (EXPERTS, 2, D, FF), D ** -0.5, 0.125, ((0, 16), (3, 2)))
    expert_outer = normal_values(splits[14], (EXPERTS, FF, D), (FF * EXPERTS // 8192 + 1) ** -0.5, 3.5, ((0, 16), (1, 2)))
    return {"tokens_in": tokens_in, "cotangent": cotangent, "expert_ids": expert_ids, "attention_gain": attention_gain, "query_weight": query_weight, "latent_down": latent_down, "latent_gain": latent_gain, "latent_up": latent_up, "output_weight": output_weight, "feedforward_gain": feedforward_gain, "router_weight": router_weight, "shared_inner": shared_inner, "shared_outer": shared_outer, "expert_inner": expert_inner, "expert_outer": expert_outer}


@jax.custom_vjp
def low(v):
    return lax.optimization_barrier(v.astype(jnp.bfloat16)).astype(jnp.float32)

@jax.custom_vjp
def low_back(v):
    return v

def low_keep(v):
    return (low(v), None)

def low_pass(kept, grad):
    return (grad,)

def back_keep(v):
    return (v, None)

def back_low(kept, grad):
    return (low(grad),)
low.defvjp(low_keep, low_pass)
low_back.defvjp(back_keep, back_low)
EPSILON = 1e-06
THETA = 10000.0

def highest(left_side, right_side):
    return jnp.dot(left_side, right_side, precision=lax.Precision.HIGHEST, preferred_element_type=jnp.float32)

def norm_rows(values, gain_vector):
    return values * lax.rsqrt(lax.optimization_barrier(jnp.mean(values * values, axis=-1, keepdims=True)) + EPSILON) * gain_vector

def rotate(values, cosine_table, sine_table):
    middle = values.shape[-1] // 2
    first_half = values[..., :middle]
    second_half = values[..., middle:]
    return jnp.concatenate([first_half * cosine_table - second_half * sine_table, second_half * cosine_table + first_half * sine_table], axis=-1)

def angles(positions):
    inverse = THETA ** (-jnp.arange(DR // 2, dtype=jnp.float32) * 2.0 / DR)
    phases = positions.astype(jnp.float32)[:, None] * inverse[None, :]
    return (jnp.cos(phases), jnp.sin(phases))

def gated(inner_out):
    return jax.nn.silu(inner_out[..., 0, :]) * inner_out[..., 1, :]

def token_positions():
    ordinal = jnp.arange(TOKENS, dtype=jnp.int32)
    within = ordinal % TOK_DEV
    block_side = ordinal // TOK_DEV % 2
    return jnp.where(block_side == 0, within, TOK_DEV + within % CL)

def group_mask():
    ordinal = jnp.arange(2 * TOK_DEV, dtype=jnp.int32)
    query_place = ordinal[:, None]
    key_place = ordinal[None, :]
    prompt_key = key_place < TOK_DEV
    later_query = query_place >= TOK_DEV
    causal = key_place <= query_place
    same_block = (query_place - TOK_DEV) // CL == (key_place - TOK_DEV) // CL
    return jnp.where(prompt_key, later_query | causal, later_query & causal & same_block)

def group_attention(queries, key_plain, values, key_rotary):
    factor = (DN + DR) ** (-0.5)
    plain_part = jnp.einsum('qhd,khd->hqk', queries[..., :DN], key_plain, precision=lax.Precision.HIGHEST)
    rotary_part = jnp.einsum('qhr,kr->hqk', queries[..., DN:], key_rotary, precision=lax.Precision.HIGHEST)
    scores = low_back((plain_part + rotary_part) * factor)
    scores = jnp.where(group_mask()[None], scores, -1e+30)
    weights = low(jax.nn.softmax(scores, axis=-1))
    return jnp.einsum('hqk,khd->qhd', weights, values, precision=lax.Precision.HIGHEST)

def attend_group(members):
    return jax.checkpoint(group_attention)(members[0], members[1], members[2], members[3])

def expert_block(rows_in, inner_weight, outer_weight):
    inner_out = low_back(jnp.einsum('rd,gdf->rgf', rows_in, inner_weight, precision=lax.Precision.HIGHEST))
    hidden = low(gated(inner_out))
    return low(low_back(highest(hidden, outer_weight)))

def run_expert(members):
    return jax.checkpoint(expert_block)(members[0], members[1], members[2])

def slot_positions(expert_ids):
    devices_all = N_EXPERT * N_SHARD
    device_ids = expert_ids.reshape(devices_all, TOK_DEV * TOPK)
    matches = (device_ids[..., None] == jnp.arange(EXPERTS, dtype=jnp.int32)).astype(jnp.int32)
    slot_rank = lax.optimization_barrier(jnp.sum((jnp.cumsum(matches, axis=1) - matches) * matches, axis=-1))
    device_place = jnp.arange(devices_all, dtype=jnp.int32)[:, None]
    slot_index = device_ids * (devices_all * CAP) + device_place * CAP + slot_rank
    return slot_index.reshape(TOKENS, TOPK)

def layer(params, tokens_float, expert_ids):
    attention_gain, query_weight, latent_down, latent_gain, latent_up, output_weight, feedforward_gain, router_weight, shared_inner, shared_outer, expert_inner, expert_outer = params
    devices_all = N_EXPERT * N_SHARD
    cosine_table, sine_table = angles(token_positions())
    normed_one = low(norm_rows(tokens_float, attention_gain))
    query_raw = low_back(highest(normed_one, query_weight)).reshape(TOKENS, H, DN + DR)
    queries = low(jnp.concatenate([query_raw[..., :DN], rotate(query_raw[..., DN:], cosine_table[:, None, :], sine_table[:, None, :])], axis=-1))
    down_out = low_back(highest(normed_one, latent_down))
    latents = low(norm_rows(down_out[:, :KVR], latent_gain))
    key_rotary = low(rotate(down_out[:, KVR:], cosine_table, sine_table))
    expanded = low(low_back(highest(latents, latent_up))).reshape(TOKENS, H, DN + DV)
    groups = TOKENS // (2 * TOK_DEV)
    grouped = (queries.reshape(groups, 2 * TOK_DEV, H, DN + DR), expanded[..., :DN].reshape(groups, 2 * TOK_DEV, H, DN), expanded[..., DN:].reshape(groups, 2 * TOK_DEV, H, DV), key_rotary.reshape(groups, 2 * TOK_DEV, DR))
    attended = lax.map(attend_group, grouped)
    mixed_heads = low(low_back(attended.reshape(TOKENS, H * DV)))
    attention_out = low_back(highest(mixed_heads, output_weight))
    residual = tokens_float + attention_out
    normed_two = low(norm_rows(residual, feedforward_gain))
    logits = low_back(highest(normed_two, router_weight))
    route_probs = jax.nn.softmax(logits, axis=-1)
    gate_values = jnp.take_along_axis(route_probs, expert_ids, axis=1)
    slot_index = slot_positions(expert_ids)
    slot_token = jnp.full((EXPERTS * devices_all * CAP,), TOKENS, jnp.int32).at[slot_index.reshape(-1)].set(jnp.arange(TOKENS * TOPK, dtype=jnp.int32) // TOPK)
    padded = jnp.concatenate([normed_two, jnp.zeros((1, D), normed_two.dtype)], axis=0)
    expert_rows = low_back(jnp.take(padded, slot_token, axis=0)).reshape(EXPERTS, devices_all * CAP, D)
    expert_outs = lax.map(run_expert, (expert_rows, expert_inner, expert_outer))
    picked = jnp.take(expert_outs.reshape(-1, D), slot_index.reshape(-1), axis=0).reshape(TOKENS, TOPK, D)
    routed = lax.optimization_barrier(jnp.sum(gate_values[..., None] * picked, axis=1))
    shared_pre = low_back(jnp.einsum('td,gdf->tgf', normed_two, shared_inner, precision=lax.Precision.HIGHEST))
    shared_result = low_back(highest(low(gated(shared_pre)), shared_outer))
    feedforward = routed + shared_result
    result = residual + feedforward
    square_sums = jnp.stack([jnp.sum(residual * residual), jnp.sum(attention_out * attention_out), jnp.sum(feedforward * feedforward)])
    return (result, square_sums)

def reference(tokens_in, cotangent, expert_ids, attention_gain, query_weight, latent_down, latent_gain, latent_up, output_weight, feedforward_gain, router_weight, shared_inner, shared_outer, expert_inner, expert_outer):
    params = jax.tree.map(lambda weight: weight.astype(jnp.float32), (attention_gain, query_weight, latent_down, latent_gain, latent_up, output_weight, feedforward_gain, router_weight, shared_inner, shared_outer, expert_inner, expert_outer))

    def closed(weights, tokens_float):
        return layer(weights, tokens_float, expert_ids)
    result, pullback, square_sums = jax.vjp(closed, params, tokens_in.astype(jnp.float32), has_aux=True)
    weight_deltas, input_delta = pullback(cotangent.astype(jnp.float32))
    statistics = jnp.sqrt(square_sums / (TOKENS * D))
    return (result.astype(jnp.bfloat16), input_delta.astype(jnp.bfloat16), weight_deltas[0], weight_deltas[1], weight_deltas[2], weight_deltas[3], weight_deltas[4], weight_deltas[5], weight_deltas[6], weight_deltas[7], weight_deltas[8], weight_deltas[9], weight_deltas[10], weight_deltas[11], statistics)
```

```python
import jax
import jax.numpy as jnp
from jax import lax
from jax.sharding import PartitionSpec as P

D = 2048
H = 16
DN = 128
DR = 64
DV = 128
KVR = 512
TOPK = 6
CL = 64

ALL = ("expert", "shard")
EPSILON = 1e-06
THETA = 10000.0
ALIGN = 8192
ROW = 1024


def passed_along(value, axis, steps):
    count = lax.axis_size(axis)
    first, last = (max(0, -steps), min(count, count - steps))
    return lax.ppermute(value, axis, [(source, source + steps) for source in range(first, last)])


def matmul(left_side, right_side):
    return jnp.dot(left_side, right_side, preferred_element_type=jnp.float32)


def norm_rows(values, gain_vector):
    return (
        values
        * lax.rsqrt(jnp.mean(values * values, axis=-1, keepdims=True) + EPSILON)
        * gain_vector
    )


def rotate(values, cosine_table, sine_table):
    middle = values.shape[-1] // 2
    first_half = values[..., :middle]
    second_half = values[..., middle:]
    return jnp.concatenate(
        [
            first_half * cosine_table - second_half * sine_table,
            second_half * cosine_table + first_half * sine_table,
        ],
        axis=-1,
    )


def angles(positions):
    inverse = THETA ** (-jnp.arange(DR // 2, dtype=jnp.float32) * 2.0 / DR)
    phases = positions.astype(jnp.float32)[:, None] * inverse[None, :]
    return (jnp.cos(phases), jnp.sin(phases))


def gated(inner_out):
    return jax.nn.silu(inner_out[..., 0, :]) * inner_out[..., 1, :]


def masked_scores(queries, key_rows, rotary_rows, visible):
    factor = (DN + DR) ** (-0.5)
    plain_part = jnp.einsum(
        "qhd,khd->hqk", queries[..., :DN], key_rows[..., :DN], preferred_element_type=jnp.float32
    )
    rotary_part = jnp.einsum(
        "qhr,kr->hqk", queries[..., DN:], rotary_rows, preferred_element_type=jnp.float32
    )
    return jnp.where(visible[None], (plain_part + rotary_part) * factor, -1e30)


def flat_pack(parts):
    flats = [part.reshape(part.shape[0], -1) for part in parts]
    sizes = [flat.shape[1] for flat in flats]
    pad = (-sum(sizes)) % ALIGN
    if pad:
        flats.append(jnp.zeros((flats[0].shape[0], pad), flats[0].dtype))
    return jnp.concatenate(flats, axis=1), sizes


def flat_unpack(packed, sizes, shapes):
    pieces = []
    offset = 0
    for size, shape in zip(sizes, shapes):
        pieces.append(packed[:, offset : offset + size].reshape((packed.shape[0],) + shape))
        offset += size
    return pieces


def gather_packed(parts, axis):
    packed, sizes = flat_pack([part[None] for part in parts])
    gathered = lax.all_gather(packed[0], axis, axis=0, tiled=False)
    return flat_unpack(gathered, sizes, [part.shape for part in parts])


def scatter_packed(parts, axis, count):
    packed, sizes = flat_pack([part.reshape((count, -1)) for part in parts])
    rows = packed.reshape(-1, ROW)
    local = lax.psum_scatter(rows, axis, scatter_dimension=0, tiled=True).reshape(1, -1)
    shapes = [(part.shape[0] // count,) + part.shape[1:] for part in parts]
    return [piece[0] for piece in flat_unpack(local, sizes, shapes)]


def shards(
    tokens_in,
    cotangent,
    expert_ids,
    attention_gain,
    query_weight,
    latent_down,
    latent_gain,
    latent_up,
    output_weight,
    feedforward_gain,
    router_weight,
    shared_inner,
    shared_outer,
    expert_inner,
    expert_outer,
):
    tok_rows = tokens_in.shape[0]
    experts_all = lax.axis_size("expert")
    shard_count = lax.axis_size("shard")
    devices = experts_all * shard_count
    slot_cap = tok_rows * TOPK * 4 // (3 * experts_all)
    factor = (DN + DR) ** (-0.5)
    side_index = lax.axis_index("shard")
    ordinal = jnp.arange(tok_rows, dtype=jnp.int32)
    positions = jnp.where(side_index == 0, ordinal, tok_rows + ordinal % CL)
    cosine_table, sine_table = angles(positions)
    query_place = ordinal[:, None]
    key_place = ordinal[None, :]
    causal = key_place <= query_place
    same_block = query_place // CL == key_place // CL
    local_mask = jnp.where(side_index == 0, causal, causal & same_block)
    remote_mask = jnp.broadcast_to(side_index == 1, (tok_rows, tok_rows))
    visible = jnp.concatenate([remote_mask, local_mask], axis=1)

    q_g, down_g, up_g, out_t_g, gain_one_g, gain_latent_g = gather_packed(
        [query_weight, latent_down, latent_up, output_weight.T, attention_gain, latent_gain], ALL
    )
    query_full = q_g.reshape(-1, q_g.shape[-1])
    down_full = down_g.reshape(-1, down_g.shape[-1])
    up_full = up_g.reshape(-1, up_g.shape[-1])
    output_t_full = out_t_g.reshape(-1, out_t_g.shape[-1])
    gain_one_float = gain_one_g.reshape(-1).astype(jnp.float32)
    gain_latent_float = gain_latent_g.reshape(-1).astype(jnp.float32)

    si_g, so_t_g, router_g, gain_two_g = gather_packed(
        [jnp.transpose(shared_inner, (1, 0, 2)), shared_outer.T, router_weight, feedforward_gain],
        ALL,
    )
    shared_in_full = si_g.reshape((-1,) + si_g.shape[2:])
    shared_out_t_full = so_t_g.reshape(-1, so_t_g.shape[-1])
    router_full = router_g.reshape(-1, router_g.shape[-1])
    gain_two_float = gain_two_g.reshape(-1).astype(jnp.float32)

    ei_g, eo_g = gather_packed([expert_inner[0], expert_outer[0]], "shard")
    inner_halves = ei_g
    outer_matrix = eo_g.reshape(-1, eo_g.shape[-1])

    tokens_float = tokens_in.astype(jnp.float32)
    normed_one = norm_rows(tokens_float, gain_one_float).astype(jnp.bfloat16)
    query_raw = matmul(normed_one, query_full).reshape(tok_rows, H, DN + DR)
    queries = jnp.concatenate(
        [
            query_raw[..., :DN],
            rotate(query_raw[..., DN:], cosine_table[:, None, :], sine_table[:, None, :]),
        ],
        axis=-1,
    ).astype(jnp.bfloat16)
    down_out = matmul(normed_one, down_full)
    latent_raw = down_out[:, :KVR]
    latents = norm_rows(latent_raw, gain_latent_float).astype(jnp.bfloat16)
    key_rotary = rotate(down_out[:, KVR:], cosine_table, sine_table).astype(jnp.bfloat16)
    expanded = matmul(latents, up_full).astype(jnp.bfloat16).reshape(tok_rows, H, DN + DV)
    kv_local = jnp.concatenate([expanded.reshape(tok_rows, -1), key_rotary], axis=1)
    kv_remote = passed_along(kv_local, "shard", 1)
    remote_expanded = kv_remote[:, : H * (DN + DV)].reshape(tok_rows, H, DN + DV)
    remote_rotary = kv_remote[:, H * (DN + DV) :]
    key_rows = jnp.concatenate([remote_expanded, expanded], axis=0)
    rotary_rows = jnp.concatenate([remote_rotary, key_rotary], axis=0)
    scores = masked_scores(queries, key_rows, rotary_rows, visible)
    score_max = jnp.max(scores, axis=-1, keepdims=True)
    log_total = score_max + jnp.log(jnp.sum(jnp.exp(scores - score_max), axis=-1, keepdims=True))
    weights_float = jnp.exp(scores - log_total)
    weights_low = weights_float.astype(jnp.bfloat16)
    mixed_heads = (
        jnp.einsum(
            "hqk,khd->qhd", weights_low, key_rows[..., DN:], preferred_element_type=jnp.float32
        )
        .astype(jnp.bfloat16)
        .reshape(tok_rows, H * DV)
    )
    attention_out = jnp.einsum(
        "tc,dc->td", mixed_heads, output_t_full, preferred_element_type=jnp.float32
    )
    residual = tokens_float + attention_out
    normed_two = norm_rows(residual, gain_two_float).astype(jnp.bfloat16)
    logits = matmul(normed_two, router_full)
    route_probs = jax.nn.softmax(logits, axis=-1)
    gate_values = jnp.take_along_axis(route_probs, expert_ids, axis=1)
    flat_experts = expert_ids.reshape(-1)
    expert_match = (
        flat_experts[:, None] == jnp.arange(experts_all, dtype=jnp.int32)[None, :]
    ).astype(jnp.int32)
    slot_rank = jnp.sum((jnp.cumsum(expert_match, axis=0) - expert_match) * expert_match, axis=1)
    pair_count = tok_rows * TOPK
    slot_of = flat_experts * slot_cap + slot_rank
    slot_pair = (
        jnp.full((experts_all * slot_cap,), pair_count, jnp.int32)
        .at[slot_of]
        .set(jnp.arange(pair_count, dtype=jnp.int32))
    )
    slot_token = slot_pair // TOPK
    delta_out = cotangent.astype(jnp.float32)
    padded_rows = jnp.concatenate([normed_two, jnp.zeros((1, D), jnp.bfloat16)], axis=0)
    send_rows = jnp.take(padded_rows, slot_token, axis=0)
    padded_gates = jnp.concatenate([gate_values.reshape(-1), jnp.zeros((1,), jnp.float32)])
    slot_gate = jnp.take(padded_gates, slot_pair, axis=0)
    padded_delta = jnp.concatenate([delta_out, jnp.zeros((1, D), jnp.float32)], axis=0)
    send_delta = (jnp.take(padded_delta, slot_token, axis=0) * slot_gate[:, None]).astype(
        jnp.bfloat16
    )
    outgoing = jnp.stack(
        [send_rows.reshape(experts_all, slot_cap, D), send_delta.reshape(experts_all, slot_cap, D)],
        axis=1,
    )
    incoming = lax.all_to_all(outgoing, "expert", split_axis=0, concat_axis=0, tiled=True)
    arrived = incoming[:, 0].reshape(-1, D)
    delta_arrived = incoming[:, 1].reshape(-1, D)

    expert_pre = jnp.einsum(
        "rd,sgdf->rgsf", arrived, inner_halves, preferred_element_type=jnp.float32
    ).reshape(arrived.shape[0], 2, -1)
    expert_hidden = gated(expert_pre).astype(jnp.bfloat16)
    expert_result = matmul(expert_hidden, outer_matrix).astype(jnp.bfloat16)
    delta_outer_matrix = jnp.einsum(
        "rf,rd->fd", expert_hidden, delta_arrived, preferred_element_type=jnp.float32
    )
    delta_expert_hidden = jnp.einsum(
        "rd,fd->rf", delta_arrived, outer_matrix, preferred_element_type=jnp.float32
    )
    unused_expert, expert_back = jax.vjp(gated, expert_pre)
    delta_expert_pre = expert_back(delta_expert_hidden)[0].astype(jnp.bfloat16)
    delta_pre_halves = delta_expert_pre.reshape(arrived.shape[0], 2, shard_count, -1)
    delta_inner_halves = jnp.einsum(
        "rd,rgsf->sgdf", arrived, delta_pre_halves, preferred_element_type=jnp.float32
    )
    delta_rows = jnp.einsum(
        "rgsf,sgdf->rd", delta_pre_halves, inner_halves, preferred_element_type=jnp.float32
    ).astype(jnp.bfloat16)
    delta_expert_inner, delta_expert_outer = scatter_packed(
        [
            delta_inner_halves.astype(jnp.bfloat16),
            delta_outer_matrix.astype(jnp.bfloat16).reshape(shard_count, -1, D),
        ],
        "shard",
        shard_count,
    )
    going_back = jnp.stack(
        [
            expert_result.reshape(experts_all, slot_cap, D),
            delta_rows.reshape(experts_all, slot_cap, D),
        ],
        axis=1,
    )
    coming_back = lax.all_to_all(going_back, "expert", split_axis=0, concat_axis=0, tiled=True)
    returned = coming_back[:, 0].reshape(-1, D)
    delta_returned = coming_back[:, 1].reshape(-1, D)

    picked = jnp.take(returned, slot_of, axis=0).reshape(tok_rows, TOPK, D).astype(jnp.float32)
    routed = jnp.sum(gate_values[..., None] * picked, axis=1)
    shared_pre = jnp.einsum(
        "td,dgf->tgf", normed_two, shared_in_full, preferred_element_type=jnp.float32
    )
    shared_hidden = gated(shared_pre).astype(jnp.bfloat16)
    shared_result = jnp.einsum(
        "tf,df->td", shared_hidden, shared_out_t_full, preferred_element_type=jnp.float32
    )
    feedforward = routed + shared_result
    layer_output = (residual + feedforward).astype(jnp.bfloat16)
    square_sums = lax.psum(
        jnp.stack(
            [
                jnp.sum(residual * residual),
                jnp.sum(attention_out * attention_out),
                jnp.sum(feedforward * feedforward),
            ]
        ),
        ALL,
    )
    statistics = jnp.sqrt(square_sums / (tok_rows * D * devices))

    delta_shared_outer_t = jnp.einsum(
        "td,tf->df", cotangent, shared_hidden, preferred_element_type=jnp.float32
    )
    delta_shared_hidden = jnp.einsum(
        "td,df->tf", cotangent, shared_out_t_full, preferred_element_type=jnp.float32
    )
    unused_shared, shared_back = jax.vjp(gated, shared_pre)
    delta_shared_pre = shared_back(delta_shared_hidden)[0].astype(jnp.bfloat16)
    delta_shared_inner_t = jnp.einsum(
        "td,tgf->dgf", normed_two, delta_shared_pre, preferred_element_type=jnp.float32
    )
    delta_normed = jnp.einsum(
        "tgf,dgf->td", delta_shared_pre, shared_in_full, preferred_element_type=jnp.float32
    )
    delta_gates = jnp.sum(delta_out[:, None, :] * picked, axis=-1)
    delta_normed = delta_normed + jnp.sum(
        jnp.take(delta_returned, slot_of, axis=0).reshape(tok_rows, TOPK, D).astype(jnp.float32),
        axis=1,
    )
    match_float = expert_match.reshape(tok_rows, TOPK, experts_all).astype(jnp.float32)
    delta_probs = jnp.einsum("tk,tke->te", delta_gates, match_float)
    delta_logits = (
        route_probs * (delta_probs - jnp.sum(route_probs * delta_probs, axis=-1, keepdims=True))
    ).astype(jnp.bfloat16)
    delta_router = jnp.einsum(
        "td,te->de", normed_two, delta_logits, preferred_element_type=jnp.float32
    )
    delta_normed = delta_normed + jnp.einsum(
        "te,de->td", delta_logits, router_full, preferred_element_type=jnp.float32
    )
    unused_second, second_back = jax.vjp(norm_rows, residual, gain_two_float)
    delta_residual_norm, delta_gain_two = second_back(delta_normed)
    delta_residual = delta_out + delta_residual_norm
    ffn_grads = scatter_packed(
        [
            delta_shared_inner_t.astype(jnp.bfloat16),
            delta_shared_outer_t.astype(jnp.bfloat16),
            delta_router.astype(jnp.bfloat16),
            delta_gain_two.astype(jnp.bfloat16),
        ],
        ALL,
        devices,
    )
    delta_shared_inner = jnp.transpose(ffn_grads[0], (1, 0, 2)).astype(jnp.float32)
    delta_shared_outer = ffn_grads[1].T.astype(jnp.float32)
    delta_router_local = ffn_grads[2].astype(jnp.float32)
    delta_gain_two_local = ffn_grads[3].astype(jnp.float32)

    delta_attention = delta_residual.astype(jnp.bfloat16)
    delta_output_t = jnp.einsum(
        "td,tc->dc", delta_attention, mixed_heads, preferred_element_type=jnp.float32
    )
    delta_mixed = (
        jnp.einsum("td,dc->tc", delta_attention, output_t_full, preferred_element_type=jnp.float32)
        .astype(jnp.bfloat16)
        .reshape(tok_rows, H, DV)
    )
    delta_weights = jnp.einsum(
        "qhd,khd->hqk", delta_mixed, key_rows[..., DN:], preferred_element_type=jnp.float32
    )
    delta_scores = (
        weights_float
        * (delta_weights - jnp.sum(weights_float * delta_weights, axis=-1, keepdims=True))
    ).astype(jnp.bfloat16)
    delta_values = jnp.einsum(
        "hqk,qhd->khd", weights_low, delta_mixed, preferred_element_type=jnp.float32
    )
    delta_query_plain = (
        jnp.einsum(
            "hqk,khd->qhd", delta_scores, key_rows[..., :DN], preferred_element_type=jnp.float32
        )
        * factor
    )
    delta_query_rotary = (
        jnp.einsum("hqk,kr->qhr", delta_scores, rotary_rows, preferred_element_type=jnp.float32)
        * factor
    )
    delta_key_plain = (
        jnp.einsum(
            "hqk,qhd->khd", delta_scores, queries[..., :DN], preferred_element_type=jnp.float32
        )
        * factor
    )
    delta_key_rotary = (
        jnp.einsum(
            "hqk,qhr->kr", delta_scores, queries[..., DN:], preferred_element_type=jnp.float32
        )
        * factor
    )
    delta_key_rows = jnp.concatenate([delta_key_plain, delta_values], axis=-1)
    back_local = jnp.concatenate(
        [delta_key_rows[:tok_rows].reshape(tok_rows, -1), delta_key_rotary[:tok_rows]], axis=1
    ).astype(jnp.bfloat16)
    back_remote = passed_along(back_local, "shard", -1).astype(jnp.float32)
    back_rows = back_remote[:, : H * (DN + DV)].reshape(tok_rows, H, DN + DV)
    back_rotary = back_remote[:, H * (DN + DV) :]
    delta_expanded = (
        (delta_key_rows[tok_rows:] + back_rows)
        .astype(jnp.bfloat16)
        .reshape(tok_rows, H * (DN + DV))
    )
    delta_rotary_total = delta_key_rotary[tok_rows:] + back_rotary
    delta_latent_up = jnp.einsum(
        "tl,tc->lc", latents, delta_expanded, preferred_element_type=jnp.float32
    )
    delta_latents = jnp.einsum(
        "tc,lc->tl", delta_expanded, up_full, preferred_element_type=jnp.float32
    )
    unused_latent, latent_back = jax.vjp(norm_rows, latent_raw, gain_latent_float)
    delta_latent_raw, delta_gain_latent = latent_back(delta_latents)
    delta_down_out = jnp.concatenate(
        [delta_latent_raw, rotate(delta_rotary_total, cosine_table, -sine_table)], axis=-1
    ).astype(jnp.bfloat16)
    delta_latent_down = jnp.einsum(
        "td,tc->dc", normed_one, delta_down_out, preferred_element_type=jnp.float32
    )
    delta_query_raw = (
        jnp.concatenate(
            [
                delta_query_plain,
                rotate(delta_query_rotary, cosine_table[:, None, :], -sine_table[:, None, :]),
            ],
            axis=-1,
        )
        .astype(jnp.bfloat16)
        .reshape(tok_rows, H * (DN + DR))
    )
    delta_query_weight = jnp.einsum(
        "td,tc->dc", normed_one, delta_query_raw, preferred_element_type=jnp.float32
    )
    delta_normed_one = jnp.einsum(
        "tc,dc->td", delta_query_raw, query_full, preferred_element_type=jnp.float32
    ) + jnp.einsum("tc,dc->td", delta_down_out, down_full, preferred_element_type=jnp.float32)
    unused_first, first_back = jax.vjp(norm_rows, tokens_float, gain_one_float)
    delta_tokens_norm, delta_gain_one = first_back(delta_normed_one)
    input_gradient = (delta_residual + delta_tokens_norm).astype(jnp.bfloat16)
    att_grads = scatter_packed(
        [
            delta_query_weight.astype(jnp.bfloat16),
            delta_latent_down.astype(jnp.bfloat16),
            delta_latent_up.astype(jnp.bfloat16),
            delta_output_t.astype(jnp.bfloat16),
            delta_gain_one.astype(jnp.bfloat16),
            delta_gain_latent.astype(jnp.bfloat16),
        ],
        ALL,
        devices,
    )
    return (
        layer_output,
        input_gradient,
        att_grads[4].astype(jnp.float32),
        att_grads[0].astype(jnp.float32),
        att_grads[1].astype(jnp.float32),
        att_grads[5].astype(jnp.float32),
        att_grads[2].astype(jnp.float32),
        att_grads[3].T.astype(jnp.float32),
        delta_gain_two_local,
        delta_router_local,
        delta_shared_inner,
        delta_shared_outer,
        delta_expert_inner.astype(jnp.float32),
        delta_expert_outer.astype(jnp.float32),
        statistics,
    )


def solution(mesh):
    return jax.shard_map(
        shards,
        mesh=mesh,
        in_specs=(
            P(ALL, None),
            P(ALL, None),
            P(ALL, None),
            P(ALL),
            P(ALL, None),
            P(ALL, None),
            P(ALL),
            P(ALL, None),
            P(None, ALL),
            P(ALL),
            P(ALL, None),
            P(None, ALL, None),
            P(None, ALL),
            P("expert", None, None, "shard"),
            P("expert", "shard", None),
        ),
        out_specs=(
            P(ALL, None),
            P(ALL, None),
            P(ALL),
            P(ALL, None),
            P(ALL, None),
            P(ALL),
            P(ALL, None),
            P(None, ALL),
            P(ALL),
            P(ALL, None),
            P(None, ALL, None),
            P(None, ALL),
            P("expert", None, None, "shard"),
            P("expert", "shard", None),
            P(),
        ),
        check_vma=False,
    )
```

```python
import jax
import jax.numpy as jnp
from jax import lax
from jax.sharding import PartitionSpec as P

D = 2048
H = 16
DN = 128
DR = 64
DV = 128
KVR = 512
TOPK = 6
CL = 64

ALL = ("expert", "shard")
EPSILON = 1e-06
THETA = 10000.0


def passed_along(value, axis, steps):
    count = lax.axis_size(axis)
    first, last = (max(0, -steps), min(count, count - steps))
    return lax.ppermute(value, axis, [(source, source + steps) for source in range(first, last)])


def matmul(left_side, right_side):
    return jnp.dot(left_side, right_side, preferred_element_type=jnp.float32)


def norm_rows(values, gain_vector):
    return (
        values
        * lax.rsqrt(jnp.mean(values * values, axis=-1, keepdims=True) + EPSILON)
        * gain_vector
    )


def rotate(values, cosine_table, sine_table):
    middle = values.shape[-1] // 2
    first_half = values[..., :middle]
    second_half = values[..., middle:]
    return jnp.concatenate(
        [
            first_half * cosine_table - second_half * sine_table,
            second_half * cosine_table + first_half * sine_table,
        ],
        axis=-1,
    )


def angles(positions):
    inverse = THETA ** (-jnp.arange(DR // 2, dtype=jnp.float32) * 2.0 / DR)
    phases = positions.astype(jnp.float32)[:, None] * inverse[None, :]
    return (jnp.cos(phases), jnp.sin(phases))


def gated(inner_out):
    return jax.nn.silu(inner_out[..., 0, :]) * inner_out[..., 1, :]


def masked_scores(queries, key_rows, rotary_rows, visible):
    factor = (DN + DR) ** (-0.5)
    plain_part = jnp.einsum(
        "qhd,khd->hqk", queries[..., :DN], key_rows[..., :DN], preferred_element_type=jnp.float32
    )
    rotary_part = jnp.einsum(
        "qhr,kr->hqk", queries[..., DN:], rotary_rows, preferred_element_type=jnp.float32
    )
    return jnp.where(visible[None], (plain_part + rotary_part) * factor, -1e30)


def swap_shard(value):
    return lax.ppermute(value, "shard", [(0, 1), (1, 0)])


def gather_blocks(local):
    side = lax.axis_index("shard")
    mine = lax.all_gather(local, "expert", axis=0, tiled=False)
    partner = swap_shard(mine)
    lower = jnp.where(side == 0, mine, partner)
    upper = jnp.where(side == 0, partner, mine)
    return jnp.stack([lower, upper], axis=1)


def gather_rows(local):
    blocks = gather_blocks(local)
    return blocks.reshape((-1,) + local.shape[1:])


def scatter_blocks(blocks):
    side = lax.axis_index("shard")
    mine = lax.dynamic_index_in_dim(blocks, side, axis=1, keepdims=False)
    theirs = lax.dynamic_index_in_dim(blocks, 1 - side, axis=1, keepdims=False)
    arrived = swap_shard(theirs.astype(jnp.bfloat16))
    total = (mine + arrived.astype(jnp.float32)).astype(jnp.bfloat16)
    rows = total.reshape((-1,) + total.shape[2:])
    return lax.psum_scatter(rows, "expert", scatter_dimension=0, tiled=True)


def scatter_rows(full, experts):
    blocks = full.reshape((experts, 2, -1) + full.shape[1:])
    return scatter_blocks(blocks).astype(jnp.float32)


def pack_small(parts, devices):
    packed = jnp.concatenate(parts, axis=1)
    pad = (-packed.shape[1]) % 1024
    if pad:
        packed = jnp.concatenate([packed, jnp.zeros((devices, pad), packed.dtype)], axis=1)
    return packed


def gated_pair(gate_part, up_part):
    return jax.nn.silu(gate_part) * up_part


def shards(
    tokens_in,
    cotangent,
    expert_ids,
    attention_gain,
    query_weight,
    latent_down,
    latent_gain,
    latent_up,
    output_weight,
    feedforward_gain,
    router_weight,
    shared_inner,
    shared_outer,
    expert_inner,
    expert_outer,
):
    tok_rows = tokens_in.shape[0]
    experts_all = lax.axis_size("expert")
    shard_count = lax.axis_size("shard")
    devices = experts_all * shard_count
    slot_cap = tok_rows * TOPK * 4 // (3 * experts_all)
    factor = (DN + DR) ** (-0.5)
    side_index = lax.axis_index("shard")
    ordinal = jnp.arange(tok_rows, dtype=jnp.int32)
    positions = jnp.where(side_index == 0, ordinal, tok_rows + ordinal % CL)
    cosine_table, sine_table = angles(positions)
    query_place = ordinal[:, None]
    key_place = ordinal[None, :]
    causal = key_place <= query_place
    same_block = query_place // CL == key_place // CL
    local_mask = jnp.where(side_index == 0, causal, causal & same_block)
    remote_mask = jnp.broadcast_to(side_index == 1, (tok_rows, tok_rows))
    visible = jnp.concatenate([remote_mask, local_mask], axis=1)

    small_sizes = [attention_gain.shape[0], latent_gain.shape[0], feedforward_gain.shape[0]]
    small_local = jnp.concatenate(
        [attention_gain, latent_gain, feedforward_gain, router_weight.reshape(-1)]
    )
    small_all = lax.all_gather(small_local, ALL, axis=0, tiled=False)
    cut_one, cut_two, cut_three = (
        small_sizes[0],
        small_sizes[0] + small_sizes[1],
        sum(small_sizes),
    )
    gain_one_float = small_all[:, :cut_one].reshape(-1).astype(jnp.float32)
    gain_latent_float = small_all[:, cut_one:cut_two].reshape(-1).astype(jnp.float32)
    gain_two_float = small_all[:, cut_two:cut_three].reshape(-1).astype(jnp.float32)
    router_full = small_all[:, cut_three:].reshape(-1, router_weight.shape[1])

    down_full = gather_rows(latent_down)
    query_full = gather_rows(query_weight)
    up_full = gather_rows(latent_up)
    output_t_full = gather_rows(output_weight.T)
    inner_blocks = gather_blocks(shared_inner.reshape(-1, shared_inner.shape[-1]))
    inner_blocks = inner_blocks.reshape(inner_blocks.shape[:2] + shared_inner.shape)
    shared_in_full = jnp.transpose(inner_blocks, (2, 0, 1, 3, 4)).reshape(
        (shared_inner.shape[0], -1, shared_inner.shape[-1])
    )
    shared_out_t_full = gather_rows(shared_outer.T)

    inner_halves = (expert_inner[0], swap_shard(expert_inner[0]))
    outer_halves = (expert_outer[0], swap_shard(expert_outer[0]))

    tokens_float = tokens_in.astype(jnp.float32)
    normed_one = norm_rows(tokens_float, gain_one_float).astype(jnp.bfloat16)
    query_raw = matmul(normed_one, query_full).reshape(tok_rows, H, DN + DR)
    queries = jnp.concatenate(
        [
            query_raw[..., :DN],
            rotate(query_raw[..., DN:], cosine_table[:, None, :], sine_table[:, None, :]),
        ],
        axis=-1,
    ).astype(jnp.bfloat16)
    down_out = matmul(normed_one, down_full)
    latent_raw = down_out[:, :KVR]
    latents = norm_rows(latent_raw, gain_latent_float).astype(jnp.bfloat16)
    key_rotary = rotate(down_out[:, KVR:], cosine_table, sine_table).astype(jnp.bfloat16)
    expanded = matmul(latents, up_full).astype(jnp.bfloat16).reshape(tok_rows, H, DN + DV)
    kv_local = jnp.concatenate([expanded.reshape(tok_rows, -1), key_rotary], axis=1)
    kv_remote = passed_along(kv_local, "shard", 1)
    remote_expanded = kv_remote[:, : H * (DN + DV)].reshape(tok_rows, H, DN + DV)
    remote_rotary = kv_remote[:, H * (DN + DV) :]
    key_rows = jnp.concatenate([remote_expanded, expanded], axis=0)
    rotary_rows = jnp.concatenate([remote_rotary, key_rotary], axis=0)
    scores = masked_scores(queries, key_rows, rotary_rows, visible)
    score_max = jnp.max(scores, axis=-1, keepdims=True)
    log_total = score_max + jnp.log(jnp.sum(jnp.exp(scores - score_max), axis=-1, keepdims=True))
    weights_float = jnp.exp(scores - log_total)
    weights_low = weights_float.astype(jnp.bfloat16)
    mixed_heads = (
        jnp.einsum(
            "hqk,khd->qhd", weights_low, key_rows[..., DN:], preferred_element_type=jnp.float32
        )
        .astype(jnp.bfloat16)
        .reshape(tok_rows, H * DV)
    )
    attention_out = jnp.einsum(
        "tc,dc->td", mixed_heads, output_t_full, preferred_element_type=jnp.float32
    )
    residual = tokens_float + attention_out
    normed_two = norm_rows(residual, gain_two_float).astype(jnp.bfloat16)
    logits = matmul(normed_two, router_full)
    route_probs = jax.nn.softmax(logits, axis=-1)
    gate_values = jnp.take_along_axis(route_probs, expert_ids, axis=1)
    flat_experts = expert_ids.reshape(-1)
    expert_match = (
        flat_experts[:, None] == jnp.arange(experts_all, dtype=jnp.int32)[None, :]
    ).astype(jnp.int32)
    slot_rank = jnp.sum((jnp.cumsum(expert_match, axis=0) - expert_match) * expert_match, axis=1)
    pair_count = tok_rows * TOPK
    slot_of = flat_experts * slot_cap + slot_rank
    slot_pair = (
        jnp.full((experts_all * slot_cap,), pair_count, jnp.int32)
        .at[slot_of]
        .set(jnp.arange(pair_count, dtype=jnp.int32))
    )
    slot_token = slot_pair // TOPK
    delta_out = cotangent.astype(jnp.float32)
    padded_rows = jnp.concatenate([normed_two, jnp.zeros((1, D), jnp.bfloat16)], axis=0)
    send_rows = jnp.take(padded_rows, slot_token, axis=0)
    padded_gates = jnp.concatenate([gate_values.reshape(-1), jnp.zeros((1,), jnp.float32)])
    slot_gate = jnp.take(padded_gates, slot_pair, axis=0)
    padded_delta = jnp.concatenate([delta_out, jnp.zeros((1, D), jnp.float32)], axis=0)
    send_delta = (jnp.take(padded_delta, slot_token, axis=0) * slot_gate[:, None]).astype(
        jnp.bfloat16
    )
    outgoing = jnp.stack(
        [send_rows.reshape(experts_all, slot_cap, D), send_delta.reshape(experts_all, slot_cap, D)],
        axis=1,
    )
    incoming = lax.all_to_all(outgoing, "expert", split_axis=0, concat_axis=0, tiled=True)
    arrived = incoming[:, 0].reshape(-1, D)
    delta_arrived = incoming[:, 1].reshape(-1, D)

    expert_pre = [
        jnp.einsum("rd,gdf->rgf", arrived, weight, preferred_element_type=jnp.float32)
        for weight in inner_halves
    ]
    expert_hidden = [gated(pre).astype(jnp.bfloat16) for pre in expert_pre]
    expert_result = sum(
        matmul(hidden, weight) for hidden, weight in zip(expert_hidden, outer_halves)
    ).astype(jnp.bfloat16)
    delta_outer_halves = [
        jnp.einsum("rf,rd->fd", hidden, delta_arrived, preferred_element_type=jnp.float32)
        for hidden in expert_hidden
    ]
    delta_pre_halves = []
    for pre, weight in zip(expert_pre, outer_halves):
        delta_hidden = jnp.einsum(
            "rd,fd->rf", delta_arrived, weight, preferred_element_type=jnp.float32
        )
        unused_expert, expert_back = jax.vjp(gated, pre)
        delta_pre_halves.append(expert_back(delta_hidden)[0].astype(jnp.bfloat16))
    delta_inner_halves = [
        jnp.einsum("rd,rgf->gdf", arrived, delta_pre, preferred_element_type=jnp.float32)
        for delta_pre in delta_pre_halves
    ]
    delta_rows = sum(
        jnp.einsum("rgf,gdf->rd", delta_pre, weight, preferred_element_type=jnp.float32)
        for delta_pre, weight in zip(delta_pre_halves, inner_halves)
    ).astype(jnp.bfloat16)
    going_back = jnp.stack(
        [
            expert_result.reshape(experts_all, slot_cap, D),
            delta_rows.reshape(experts_all, slot_cap, D),
        ],
        axis=1,
    )
    coming_back = lax.all_to_all(going_back, "expert", split_axis=0, concat_axis=0, tiled=True)
    returned = coming_back[:, 0].reshape(-1, D)
    delta_returned = coming_back[:, 1].reshape(-1, D)
    inner_from_partner = swap_shard(delta_inner_halves[1].astype(jnp.bfloat16))
    outer_from_partner = swap_shard(delta_outer_halves[1].astype(jnp.bfloat16))
    delta_expert_inner = delta_inner_halves[0] + inner_from_partner.astype(jnp.float32)
    delta_expert_outer = delta_outer_halves[0] + outer_from_partner.astype(jnp.float32)

    picked = jnp.take(returned, slot_of, axis=0).reshape(tok_rows, TOPK, D).astype(jnp.float32)
    routed = jnp.sum(gate_values[..., None] * picked, axis=1)
    shared_gate = matmul(normed_two, shared_in_full[0])
    shared_up = matmul(normed_two, shared_in_full[1])
    shared_hidden = gated_pair(shared_gate, shared_up).astype(jnp.bfloat16)
    shared_result = jnp.einsum(
        "tf,df->td", shared_hidden, shared_out_t_full, preferred_element_type=jnp.float32
    )
    feedforward = routed + shared_result
    layer_output = (residual + feedforward).astype(jnp.bfloat16)
    square_sums = jnp.stack(
        [
            jnp.sum(residual * residual),
            jnp.sum(attention_out * attention_out),
            jnp.sum(feedforward * feedforward),
        ]
    )

    delta_shared_outer_t = jnp.einsum(
        "td,tf->df", cotangent, shared_hidden, preferred_element_type=jnp.float32
    )
    delta_shared_hidden = jnp.einsum(
        "td,df->tf", cotangent, shared_out_t_full, preferred_element_type=jnp.float32
    )
    unused_shared, shared_back = jax.vjp(gated_pair, shared_gate, shared_up)
    delta_gate, delta_up = [
        part.astype(jnp.bfloat16) for part in shared_back(delta_shared_hidden)
    ]
    delta_shared_inner = jnp.stack(
        [
            jnp.einsum("td,tf->df", normed_two, part, preferred_element_type=jnp.float32)
            for part in (delta_gate, delta_up)
        ]
    )
    delta_normed = matmul(delta_gate, shared_in_full[0].T) + matmul(
        delta_up, shared_in_full[1].T
    )
    delta_gates = jnp.sum(delta_out[:, None, :] * picked, axis=-1)
    delta_normed = delta_normed + jnp.sum(
        jnp.take(delta_returned, slot_of, axis=0).reshape(tok_rows, TOPK, D).astype(jnp.float32),
        axis=1,
    )
    match_float = expert_match.reshape(tok_rows, TOPK, experts_all).astype(jnp.float32)
    delta_probs = jnp.einsum("tk,tke->te", delta_gates, match_float)
    delta_logits = (
        route_probs * (delta_probs - jnp.sum(route_probs * delta_probs, axis=-1, keepdims=True))
    ).astype(jnp.bfloat16)
    delta_router = jnp.einsum(
        "td,te->de", normed_two, delta_logits, preferred_element_type=jnp.float32
    )
    delta_normed = delta_normed + jnp.einsum(
        "te,de->td", delta_logits, router_full, preferred_element_type=jnp.float32
    )
    unused_second, second_back = jax.vjp(norm_rows, residual, gain_two_float)
    delta_residual_norm, delta_gain_two = second_back(delta_normed)
    delta_residual = delta_out + delta_residual_norm
    inner_grad_blocks = jnp.transpose(
        delta_shared_inner.reshape(
            (shared_inner.shape[0], experts_all, shard_count) + shared_inner.shape[1:]
        ),
        (1, 2, 0, 3, 4),
    ).reshape((experts_all, shard_count, -1, shared_inner.shape[-1]))
    delta_shared_inner_local = (
        scatter_blocks(inner_grad_blocks).astype(jnp.float32).reshape(shared_inner.shape)
    )
    delta_shared_outer_local = scatter_rows(delta_shared_outer_t, experts_all).T

    delta_attention = delta_residual.astype(jnp.bfloat16)
    delta_output_t = jnp.einsum(
        "td,tc->dc", delta_attention, mixed_heads, preferred_element_type=jnp.float32
    )
    delta_output_local = scatter_rows(delta_output_t, experts_all).T
    delta_mixed = (
        jnp.einsum("td,dc->tc", delta_attention, output_t_full, preferred_element_type=jnp.float32)
        .astype(jnp.bfloat16)
        .reshape(tok_rows, H, DV)
    )
    delta_weights = jnp.einsum(
        "qhd,khd->hqk", delta_mixed, key_rows[..., DN:], preferred_element_type=jnp.float32
    )
    delta_scores = (
        weights_float
        * (delta_weights - jnp.sum(weights_float * delta_weights, axis=-1, keepdims=True))
    ).astype(jnp.bfloat16)
    delta_values = jnp.einsum(
        "hqk,qhd->khd", weights_low, delta_mixed, preferred_element_type=jnp.float32
    )
    delta_query_plain = (
        jnp.einsum(
            "hqk,khd->qhd", delta_scores, key_rows[..., :DN], preferred_element_type=jnp.float32
        )
        * factor
    )
    delta_query_rotary = (
        jnp.einsum("hqk,kr->qhr", delta_scores, rotary_rows, preferred_element_type=jnp.float32)
        * factor
    )
    delta_key_plain = (
        jnp.einsum(
            "hqk,qhd->khd", delta_scores, queries[..., :DN], preferred_element_type=jnp.float32
        )
        * factor
    )
    delta_key_rotary = (
        jnp.einsum(
            "hqk,qhr->kr", delta_scores, queries[..., DN:], preferred_element_type=jnp.float32
        )
        * factor
    )
    delta_key_rows = jnp.concatenate([delta_key_plain, delta_values], axis=-1)
    back_local = jnp.concatenate(
        [delta_key_rows[:tok_rows].reshape(tok_rows, -1), delta_key_rotary[:tok_rows]], axis=1
    ).astype(jnp.bfloat16)
    back_remote = passed_along(back_local, "shard", -1).astype(jnp.float32)
    back_rows = back_remote[:, : H * (DN + DV)].reshape(tok_rows, H, DN + DV)
    back_rotary = back_remote[:, H * (DN + DV) :]
    delta_expanded = (
        (delta_key_rows[tok_rows:] + back_rows)
        .astype(jnp.bfloat16)
        .reshape(tok_rows, H * (DN + DV))
    )
    delta_rotary_total = delta_key_rotary[tok_rows:] + back_rotary
    delta_latent_up = jnp.einsum(
        "tl,tc->lc", latents, delta_expanded, preferred_element_type=jnp.float32
    )
    delta_latent_up_local = scatter_rows(delta_latent_up, experts_all)
    delta_latents = jnp.einsum(
        "tc,lc->tl", delta_expanded, up_full, preferred_element_type=jnp.float32
    )
    unused_latent, latent_back = jax.vjp(norm_rows, latent_raw, gain_latent_float)
    delta_latent_raw, delta_gain_latent = latent_back(delta_latents)
    delta_down_out = jnp.concatenate(
        [delta_latent_raw, rotate(delta_rotary_total, cosine_table, -sine_table)], axis=-1
    ).astype(jnp.bfloat16)
    delta_latent_down = jnp.einsum(
        "td,tc->dc", normed_one, delta_down_out, preferred_element_type=jnp.float32
    )
    delta_query_raw = (
        jnp.concatenate(
            [
                delta_query_plain,
                rotate(delta_query_rotary, cosine_table[:, None, :], -sine_table[:, None, :]),
            ],
            axis=-1,
        )
        .astype(jnp.bfloat16)
        .reshape(tok_rows, H * (DN + DR))
    )
    delta_query_weight = jnp.einsum(
        "td,tc->dc", normed_one, delta_query_raw, preferred_element_type=jnp.float32
    )
    delta_latent_down_local = scatter_rows(delta_latent_down, experts_all)
    delta_query_local = scatter_rows(delta_query_weight, experts_all)
    delta_normed_one = jnp.einsum(
        "tc,dc->td", delta_query_raw, query_full, preferred_element_type=jnp.float32
    ) + jnp.einsum("tc,dc->td", delta_down_out, down_full, preferred_element_type=jnp.float32)
    unused_first, first_back = jax.vjp(norm_rows, tokens_float, gain_one_float)
    delta_tokens_norm, delta_gain_one = first_back(delta_normed_one)
    input_gradient = (delta_residual + delta_tokens_norm).astype(jnp.bfloat16)

    small_parts = [
        delta_gain_one.reshape(devices, -1),
        delta_gain_latent.reshape(devices, -1),
        delta_gain_two.reshape(devices, -1),
        delta_router.reshape(devices, -1),
        jnp.broadcast_to(square_sums[None], (devices, 3)),
    ]
    small_packed = pack_small(small_parts, devices)
    small_sum = lax.psum_scatter(
        small_packed.reshape(-1, 128), ALL, scatter_dimension=0, tiled=True
    ).reshape(-1)
    small_cuts = [0]
    for part in small_parts:
        small_cuts.append(small_cuts[-1] + part.shape[1])
    small_pieces = [small_sum[small_cuts[i] : small_cuts[i + 1]] for i in range(len(small_parts))]
    statistics = jnp.sqrt(small_pieces[4] / (tok_rows * D * devices))
    return (
        layer_output,
        input_gradient,
        small_pieces[0],
        delta_query_local,
        delta_latent_down_local,
        small_pieces[1],
        delta_latent_up_local,
        delta_output_local,
        small_pieces[2],
        small_pieces[3].reshape(router_weight.shape),
        delta_shared_inner_local,
        delta_shared_outer_local,
        delta_expert_inner[None],
        delta_expert_outer[None],
        statistics,
    )


def solution(mesh):
    return jax.shard_map(
        shards,
        mesh=mesh,
        in_specs=(
            P(ALL, None),
            P(ALL, None),
            P(ALL, None),
            P(ALL),
            P(ALL, None),
            P(ALL, None),
            P(ALL),
            P(ALL, None),
            P(None, ALL),
            P(ALL),
            P(ALL, None),
            P(None, ALL, None),
            P(None, ALL),
            P("expert", None, None, "shard"),
            P("expert", "shard", None),
        ),
        out_specs=(
            P(ALL, None),
            P(ALL, None),
            P(ALL),
            P(ALL, None),
            P(ALL, None),
            P(ALL),
            P(ALL, None),
            P(None, ALL),
            P(ALL),
            P(ALL, None),
            P(None, ALL, None),
            P(None, ALL),
            P("expert", None, None, "shard"),
            P("expert", "shard", None),
            P(),
        ),
        check_vma=False,
    )
```

```python
import jax
import jax.numpy as jnp
from jax import lax
from jax.sharding import PartitionSpec as P

D = 2048
H = 16
DN = 128
DR = 64
DV = 128
KVR = 512
TOPK = 6
CL = 64

ALL = ("expert", "shard")
EPSILON = 1e-06
THETA = 10000.0


def passed_along(value, axis, steps):
    count = lax.axis_size(axis)
    first, last = (max(0, -steps), min(count, count - steps))
    return lax.ppermute(value, axis, [(source, source + steps) for source in range(first, last)])


def matmul(left_side, right_side):
    return jnp.dot(left_side, right_side, preferred_element_type=jnp.float32)


def norm_rows(values, gain_vector):
    return (
        values
        * lax.rsqrt(jnp.mean(values * values, axis=-1, keepdims=True) + EPSILON)
        * gain_vector
    )


def rotate(values, cosine_table, sine_table):
    middle = values.shape[-1] // 2
    first_half = values[..., :middle]
    second_half = values[..., middle:]
    return jnp.concatenate(
        [
            first_half * cosine_table - second_half * sine_table,
            second_half * cosine_table + first_half * sine_table,
        ],
        axis=-1,
    )


def angles(positions):
    inverse = THETA ** (-jnp.arange(DR // 2, dtype=jnp.float32) * 2.0 / DR)
    phases = positions.astype(jnp.float32)[:, None] * inverse[None, :]
    return (jnp.cos(phases), jnp.sin(phases))


def gated(inner_out):
    return jax.nn.silu(inner_out[..., 0, :]) * inner_out[..., 1, :]


def masked_scores(queries, key_rows, rotary_rows, visible):
    factor = (DN + DR) ** (-0.5)
    plain_part = jnp.einsum(
        "qhd,khd->hqk", queries[..., :DN], key_rows[..., :DN], preferred_element_type=jnp.float32
    )
    rotary_part = jnp.einsum(
        "qhr,kr->hqk", queries[..., DN:], rotary_rows, preferred_element_type=jnp.float32
    )
    return jnp.where(visible[None], (plain_part + rotary_part) * factor, -1e30)


def swap_shard(value):
    return lax.ppermute(value, "shard", [(0, 1), (1, 0)])


def gather_over_expert(local, by_exchange):
    if by_exchange:
        copies = jnp.broadcast_to(local[None], (lax.axis_size("expert"),) + local.shape)
        return lax.all_to_all(copies, "expert", split_axis=0, concat_axis=0, tiled=True)
    return lax.all_gather(local, "expert", axis=0, tiled=False)


def gather_halves(local, by_exchange=False):
    side = lax.axis_index("shard")
    mine = gather_over_expert(local, by_exchange)
    partner = swap_shard(mine)
    return jnp.where(side == 0, mine, partner), jnp.where(side == 0, partner, mine)


def assemble(halves, first=None, last=None):
    lower, upper = [half[:, first:last] for half in halves]
    full = jnp.stack([lower, upper], axis=1)
    return full.reshape((-1,) + full.shape[3:])


def gather_rows(local, by_exchange=False):
    return assemble(gather_halves(local, by_exchange))


def pair_total(blocks):
    side = lax.axis_index("shard")
    mine = lax.dynamic_index_in_dim(blocks, side, axis=1, keepdims=False)
    theirs = lax.dynamic_index_in_dim(blocks, 1 - side, axis=1, keepdims=False)
    arrived = swap_shard(theirs.astype(jnp.bfloat16))
    return (mine + arrived.astype(jnp.float32)).astype(jnp.bfloat16)


def reduce_over_expert(total, by_exchange=False):
    if by_exchange:
        got = lax.all_to_all(total, "expert", split_axis=0, concat_axis=0, tiled=True)
        return jnp.sum(got.astype(jnp.float32), axis=0)
    rows = total.reshape((-1,) + total.shape[2:])
    return lax.psum_scatter(rows, "expert", scatter_dimension=0, tiled=True).astype(jnp.float32)


def scatter_rows(full, experts, by_exchange=False):
    blocks = full.reshape((experts, 2, -1) + full.shape[1:])
    return reduce_over_expert(pair_total(blocks), by_exchange)


def gated_pair(gate_part, up_part):
    return jax.nn.silu(gate_part) * up_part


def shards(
    tokens_in,
    cotangent,
    expert_ids,
    attention_gain,
    query_weight,
    latent_down,
    latent_gain,
    latent_up,
    output_weight,
    feedforward_gain,
    router_weight,
    shared_inner,
    shared_outer,
    expert_inner,
    expert_outer,
):
    tok_rows = tokens_in.shape[0]
    experts_all = lax.axis_size("expert")
    shard_count = lax.axis_size("shard")
    devices = experts_all * shard_count
    slot_cap = tok_rows * TOPK * 4 // (3 * experts_all)
    factor = (DN + DR) ** (-0.5)
    side_index = lax.axis_index("shard")
    ordinal = jnp.arange(tok_rows, dtype=jnp.int32)
    positions = jnp.where(side_index == 0, ordinal, tok_rows + ordinal % CL)
    cosine_table, sine_table = angles(positions)
    query_place = ordinal[:, None]
    key_place = ordinal[None, :]
    causal = key_place <= query_place
    same_block = query_place // CL == key_place // CL
    local_mask = jnp.where(side_index == 0, causal, causal & same_block)
    remote_mask = jnp.broadcast_to(side_index == 1, (tok_rows, tok_rows))
    visible = jnp.concatenate([remote_mask, local_mask], axis=1)

    small_sizes = [
        attention_gain.shape[0],
        latent_gain.shape[0],
        feedforward_gain.shape[0],
        router_weight.size,
    ]
    small_local = jnp.concatenate(
        [attention_gain, latent_gain, feedforward_gain, router_weight.reshape(-1)]
    )
    width = latent_down.shape[1]
    small_rows = -(-small_local.shape[0] // width)
    small_local = jnp.concatenate(
        [small_local, jnp.zeros((small_rows * width - small_local.shape[0],), jnp.bfloat16)]
    ).reshape(small_rows, width)
    down_rows = latent_down.shape[0]
    down_halves = gather_halves(jnp.concatenate([latent_down, small_local], axis=0))
    down_full = assemble(down_halves, 0, down_rows)
    small_all = assemble(down_halves, down_rows).reshape(devices, -1)
    cuts = [0]
    for size in small_sizes:
        cuts.append(cuts[-1] + size)
    gain_one_float = small_all[:, cuts[0] : cuts[1]].reshape(-1).astype(jnp.float32)
    gain_latent_float = small_all[:, cuts[1] : cuts[2]].reshape(-1).astype(jnp.float32)
    gain_two_float = small_all[:, cuts[2] : cuts[3]].reshape(-1).astype(jnp.float32)
    router_full = small_all[:, cuts[3] : cuts[4]].reshape(-1, router_weight.shape[1])

    query_full = gather_rows(query_weight)
    up_full = gather_rows(latent_up)
    output_t_full = gather_rows(output_weight.T)
    inner_rows = shared_inner.shape[0] * shared_inner.shape[1]
    ffn_halves = gather_halves(
        jnp.concatenate(
            [shared_inner.reshape(inner_rows, shared_inner.shape[-1]), shared_outer.T], axis=0
        ),
        by_exchange=True,
    )
    shared_in_full = [
        assemble(ffn_halves, g * shared_inner.shape[1], (g + 1) * shared_inner.shape[1])
        for g in range(shared_inner.shape[0])
    ]
    shared_out_t_full = assemble(ffn_halves, inner_rows)

    inner_halves = (expert_inner[0], swap_shard(expert_inner[0]))
    outer_halves = (expert_outer[0], swap_shard(expert_outer[0]))

    tokens_float = tokens_in.astype(jnp.float32)
    normed_one = norm_rows(tokens_float, gain_one_float).astype(jnp.bfloat16)
    query_raw = matmul(normed_one, query_full).reshape(tok_rows, H, DN + DR)
    queries = jnp.concatenate(
        [
            query_raw[..., :DN],
            rotate(query_raw[..., DN:], cosine_table[:, None, :], sine_table[:, None, :]),
        ],
        axis=-1,
    ).astype(jnp.bfloat16)
    down_out = matmul(normed_one, down_full)
    latent_raw = down_out[:, :KVR]
    latents = norm_rows(latent_raw, gain_latent_float).astype(jnp.bfloat16)
    key_rotary = rotate(down_out[:, KVR:], cosine_table, sine_table).astype(jnp.bfloat16)
    expanded = matmul(latents, up_full).astype(jnp.bfloat16).reshape(tok_rows, H, DN + DV)
    kv_local = jnp.concatenate([expanded.reshape(tok_rows, -1), key_rotary], axis=1)
    kv_remote = passed_along(kv_local, "shard", 1)
    remote_expanded = kv_remote[:, : H * (DN + DV)].reshape(tok_rows, H, DN + DV)
    remote_rotary = kv_remote[:, H * (DN + DV) :]
    key_rows = jnp.concatenate([remote_expanded, expanded], axis=0)
    rotary_rows = jnp.concatenate([remote_rotary, key_rotary], axis=0)
    scores = masked_scores(queries, key_rows, rotary_rows, visible)
    score_max = jnp.max(scores, axis=-1, keepdims=True)
    log_total = score_max + jnp.log(jnp.sum(jnp.exp(scores - score_max), axis=-1, keepdims=True))
    weights_float = jnp.exp(scores - log_total)
    weights_low = weights_float.astype(jnp.bfloat16)
    mixed_heads = (
        jnp.einsum(
            "hqk,khd->qhd", weights_low, key_rows[..., DN:], preferred_element_type=jnp.float32
        )
        .astype(jnp.bfloat16)
        .reshape(tok_rows, H * DV)
    )
    attention_out = jnp.einsum(
        "tc,dc->td", mixed_heads, output_t_full, preferred_element_type=jnp.float32
    )
    residual = tokens_float + attention_out
    normed_two = norm_rows(residual, gain_two_float).astype(jnp.bfloat16)
    logits = matmul(normed_two, router_full)
    route_probs = jax.nn.softmax(logits, axis=-1)
    gate_values = jnp.take_along_axis(route_probs, expert_ids, axis=1)
    flat_experts = expert_ids.reshape(-1)
    expert_match = (
        flat_experts[:, None] == jnp.arange(experts_all, dtype=jnp.int32)[None, :]
    ).astype(jnp.int32)
    slot_rank = jnp.sum((jnp.cumsum(expert_match, axis=0) - expert_match) * expert_match, axis=1)
    pair_count = tok_rows * TOPK
    slot_of = flat_experts * slot_cap + slot_rank
    slot_pair = (
        jnp.full((experts_all * slot_cap,), pair_count, jnp.int32)
        .at[slot_of]
        .set(jnp.arange(pair_count, dtype=jnp.int32))
    )
    slot_token = slot_pair // TOPK
    delta_out = cotangent.astype(jnp.float32)
    padded_rows = jnp.concatenate([normed_two, jnp.zeros((1, D), jnp.bfloat16)], axis=0)
    send_rows = jnp.take(padded_rows, slot_token, axis=0)
    padded_gates = jnp.concatenate([gate_values.reshape(-1), jnp.zeros((1,), jnp.float32)])
    slot_gate = jnp.take(padded_gates, slot_pair, axis=0)
    padded_delta = jnp.concatenate([delta_out, jnp.zeros((1, D), jnp.float32)], axis=0)
    send_delta = (jnp.take(padded_delta, slot_token, axis=0) * slot_gate[:, None]).astype(
        jnp.bfloat16
    )
    outgoing = jnp.stack(
        [send_rows.reshape(experts_all, slot_cap, D), send_delta.reshape(experts_all, slot_cap, D)],
        axis=1,
    )
    incoming = lax.all_to_all(outgoing, "expert", split_axis=0, concat_axis=0, tiled=True)
    arrived = incoming[:, 0].reshape(-1, D)
    delta_arrived = incoming[:, 1].reshape(-1, D)

    expert_pre = [
        jnp.einsum("rd,gdf->rgf", arrived, weight, preferred_element_type=jnp.float32)
        for weight in inner_halves
    ]
    expert_hidden = [gated(pre).astype(jnp.bfloat16) for pre in expert_pre]
    expert_result = sum(
        matmul(hidden, weight) for hidden, weight in zip(expert_hidden, outer_halves)
    ).astype(jnp.bfloat16)
    delta_outer_halves = [
        jnp.einsum("rf,rd->fd", hidden, delta_arrived, preferred_element_type=jnp.float32)
        for hidden in expert_hidden
    ]
    delta_pre_halves = []
    for pre, weight in zip(expert_pre, outer_halves):
        delta_hidden = jnp.einsum(
            "rd,fd->rf", delta_arrived, weight, preferred_element_type=jnp.float32
        )
        unused_expert, expert_back = jax.vjp(gated, pre)
        delta_pre_halves.append(expert_back(delta_hidden)[0].astype(jnp.bfloat16))
    delta_inner_halves = [
        jnp.einsum("rd,rgf->gdf", arrived, delta_pre, preferred_element_type=jnp.float32)
        for delta_pre in delta_pre_halves
    ]
    delta_rows = sum(
        jnp.einsum("rgf,gdf->rd", delta_pre, weight, preferred_element_type=jnp.float32)
        for delta_pre, weight in zip(delta_pre_halves, inner_halves)
    ).astype(jnp.bfloat16)
    going_back = jnp.stack(
        [
            expert_result.reshape(experts_all, slot_cap, D),
            delta_rows.reshape(experts_all, slot_cap, D),
        ],
        axis=1,
    )
    coming_back = lax.all_to_all(going_back, "expert", split_axis=0, concat_axis=0, tiled=True)
    returned = coming_back[:, 0].reshape(-1, D)
    delta_returned = coming_back[:, 1].reshape(-1, D)
    inner_from_partner = swap_shard(delta_inner_halves[1].astype(jnp.bfloat16))
    outer_from_partner = swap_shard(delta_outer_halves[1].astype(jnp.bfloat16))
    delta_expert_inner = delta_inner_halves[0] + inner_from_partner.astype(jnp.float32)
    delta_expert_outer = delta_outer_halves[0] + outer_from_partner.astype(jnp.float32)

    picked = jnp.take(returned, slot_of, axis=0).reshape(tok_rows, TOPK, D).astype(jnp.float32)
    routed = jnp.sum(gate_values[..., None] * picked, axis=1)
    shared_gate = matmul(normed_two, shared_in_full[0])
    shared_up = matmul(normed_two, shared_in_full[1])
    shared_hidden = gated_pair(shared_gate, shared_up).astype(jnp.bfloat16)
    shared_result = jnp.einsum(
        "tf,df->td", shared_hidden, shared_out_t_full, preferred_element_type=jnp.float32
    )
    feedforward = routed + shared_result
    layer_output = (residual + feedforward).astype(jnp.bfloat16)
    square_sums = jnp.stack(
        [
            jnp.sum(residual * residual),
            jnp.sum(attention_out * attention_out),
            jnp.sum(feedforward * feedforward),
        ]
    )

    delta_shared_outer_t = jnp.einsum(
        "td,tf->df", cotangent, shared_hidden, preferred_element_type=jnp.float32
    )
    delta_shared_hidden = jnp.einsum(
        "td,df->tf", cotangent, shared_out_t_full, preferred_element_type=jnp.float32
    )
    unused_shared, shared_back = jax.vjp(gated_pair, shared_gate, shared_up)
    delta_gate, delta_up = [
        part.astype(jnp.bfloat16) for part in shared_back(delta_shared_hidden)
    ]
    delta_shared_inner = jnp.stack(
        [
            jnp.einsum("td,tf->df", normed_two, part, preferred_element_type=jnp.float32)
            for part in (delta_gate, delta_up)
        ]
    )
    delta_normed = matmul(delta_gate, shared_in_full[0].T) + matmul(
        delta_up, shared_in_full[1].T
    )
    delta_gates = jnp.sum(delta_out[:, None, :] * picked, axis=-1)
    delta_normed = delta_normed + jnp.sum(
        jnp.take(delta_returned, slot_of, axis=0).reshape(tok_rows, TOPK, D).astype(jnp.float32),
        axis=1,
    )
    match_float = expert_match.reshape(tok_rows, TOPK, experts_all).astype(jnp.float32)
    delta_probs = jnp.einsum("tk,tke->te", delta_gates, match_float)
    delta_logits = (
        route_probs * (delta_probs - jnp.sum(route_probs * delta_probs, axis=-1, keepdims=True))
    ).astype(jnp.bfloat16)
    delta_router = jnp.einsum(
        "td,te->de", normed_two, delta_logits, preferred_element_type=jnp.float32
    )
    delta_normed = delta_normed + jnp.einsum(
        "te,de->td", delta_logits, router_full, preferred_element_type=jnp.float32
    )
    unused_second, second_back = jax.vjp(norm_rows, residual, gain_two_float)
    delta_residual_norm, delta_gain_two = second_back(delta_normed)
    delta_residual = delta_out + delta_residual_norm
    inner_grad_blocks = jnp.transpose(
        delta_shared_inner.reshape(
            (shared_inner.shape[0], experts_all, shard_count) + shared_inner.shape[1:]
        ),
        (1, 2, 0, 3, 4),
    ).reshape((experts_all, shard_count, -1, shared_inner.shape[-1]))
    outer_grad_blocks = delta_shared_outer_t.reshape(
        (experts_all, shard_count, -1, delta_shared_outer_t.shape[-1])
    )
    ffn_total = jnp.concatenate(
        [pair_total(inner_grad_blocks), pair_total(outer_grad_blocks)], axis=1
    )
    ffn_local = reduce_over_expert(ffn_total, by_exchange=True)
    delta_shared_inner_local = ffn_local[:inner_rows].reshape(shared_inner.shape)
    delta_shared_outer_local = ffn_local[inner_rows:].T

    delta_attention = delta_residual.astype(jnp.bfloat16)
    delta_output_t = jnp.einsum(
        "td,tc->dc", delta_attention, mixed_heads, preferred_element_type=jnp.float32
    )
    delta_output_local = scatter_rows(delta_output_t, experts_all).T
    delta_mixed = (
        jnp.einsum("td,dc->tc", delta_attention, output_t_full, preferred_element_type=jnp.float32)
        .astype(jnp.bfloat16)
        .reshape(tok_rows, H, DV)
    )
    delta_weights = jnp.einsum(
        "qhd,khd->hqk", delta_mixed, key_rows[..., DN:], preferred_element_type=jnp.float32
    )
    delta_scores = (
        weights_float
        * (delta_weights - jnp.sum(weights_float * delta_weights, axis=-1, keepdims=True))
    ).astype(jnp.bfloat16)
    delta_values = jnp.einsum(
        "hqk,qhd->khd", weights_low, delta_mixed, preferred_element_type=jnp.float32
    )
    delta_query_plain = (
        jnp.einsum(
            "hqk,khd->qhd", delta_scores, key_rows[..., :DN], preferred_element_type=jnp.float32
        )
        * factor
    )
    delta_query_rotary = (
        jnp.einsum("hqk,kr->qhr", delta_scores, rotary_rows, preferred_element_type=jnp.float32)
        * factor
    )
    delta_key_plain = (
        jnp.einsum(
            "hqk,qhd->khd", delta_scores, queries[..., :DN], preferred_element_type=jnp.float32
        )
        * factor
    )
    delta_key_rotary = (
        jnp.einsum(
            "hqk,qhr->kr", delta_scores, queries[..., DN:], preferred_element_type=jnp.float32
        )
        * factor
    )
    delta_key_rows = jnp.concatenate([delta_key_plain, delta_values], axis=-1)
    back_local = jnp.concatenate(
        [delta_key_rows[:tok_rows].reshape(tok_rows, -1), delta_key_rotary[:tok_rows]], axis=1
    ).astype(jnp.bfloat16)
    back_remote = passed_along(back_local, "shard", -1).astype(jnp.float32)
    back_rows = back_remote[:, : H * (DN + DV)].reshape(tok_rows, H, DN + DV)
    back_rotary = back_remote[:, H * (DN + DV) :]
    delta_expanded = (
        (delta_key_rows[tok_rows:] + back_rows)
        .astype(jnp.bfloat16)
        .reshape(tok_rows, H * (DN + DV))
    )
    delta_rotary_total = delta_key_rotary[tok_rows:] + back_rotary
    delta_latent_up = jnp.einsum(
        "tl,tc->lc", latents, delta_expanded, preferred_element_type=jnp.float32
    )
    delta_latent_up_local = scatter_rows(delta_latent_up, experts_all)
    delta_latents = jnp.einsum(
        "tc,lc->tl", delta_expanded, up_full, preferred_element_type=jnp.float32
    )
    unused_latent, latent_back = jax.vjp(norm_rows, latent_raw, gain_latent_float)
    delta_latent_raw, delta_gain_latent = latent_back(delta_latents)
    delta_down_out = jnp.concatenate(
        [delta_latent_raw, rotate(delta_rotary_total, cosine_table, -sine_table)], axis=-1
    ).astype(jnp.bfloat16)
    delta_latent_down = jnp.einsum(
        "td,tc->dc", normed_one, delta_down_out, preferred_element_type=jnp.float32
    )
    delta_query_raw = (
        jnp.concatenate(
            [
                delta_query_plain,
                rotate(delta_query_rotary, cosine_table[:, None, :], -sine_table[:, None, :]),
            ],
            axis=-1,
        )
        .astype(jnp.bfloat16)
        .reshape(tok_rows, H * (DN + DR))
    )
    delta_query_weight = jnp.einsum(
        "td,tc->dc", normed_one, delta_query_raw, preferred_element_type=jnp.float32
    )
    delta_latent_down_local = scatter_rows(delta_latent_down, experts_all)
    delta_query_local = scatter_rows(delta_query_weight, experts_all, by_exchange=True)
    delta_normed_one = jnp.einsum(
        "tc,dc->td", delta_query_raw, query_full, preferred_element_type=jnp.float32
    ) + jnp.einsum("tc,dc->td", delta_down_out, down_full, preferred_element_type=jnp.float32)
    unused_first, first_back = jax.vjp(norm_rows, tokens_float, gain_one_float)
    delta_tokens_norm, delta_gain_one = first_back(delta_normed_one)
    input_gradient = (delta_residual + delta_tokens_norm).astype(jnp.bfloat16)

    small_parts = [
        delta_gain_one.reshape(devices, -1),
        delta_gain_latent.reshape(devices, -1),
        delta_gain_two.reshape(devices, -1),
        delta_router.reshape(devices, -1),
        jnp.broadcast_to(square_sums[None], (devices, 3)),
    ]
    small_packed = jnp.concatenate(small_parts, axis=1)
    small_sum = lax.dynamic_index_in_dim(
        lax.psum(small_packed, ALL), lax.axis_index(ALL), axis=0, keepdims=False
    )
    small_cuts = [0]
    for part in small_parts:
        small_cuts.append(small_cuts[-1] + part.shape[1])
    small_pieces = [small_sum[small_cuts[i] : small_cuts[i + 1]] for i in range(len(small_parts))]
    statistics = jnp.sqrt(small_pieces[4] / (tok_rows * D * devices))
    return (
        layer_output,
        input_gradient,
        small_pieces[0],
        delta_query_local,
        delta_latent_down_local,
        small_pieces[1],
        delta_latent_up_local,
        delta_output_local,
        small_pieces[2],
        small_pieces[3].reshape(router_weight.shape),
        delta_shared_inner_local,
        delta_shared_outer_local,
        delta_expert_inner[None],
        delta_expert_outer[None],
        statistics,
    )


def solution(mesh):
    return jax.shard_map(
        shards,
        mesh=mesh,
        in_specs=(
            P(ALL, None),
            P(ALL, None),
            P(ALL, None),
            P(ALL),
            P(ALL, None),
            P(ALL, None),
            P(ALL),
            P(ALL, None),
            P(None, ALL),
            P(ALL),
            P(ALL, None),
            P(None, ALL, None),
            P(None, ALL),
            P("expert", None, None, "shard"),
            P("expert", "shard", None),
        ),
        out_specs=(
            P(ALL, None),
            P(ALL, None),
            P(ALL),
            P(ALL, None),
            P(ALL, None),
            P(ALL),
            P(ALL, None),
            P(None, ALL),
            P(ALL),
            P(ALL, None),
            P(None, ALL, None),
            P(None, ALL),
            P("expert", None, None, "shard"),
            P("expert", "shard", None),
            P(),
        ),
        check_vma=False,
    )
```

```python
import jax
import jax.numpy as jnp
from jax import lax
from jax.sharding import PartitionSpec as P

D = 2048
H = 16
DN = 128
DR = 64
DV = 128
KVR = 512
TOPK = 6
CL = 64

ALL = ("expert", "shard")
EPSILON = 1e-06
THETA = 10000.0


def passed_along(value, axis, steps):
    count = lax.axis_size(axis)
    first, last = (max(0, -steps), min(count, count - steps))
    return lax.ppermute(value, axis, [(source, source + steps) for source in range(first, last)])


def matmul(left_side, right_side):
    return jnp.dot(left_side, right_side, preferred_element_type=jnp.float32)


def norm_rows(values, gain_vector):
    return (
        values
        * lax.rsqrt(jnp.mean(values * values, axis=-1, keepdims=True) + EPSILON)
        * gain_vector
    )


def rotate(values, cosine_table, sine_table):
    middle = values.shape[-1] // 2
    first_half = values[..., :middle]
    second_half = values[..., middle:]
    return jnp.concatenate(
        [
            first_half * cosine_table - second_half * sine_table,
            second_half * cosine_table + first_half * sine_table,
        ],
        axis=-1,
    )


def angles(positions):
    inverse = THETA ** (-jnp.arange(DR // 2, dtype=jnp.float32) * 2.0 / DR)
    phases = positions.astype(jnp.float32)[:, None] * inverse[None, :]
    return (jnp.cos(phases), jnp.sin(phases))


def gated(inner_out):
    return jax.nn.silu(inner_out[..., 0, :]) * inner_out[..., 1, :]


def masked_scores(queries, key_rows, rotary_rows, visible):
    factor = (DN + DR) ** (-0.5)
    plain_part = jnp.einsum(
        "qhd,khd->hqk", queries[..., :DN], key_rows[..., :DN], preferred_element_type=jnp.float32
    )
    rotary_part = jnp.einsum(
        "qhr,kr->hqk", queries[..., DN:], rotary_rows, preferred_element_type=jnp.float32
    )
    return jnp.where(visible[None], (plain_part + rotary_part) * factor, -1e30)


def swap_shard(value):
    return lax.ppermute(value, "shard", [(0, 1), (1, 0)])


def pair_total(blocks):
    side = lax.axis_index("shard")
    mine = lax.dynamic_index_in_dim(blocks, side, axis=1, keepdims=False)
    theirs = lax.dynamic_index_in_dim(blocks, 1 - side, axis=1, keepdims=False)
    arrived = swap_shard(theirs.astype(jnp.bfloat16))
    return (mine + arrived.astype(jnp.float32)).astype(jnp.bfloat16)


def reduce_over_expert(total):
    rows = total.reshape((-1,) + total.shape[2:])
    return lax.psum_scatter(rows, "expert", scatter_dimension=0, tiled=True).astype(jnp.float32)


def scatter_rows(full, experts):
    blocks = full.reshape((experts, 2, -1) + full.shape[1:])
    return reduce_over_expert(pair_total(blocks))


def gated_pair(gate_part, up_part):
    return jax.nn.silu(gate_part) * up_part


def shards(
    tokens_in,
    cotangent,
    expert_ids,
    attention_gain,
    query_weight,
    latent_down,
    latent_gain,
    latent_up,
    output_weight,
    feedforward_gain,
    router_weight,
    shared_inner,
    shared_outer,
    expert_inner,
    expert_outer,
):
    tok_rows = tokens_in.shape[0]
    experts_all = lax.axis_size("expert")
    shard_count = lax.axis_size("shard")
    devices = experts_all * shard_count
    slot_cap = tok_rows * TOPK * 4 // (3 * experts_all)
    factor = (DN + DR) ** (-0.5)
    side_index = lax.axis_index("shard")
    ordinal = jnp.arange(tok_rows, dtype=jnp.int32)
    positions = jnp.where(side_index == 0, ordinal, tok_rows + ordinal % CL)
    cosine_table, sine_table = angles(positions)
    query_place = ordinal[:, None]
    key_place = ordinal[None, :]
    causal = key_place <= query_place
    same_block = query_place // CL == key_place // CL
    local_mask = jnp.where(side_index == 0, causal, causal & same_block)
    remote_mask = jnp.broadcast_to(side_index == 1, (tok_rows, tok_rows))
    visible = jnp.concatenate([remote_mask, local_mask], axis=1)

    small_sizes = [
        attention_gain.shape[0],
        latent_gain.shape[0],
        feedforward_gain.shape[0],
        router_weight.size,
    ]
    small_local = jnp.concatenate(
        [attention_gain, latent_gain, feedforward_gain, router_weight.reshape(-1)]
    )
    width = latent_down.shape[1]
    small_rows = -(-small_local.shape[0] // width)
    small_local = jnp.concatenate(
        [small_local, jnp.zeros((small_rows * width - small_local.shape[0],), jnp.bfloat16)]
    ).reshape(small_rows, width)
    down_rows = latent_down.shape[0]
    down_all = lax.all_gather(
        jnp.concatenate([latent_down, small_local], axis=0), ALL, axis=0, tiled=False
    )
    down_full = down_all[:, :down_rows].reshape(-1, width)
    small_all = down_all[:, down_rows:].reshape(devices, -1)
    cuts = [0]
    for size in small_sizes:
        cuts.append(cuts[-1] + size)
    gain_one_float = small_all[:, cuts[0] : cuts[1]].reshape(-1).astype(jnp.float32)
    gain_latent_float = small_all[:, cuts[1] : cuts[2]].reshape(-1).astype(jnp.float32)
    gain_two_float = small_all[:, cuts[2] : cuts[3]].reshape(-1).astype(jnp.float32)
    router_full = small_all[:, cuts[3] : cuts[4]].reshape(-1, router_weight.shape[1])

    query_width = query_weight.shape[1]
    query_output_full = lax.all_gather(
        jnp.concatenate([query_weight, output_weight.T], axis=1), ALL, axis=0, tiled=True
    )
    query_full = query_output_full[:, :query_width]
    output_t_full = query_output_full[:, query_width:]
    up_full = lax.all_gather(latent_up, ALL, axis=0, tiled=True)
    inner_rows = shared_inner.shape[0] * shared_inner.shape[1]
    ffn_all = lax.all_gather(
        jnp.concatenate(
            [shared_inner.reshape(inner_rows, shared_inner.shape[-1]), shared_outer.T], axis=0
        ),
        ALL,
        axis=0,
        tiled=False,
    )
    shared_in_full = [
        ffn_all[:, g * shared_inner.shape[1] : (g + 1) * shared_inner.shape[1]].reshape(
            -1, shared_inner.shape[-1]
        )
        for g in range(shared_inner.shape[0])
    ]
    shared_out_t_full = ffn_all[:, inner_rows:].reshape(-1, shared_inner.shape[-1])

    inner_halves = (expert_inner[0], swap_shard(expert_inner[0]))
    outer_halves = (expert_outer[0], swap_shard(expert_outer[0]))

    tokens_float = tokens_in.astype(jnp.float32)
    normed_one = norm_rows(tokens_float, gain_one_float).astype(jnp.bfloat16)
    query_raw = matmul(normed_one, query_full).reshape(tok_rows, H, DN + DR)
    queries = jnp.concatenate(
        [
            query_raw[..., :DN],
            rotate(query_raw[..., DN:], cosine_table[:, None, :], sine_table[:, None, :]),
        ],
        axis=-1,
    ).astype(jnp.bfloat16)
    down_out = matmul(normed_one, down_full)
    latent_raw = down_out[:, :KVR]
    latents = norm_rows(latent_raw, gain_latent_float).astype(jnp.bfloat16)
    key_rotary = rotate(down_out[:, KVR:], cosine_table, sine_table).astype(jnp.bfloat16)
    expanded = matmul(latents, up_full).astype(jnp.bfloat16).reshape(tok_rows, H, DN + DV)
    kv_local = jnp.concatenate([expanded.reshape(tok_rows, -1), key_rotary], axis=1)
    kv_remote = passed_along(kv_local, "shard", 1)
    remote_expanded = kv_remote[:, : H * (DN + DV)].reshape(tok_rows, H, DN + DV)
    remote_rotary = kv_remote[:, H * (DN + DV) :]
    key_rows = jnp.concatenate([remote_expanded, expanded], axis=0)
    rotary_rows = jnp.concatenate([remote_rotary, key_rotary], axis=0)
    scores = masked_scores(queries, key_rows, rotary_rows, visible)
    score_max = jnp.max(scores, axis=-1, keepdims=True)
    log_total = score_max + jnp.log(jnp.sum(jnp.exp(scores - score_max), axis=-1, keepdims=True))
    weights_float = jnp.exp(scores - log_total)
    weights_low = weights_float.astype(jnp.bfloat16)
    mixed_heads = (
        jnp.einsum(
            "hqk,khd->qhd", weights_low, key_rows[..., DN:], preferred_element_type=jnp.float32
        )
        .astype(jnp.bfloat16)
        .reshape(tok_rows, H * DV)
    )
    attention_out = jnp.einsum(
        "tc,dc->td", mixed_heads, output_t_full, preferred_element_type=jnp.float32
    )
    residual = tokens_float + attention_out
    normed_two = norm_rows(residual, gain_two_float).astype(jnp.bfloat16)
    logits = matmul(normed_two, router_full)
    route_probs = jax.nn.softmax(logits, axis=-1)
    gate_values = jnp.take_along_axis(route_probs, expert_ids, axis=1)
    flat_experts = expert_ids.reshape(-1)
    expert_match = (
        flat_experts[:, None] == jnp.arange(experts_all, dtype=jnp.int32)[None, :]
    ).astype(jnp.int32)
    slot_rank = jnp.sum((jnp.cumsum(expert_match, axis=0) - expert_match) * expert_match, axis=1)
    pair_count = tok_rows * TOPK
    slot_of = flat_experts * slot_cap + slot_rank
    slot_pair = (
        jnp.full((experts_all * slot_cap,), pair_count, jnp.int32)
        .at[slot_of]
        .set(jnp.arange(pair_count, dtype=jnp.int32))
    )
    slot_token = slot_pair // TOPK
    delta_out = cotangent.astype(jnp.float32)
    padded_rows = jnp.concatenate([normed_two, jnp.zeros((1, D), jnp.bfloat16)], axis=0)
    send_rows = jnp.take(padded_rows, slot_token, axis=0)
    padded_gates = jnp.concatenate([gate_values.reshape(-1), jnp.zeros((1,), jnp.float32)])
    slot_gate = jnp.take(padded_gates, slot_pair, axis=0)
    padded_delta = jnp.concatenate([delta_out, jnp.zeros((1, D), jnp.float32)], axis=0)
    send_delta = (jnp.take(padded_delta, slot_token, axis=0) * slot_gate[:, None]).astype(
        jnp.bfloat16
    )
    outgoing = jnp.stack(
        [send_rows.reshape(experts_all, slot_cap, D), send_delta.reshape(experts_all, slot_cap, D)],
        axis=1,
    )
    incoming = lax.all_to_all(outgoing, "expert", split_axis=0, concat_axis=0, tiled=True)
    arrived = incoming[:, 0].reshape(-1, D)
    delta_arrived = incoming[:, 1].reshape(-1, D)

    expert_pre = [
        jnp.einsum("rd,gdf->rgf", arrived, weight, preferred_element_type=jnp.float32)
        for weight in inner_halves
    ]
    expert_hidden = [gated(pre).astype(jnp.bfloat16) for pre in expert_pre]
    expert_result = sum(
        matmul(hidden, weight) for hidden, weight in zip(expert_hidden, outer_halves)
    ).astype(jnp.bfloat16)
    delta_outer_halves = [
        jnp.einsum("rf,rd->fd", hidden, delta_arrived, preferred_element_type=jnp.float32)
        for hidden in expert_hidden
    ]
    delta_pre_halves = []
    for pre, weight in zip(expert_pre, outer_halves):
        delta_hidden = jnp.einsum(
            "rd,fd->rf", delta_arrived, weight, preferred_element_type=jnp.float32
        )
        unused_expert, expert_back = jax.vjp(gated, pre)
        delta_pre_halves.append(expert_back(delta_hidden)[0].astype(jnp.bfloat16))
    delta_inner_halves = [
        jnp.einsum("rd,rgf->gdf", arrived, delta_pre, preferred_element_type=jnp.float32)
        for delta_pre in delta_pre_halves
    ]
    delta_rows = sum(
        jnp.einsum("rgf,gdf->rd", delta_pre, weight, preferred_element_type=jnp.float32)
        for delta_pre, weight in zip(delta_pre_halves, inner_halves)
    ).astype(jnp.bfloat16)
    going_back = jnp.stack(
        [
            expert_result.reshape(experts_all, slot_cap, D),
            delta_rows.reshape(experts_all, slot_cap, D),
        ],
        axis=1,
    )
    coming_back = lax.all_to_all(going_back, "expert", split_axis=0, concat_axis=0, tiled=True)
    returned = coming_back[:, 0].reshape(-1, D)
    delta_returned = coming_back[:, 1].reshape(-1, D)
    inner_from_partner = swap_shard(delta_inner_halves[1].astype(jnp.bfloat16))
    outer_from_partner = swap_shard(delta_outer_halves[1].astype(jnp.bfloat16))
    delta_expert_inner = delta_inner_halves[0] + inner_from_partner.astype(jnp.float32)
    delta_expert_outer = delta_outer_halves[0] + outer_from_partner.astype(jnp.float32)

    picked = jnp.take(returned, slot_of, axis=0).reshape(tok_rows, TOPK, D).astype(jnp.float32)
    routed = jnp.sum(gate_values[..., None] * picked, axis=1)
    shared_gate = matmul(normed_two, shared_in_full[0])
    shared_up = matmul(normed_two, shared_in_full[1])
    shared_hidden = gated_pair(shared_gate, shared_up).astype(jnp.bfloat16)
    shared_result = jnp.einsum(
        "tf,df->td", shared_hidden, shared_out_t_full, preferred_element_type=jnp.float32
    )
    feedforward = routed + shared_result
    layer_output = (residual + feedforward).astype(jnp.bfloat16)
    square_sums = jnp.stack(
        [
            jnp.sum(residual * residual),
            jnp.sum(attention_out * attention_out),
            jnp.sum(feedforward * feedforward),
        ]
    )

    delta_shared_outer_t = jnp.einsum(
        "td,tf->df", cotangent, shared_hidden, preferred_element_type=jnp.float32
    )
    delta_shared_hidden = jnp.einsum(
        "td,df->tf", cotangent, shared_out_t_full, preferred_element_type=jnp.float32
    )
    unused_shared, shared_back = jax.vjp(gated_pair, shared_gate, shared_up)
    delta_gate, delta_up = [
        part.astype(jnp.bfloat16) for part in shared_back(delta_shared_hidden)
    ]
    delta_shared_inner = jnp.stack(
        [
            jnp.einsum("td,tf->df", normed_two, part, preferred_element_type=jnp.float32)
            for part in (delta_gate, delta_up)
        ]
    )
    delta_normed = matmul(delta_gate, shared_in_full[0].T) + matmul(
        delta_up, shared_in_full[1].T
    )
    delta_gates = jnp.sum(delta_out[:, None, :] * picked, axis=-1)
    delta_normed = delta_normed + jnp.sum(
        jnp.take(delta_returned, slot_of, axis=0).reshape(tok_rows, TOPK, D).astype(jnp.float32),
        axis=1,
    )
    match_float = expert_match.reshape(tok_rows, TOPK, experts_all).astype(jnp.float32)
    delta_probs = jnp.einsum("tk,tke->te", delta_gates, match_float)
    delta_logits = (
        route_probs * (delta_probs - jnp.sum(route_probs * delta_probs, axis=-1, keepdims=True))
    ).astype(jnp.bfloat16)
    delta_router = jnp.einsum(
        "td,te->de", normed_two, delta_logits, preferred_element_type=jnp.float32
    )
    delta_normed = delta_normed + jnp.einsum(
        "te,de->td", delta_logits, router_full, preferred_element_type=jnp.float32
    )
    unused_second, second_back = jax.vjp(norm_rows, residual, gain_two_float)
    delta_residual_norm, delta_gain_two = second_back(delta_normed)
    delta_residual = delta_out + delta_residual_norm
    inner_grad_blocks = jnp.transpose(
        delta_shared_inner.reshape(
            (shared_inner.shape[0], experts_all, shard_count) + shared_inner.shape[1:]
        ),
        (1, 2, 0, 3, 4),
    ).reshape((experts_all, shard_count, -1, shared_inner.shape[-1]))
    outer_grad_blocks = delta_shared_outer_t.reshape(
        (experts_all, shard_count, -1, delta_shared_outer_t.shape[-1])
    )
    ffn_total = jnp.concatenate(
        [pair_total(inner_grad_blocks), pair_total(outer_grad_blocks)], axis=1
    )
    ffn_local = reduce_over_expert(ffn_total)
    delta_shared_inner_local = ffn_local[:inner_rows].reshape(shared_inner.shape)
    delta_shared_outer_local = ffn_local[inner_rows:].T

    delta_attention = delta_residual.astype(jnp.bfloat16)
    delta_output_t = jnp.einsum(
        "td,tc->dc", delta_attention, mixed_heads, preferred_element_type=jnp.float32
    )
    delta_output_local = scatter_rows(delta_output_t, experts_all).T
    delta_mixed = (
        jnp.einsum("td,dc->tc", delta_attention, output_t_full, preferred_element_type=jnp.float32)
        .astype(jnp.bfloat16)
        .reshape(tok_rows, H, DV)
    )
    delta_weights = jnp.einsum(
        "qhd,khd->hqk", delta_mixed, key_rows[..., DN:], preferred_element_type=jnp.float32
    )
    delta_scores = (
        weights_float
        * (delta_weights - jnp.sum(weights_float * delta_weights, axis=-1, keepdims=True))
    ).astype(jnp.bfloat16)
    delta_values = jnp.einsum(
        "hqk,qhd->khd", weights_low, delta_mixed, preferred_element_type=jnp.float32
    )
    delta_query_plain = (
        jnp.einsum(
            "hqk,khd->qhd", delta_scores, key_rows[..., :DN], preferred_element_type=jnp.float32
        )
        * factor
    )
    delta_query_rotary = (
        jnp.einsum("hqk,kr->qhr", delta_scores, rotary_rows, preferred_element_type=jnp.float32)
        * factor
    )
    delta_key_plain = (
        jnp.einsum(
            "hqk,qhd->khd", delta_scores, queries[..., :DN], preferred_element_type=jnp.float32
        )
        * factor
    )
    delta_key_rotary = (
        jnp.einsum(
            "hqk,qhr->kr", delta_scores, queries[..., DN:], preferred_element_type=jnp.float32
        )
        * factor
    )
    delta_key_rows = jnp.concatenate([delta_key_plain, delta_values], axis=-1)
    back_local = jnp.concatenate(
        [delta_key_rows[:tok_rows].reshape(tok_rows, -1), delta_key_rotary[:tok_rows]], axis=1
    ).astype(jnp.bfloat16)
    back_remote = passed_along(back_local, "shard", -1).astype(jnp.float32)
    back_rows = back_remote[:, : H * (DN + DV)].reshape(tok_rows, H, DN + DV)
    back_rotary = back_remote[:, H * (DN + DV) :]
    delta_expanded = (
        (delta_key_rows[tok_rows:] + back_rows)
        .astype(jnp.bfloat16)
        .reshape(tok_rows, H * (DN + DV))
    )
    delta_rotary_total = delta_key_rotary[tok_rows:] + back_rotary
    delta_latent_up = jnp.einsum(
        "tl,tc->lc", latents, delta_expanded, preferred_element_type=jnp.float32
    )
    delta_latent_up_local = scatter_rows(delta_latent_up, experts_all)
    delta_latents = jnp.einsum(
        "tc,lc->tl", delta_expanded, up_full, preferred_element_type=jnp.float32
    )
    unused_latent, latent_back = jax.vjp(norm_rows, latent_raw, gain_latent_float)
    delta_latent_raw, delta_gain_latent = latent_back(delta_latents)
    delta_down_out = jnp.concatenate(
        [delta_latent_raw, rotate(delta_rotary_total, cosine_table, -sine_table)], axis=-1
    ).astype(jnp.bfloat16)
    delta_latent_down = jnp.einsum(
        "td,tc->dc", normed_one, delta_down_out, preferred_element_type=jnp.float32
    )
    delta_query_raw = (
        jnp.concatenate(
            [
                delta_query_plain,
                rotate(delta_query_rotary, cosine_table[:, None, :], -sine_table[:, None, :]),
            ],
            axis=-1,
        )
        .astype(jnp.bfloat16)
        .reshape(tok_rows, H * (DN + DR))
    )
    delta_query_weight = jnp.einsum(
        "td,tc->dc", normed_one, delta_query_raw, preferred_element_type=jnp.float32
    )
    delta_query_local = scatter_rows(delta_query_weight, experts_all)
    delta_normed_one = jnp.einsum(
        "tc,dc->td", delta_query_raw, query_full, preferred_element_type=jnp.float32
    ) + jnp.einsum("tc,dc->td", delta_down_out, down_full, preferred_element_type=jnp.float32)
    unused_first, first_back = jax.vjp(norm_rows, tokens_float, gain_one_float)
    delta_tokens_norm, delta_gain_one = first_back(delta_normed_one)
    input_gradient = (delta_residual + delta_tokens_norm).astype(jnp.bfloat16)

    small_parts = [
        delta_gain_one.reshape(devices, -1),
        delta_gain_latent.reshape(devices, -1),
        delta_gain_two.reshape(devices, -1),
        delta_router.reshape(devices, -1),
        jnp.broadcast_to(square_sums[None], (devices, 3)),
    ]
    small_packed = jnp.concatenate(small_parts, axis=1)
    grad_rows = down_rows + -(-small_packed.shape[1] // width)
    grad_rows = grad_rows + (-grad_rows) % 8
    small_packed = jnp.concatenate(
        [
            small_packed,
            jnp.zeros(
                (devices, (grad_rows - down_rows) * width - small_packed.shape[1]), jnp.float32
            ),
        ],
        axis=1,
    ).reshape(devices, grad_rows - down_rows, width)
    down_blocks = jnp.concatenate(
        [delta_latent_down.reshape(devices, down_rows, width), small_packed], axis=1
    ).reshape(experts_all, shard_count, grad_rows, width)
    down_local = reduce_over_expert(pair_total(down_blocks))
    delta_latent_down_local = down_local[:down_rows]
    small_sum = down_local[down_rows:].reshape(-1)
    small_cuts = [0]
    for part in small_parts:
        small_cuts.append(small_cuts[-1] + part.shape[1])
    small_pieces = [small_sum[small_cuts[i] : small_cuts[i + 1]] for i in range(len(small_parts))]
    statistics = jnp.sqrt(small_pieces[4] / (tok_rows * D * devices))
    return (
        layer_output,
        input_gradient,
        small_pieces[0],
        delta_query_local,
        delta_latent_down_local,
        small_pieces[1],
        delta_latent_up_local,
        delta_output_local,
        small_pieces[2],
        small_pieces[3].reshape(router_weight.shape),
        delta_shared_inner_local,
        delta_shared_outer_local,
        delta_expert_inner[None],
        delta_expert_outer[None],
        statistics,
    )


def solution(mesh):
    return jax.shard_map(
        shards,
        mesh=mesh,
        in_specs=(
            P(ALL, None),
            P(ALL, None),
            P(ALL, None),
            P(ALL),
            P(ALL, None),
            P(ALL, None),
            P(ALL),
            P(ALL, None),
            P(None, ALL),
            P(ALL),
            P(ALL, None),
            P(None, ALL, None),
            P(None, ALL),
            P("expert", None, None, "shard"),
            P("expert", "shard", None),
        ),
        out_specs=(
            P(ALL, None),
            P(ALL, None),
            P(ALL),
            P(ALL, None),
            P(ALL, None),
            P(ALL),
            P(ALL, None),
            P(None, ALL),
            P(ALL),
            P(ALL, None),
            P(None, ALL, None),
            P(None, ALL),
            P("expert", None, None, "shard"),
            P("expert", "shard", None),
            P(),
        ),
        check_vma=False,
    )
```

```python
import jax
import jax.numpy as jnp
from jax import lax
from jax.sharding import PartitionSpec as P

D = 2048
H = 16
DN = 128
DR = 64
DV = 128
KVR = 512
TOPK = 6
CL = 64

ALL = ("expert", "shard")
EPSILON = 1e-06
THETA = 10000.0


def passed_along(value, axis, steps):
    count = lax.axis_size(axis)
    first, last = (max(0, -steps), min(count, count - steps))
    return lax.ppermute(value, axis, [(source, source + steps) for source in range(first, last)])


def matmul(left_side, right_side):
    return jnp.dot(left_side, right_side, preferred_element_type=jnp.float32)


def norm_rows(values, gain_vector):
    return (
        values
        * lax.rsqrt(jnp.mean(values * values, axis=-1, keepdims=True) + EPSILON)
        * gain_vector
    )


def rotate(values, cosine_table, sine_table):
    middle = values.shape[-1] // 2
    first_half = values[..., :middle]
    second_half = values[..., middle:]
    return jnp.concatenate(
        [
            first_half * cosine_table - second_half * sine_table,
            second_half * cosine_table + first_half * sine_table,
        ],
        axis=-1,
    )


def angles(positions):
    inverse = THETA ** (-jnp.arange(DR // 2, dtype=jnp.float32) * 2.0 / DR)
    phases = positions.astype(jnp.float32)[:, None] * inverse[None, :]
    return (jnp.cos(phases), jnp.sin(phases))


def gated(inner_out):
    return jax.nn.silu(inner_out[..., 0, :]) * inner_out[..., 1, :]


def masked_scores(queries, key_rows, rotary_rows, visible):
    factor = (DN + DR) ** (-0.5)
    plain_part = jnp.einsum(
        "qhd,khd->hqk", queries[..., :DN], key_rows[..., :DN], preferred_element_type=jnp.float32
    )
    rotary_part = jnp.einsum(
        "qhr,kr->hqk", queries[..., DN:], rotary_rows, preferred_element_type=jnp.float32
    )
    return jnp.where(visible[None], (plain_part + rotary_part) * factor, -1e30)


def swap_shard(value):
    return lax.ppermute(value, "shard", [(0, 1), (1, 0)])


def pair_total(blocks):
    side = lax.axis_index("shard")
    mine = lax.dynamic_index_in_dim(blocks, side, axis=1, keepdims=False)
    theirs = lax.dynamic_index_in_dim(blocks, 1 - side, axis=1, keepdims=False)
    arrived = swap_shard(theirs.astype(jnp.bfloat16))
    return (mine + arrived.astype(jnp.float32)).astype(jnp.bfloat16)


def reduce_over_expert(total, by_exchange=False):
    if by_exchange:
        got = lax.all_to_all(total, "expert", split_axis=0, concat_axis=0, tiled=True)
        return jnp.sum(got.astype(jnp.float32), axis=0)
    rows = total.reshape((-1,) + total.shape[2:])
    return lax.psum_scatter(rows, "expert", scatter_dimension=0, tiled=True).astype(jnp.float32)


def scatter_rows(full, experts, by_exchange=False):
    blocks = full.reshape((experts, 2, -1) + full.shape[1:])
    return reduce_over_expert(pair_total(blocks), by_exchange)


def gated_pair(gate_part, up_part):
    return jax.nn.silu(gate_part) * up_part


def shards(
    tokens_in,
    cotangent,
    expert_ids,
    attention_gain,
    query_weight,
    latent_down,
    latent_gain,
    latent_up,
    output_weight,
    feedforward_gain,
    router_weight,
    shared_inner,
    shared_outer,
    expert_inner,
    expert_outer,
):
    tok_rows = tokens_in.shape[0]
    experts_all = lax.axis_size("expert")
    shard_count = lax.axis_size("shard")
    devices = experts_all * shard_count
    slot_cap = tok_rows * TOPK * 4 // (3 * experts_all)
    factor = (DN + DR) ** (-0.5)
    side_index = lax.axis_index("shard")
    ordinal = jnp.arange(tok_rows, dtype=jnp.int32)
    positions = jnp.where(side_index == 0, ordinal, tok_rows + ordinal % CL)
    cosine_table, sine_table = angles(positions)
    query_place = ordinal[:, None]
    key_place = ordinal[None, :]
    causal = key_place <= query_place
    same_block = query_place // CL == key_place // CL
    local_mask = jnp.where(side_index == 0, causal, causal & same_block)
    remote_mask = jnp.broadcast_to(side_index == 1, (tok_rows, tok_rows))
    visible = jnp.concatenate([remote_mask, local_mask], axis=1)

    small_sizes = [
        attention_gain.shape[0],
        latent_gain.shape[0],
        feedforward_gain.shape[0],
        router_weight.size,
    ]
    small_local = jnp.concatenate(
        [attention_gain, latent_gain, feedforward_gain, router_weight.reshape(-1)]
    )
    width = latent_down.shape[1]
    small_rows = -(-small_local.shape[0] // width)
    small_local = jnp.concatenate(
        [small_local, jnp.zeros((small_rows * width - small_local.shape[0],), jnp.bfloat16)]
    ).reshape(small_rows, width)
    down_rows = latent_down.shape[0]
    down_all = lax.all_gather(
        jnp.concatenate([latent_down, small_local], axis=0), ALL, axis=0, tiled=False
    )
    down_full = down_all[:, :down_rows].reshape(-1, width)
    small_all = down_all[:, down_rows:].reshape(devices, -1)
    cuts = [0]
    for size in small_sizes:
        cuts.append(cuts[-1] + size)
    gain_one_float = small_all[:, cuts[0] : cuts[1]].reshape(-1).astype(jnp.float32)
    gain_latent_float = small_all[:, cuts[1] : cuts[2]].reshape(-1).astype(jnp.float32)
    gain_two_float = small_all[:, cuts[2] : cuts[3]].reshape(-1).astype(jnp.float32)
    router_full = small_all[:, cuts[3] : cuts[4]].reshape(-1, router_weight.shape[1])

    query_width = query_weight.shape[1]
    query_output_full = lax.all_gather(
        jnp.concatenate([query_weight, output_weight.T], axis=1), ALL, axis=0, tiled=True
    )
    query_full = query_output_full[:, :query_width]
    output_t_full = query_output_full[:, query_width:]
    up_full = lax.all_gather(latent_up, ALL, axis=0, tiled=True)
    inner_rows = shared_inner.shape[0] * shared_inner.shape[1]
    ffn_all = lax.all_gather(
        jnp.concatenate(
            [shared_inner.reshape(inner_rows, shared_inner.shape[-1]), shared_outer.T], axis=0
        ),
        ALL,
        axis=0,
        tiled=False,
    )
    shared_in_full = [
        ffn_all[:, g * shared_inner.shape[1] : (g + 1) * shared_inner.shape[1]].reshape(
            -1, shared_inner.shape[-1]
        )
        for g in range(shared_inner.shape[0])
    ]
    shared_out_t_full = ffn_all[:, inner_rows:].reshape(-1, shared_inner.shape[-1])

    inner_halves = (expert_inner[0], swap_shard(expert_inner[0]))
    outer_halves = (expert_outer[0], swap_shard(expert_outer[0]))

    tokens_float = tokens_in.astype(jnp.float32)
    normed_one = norm_rows(tokens_float, gain_one_float).astype(jnp.bfloat16)
    query_raw = matmul(normed_one, query_full).reshape(tok_rows, H, DN + DR)
    queries = jnp.concatenate(
        [
            query_raw[..., :DN],
            rotate(query_raw[..., DN:], cosine_table[:, None, :], sine_table[:, None, :]),
        ],
        axis=-1,
    ).astype(jnp.bfloat16)
    down_out = matmul(normed_one, down_full)
    latent_raw = down_out[:, :KVR]
    latents = norm_rows(latent_raw, gain_latent_float).astype(jnp.bfloat16)
    key_rotary = rotate(down_out[:, KVR:], cosine_table, sine_table).astype(jnp.bfloat16)
    expanded = matmul(latents, up_full).astype(jnp.bfloat16).reshape(tok_rows, H, DN + DV)
    kv_local = jnp.concatenate([expanded.reshape(tok_rows, -1), key_rotary], axis=1)
    kv_remote = passed_along(kv_local, "shard", 1)
    remote_expanded = kv_remote[:, : H * (DN + DV)].reshape(tok_rows, H, DN + DV)
    remote_rotary = kv_remote[:, H * (DN + DV) :]
    key_rows = jnp.concatenate([remote_expanded, expanded], axis=0)
    rotary_rows = jnp.concatenate([remote_rotary, key_rotary], axis=0)
    scores = masked_scores(queries, key_rows, rotary_rows, visible)
    score_max = jnp.max(scores, axis=-1, keepdims=True)
    log_total = score_max + jnp.log(jnp.sum(jnp.exp(scores - score_max), axis=-1, keepdims=True))
    weights_float = jnp.exp(scores - log_total)
    weights_low = weights_float.astype(jnp.bfloat16)
    mixed_heads = (
        jnp.einsum(
            "hqk,khd->qhd", weights_low, key_rows[..., DN:], preferred_element_type=jnp.float32
        )
        .astype(jnp.bfloat16)
        .reshape(tok_rows, H * DV)
    )
    attention_out = jnp.einsum(
        "tc,dc->td", mixed_heads, output_t_full, preferred_element_type=jnp.float32
    )
    residual = tokens_float + attention_out
    normed_two = norm_rows(residual, gain_two_float).astype(jnp.bfloat16)
    logits = matmul(normed_two, router_full)
    route_probs = jax.nn.softmax(logits, axis=-1)
    gate_values = jnp.take_along_axis(route_probs, expert_ids, axis=1)
    flat_experts = expert_ids.reshape(-1)
    expert_match = (
        flat_experts[:, None] == jnp.arange(experts_all, dtype=jnp.int32)[None, :]
    ).astype(jnp.int32)
    slot_rank = jnp.sum((jnp.cumsum(expert_match, axis=0) - expert_match) * expert_match, axis=1)
    pair_count = tok_rows * TOPK
    slot_of = flat_experts * slot_cap + slot_rank
    slot_pair = (
        jnp.full((experts_all * slot_cap,), pair_count, jnp.int32)
        .at[slot_of]
        .set(jnp.arange(pair_count, dtype=jnp.int32))
    )
    slot_token = slot_pair // TOPK
    delta_out = cotangent.astype(jnp.float32)
    padded_rows = jnp.concatenate([normed_two, jnp.zeros((1, D), jnp.bfloat16)], axis=0)
    send_rows = jnp.take(padded_rows, slot_token, axis=0)
    padded_gates = jnp.concatenate([gate_values.reshape(-1), jnp.zeros((1,), jnp.float32)])
    slot_gate = jnp.take(padded_gates, slot_pair, axis=0)
    padded_delta = jnp.concatenate([delta_out, jnp.zeros((1, D), jnp.float32)], axis=0)
    send_delta = (jnp.take(padded_delta, slot_token, axis=0) * slot_gate[:, None]).astype(
        jnp.bfloat16
    )
    outgoing = jnp.stack(
        [send_rows.reshape(experts_all, slot_cap, D), send_delta.reshape(experts_all, slot_cap, D)],
        axis=1,
    )
    incoming = lax.all_to_all(outgoing, "expert", split_axis=0, concat_axis=0, tiled=True)
    arrived = incoming[:, 0].reshape(-1, D)
    delta_arrived = incoming[:, 1].reshape(-1, D)

    expert_pre = [
        jnp.einsum("rd,gdf->rgf", arrived, weight, preferred_element_type=jnp.float32)
        for weight in inner_halves
    ]
    expert_hidden = [gated(pre).astype(jnp.bfloat16) for pre in expert_pre]
    expert_result = sum(
        matmul(hidden, weight) for hidden, weight in zip(expert_hidden, outer_halves)
    ).astype(jnp.bfloat16)
    delta_outer_halves = [
        jnp.einsum("rf,rd->fd", hidden, delta_arrived, preferred_element_type=jnp.float32)
        for hidden in expert_hidden
    ]
    delta_pre_halves = []
    for pre, weight in zip(expert_pre, outer_halves):
        delta_hidden = jnp.einsum(
            "rd,fd->rf", delta_arrived, weight, preferred_element_type=jnp.float32
        )
        unused_expert, expert_back = jax.vjp(gated, pre)
        delta_pre_halves.append(expert_back(delta_hidden)[0].astype(jnp.bfloat16))
    delta_inner_halves = [
        jnp.einsum("rd,rgf->gdf", arrived, delta_pre, preferred_element_type=jnp.float32)
        for delta_pre in delta_pre_halves
    ]
    delta_rows = sum(
        jnp.einsum("rgf,gdf->rd", delta_pre, weight, preferred_element_type=jnp.float32)
        for delta_pre, weight in zip(delta_pre_halves, inner_halves)
    ).astype(jnp.bfloat16)
    going_back = jnp.stack(
        [
            expert_result.reshape(experts_all, slot_cap, D),
            delta_rows.reshape(experts_all, slot_cap, D),
        ],
        axis=1,
    )
    coming_back = lax.all_to_all(going_back, "expert", split_axis=0, concat_axis=0, tiled=True)
    returned = coming_back[:, 0].reshape(-1, D)
    delta_returned = coming_back[:, 1].reshape(-1, D)
    inner_from_partner = swap_shard(delta_inner_halves[1].astype(jnp.bfloat16))
    outer_from_partner = swap_shard(delta_outer_halves[1].astype(jnp.bfloat16))
    delta_expert_inner = delta_inner_halves[0] + inner_from_partner.astype(jnp.float32)
    delta_expert_outer = delta_outer_halves[0] + outer_from_partner.astype(jnp.float32)

    picked = jnp.take(returned, slot_of, axis=0).reshape(tok_rows, TOPK, D).astype(jnp.float32)
    routed = jnp.sum(gate_values[..., None] * picked, axis=1)
    shared_gate = matmul(normed_two, shared_in_full[0])
    shared_up = matmul(normed_two, shared_in_full[1])
    shared_hidden = gated_pair(shared_gate, shared_up).astype(jnp.bfloat16)
    shared_result = jnp.einsum(
        "tf,df->td", shared_hidden, shared_out_t_full, preferred_element_type=jnp.float32
    )
    feedforward = routed + shared_result
    layer_output = (residual + feedforward).astype(jnp.bfloat16)
    square_sums = jnp.stack(
        [
            jnp.sum(residual * residual),
            jnp.sum(attention_out * attention_out),
            jnp.sum(feedforward * feedforward),
        ]
    )

    delta_shared_outer_t = jnp.einsum(
        "td,tf->df", cotangent, shared_hidden, preferred_element_type=jnp.float32
    )
    delta_shared_hidden = jnp.einsum(
        "td,df->tf", cotangent, shared_out_t_full, preferred_element_type=jnp.float32
    )
    unused_shared, shared_back = jax.vjp(gated_pair, shared_gate, shared_up)
    delta_gate, delta_up = [
        part.astype(jnp.bfloat16) for part in shared_back(delta_shared_hidden)
    ]
    delta_shared_inner = jnp.stack(
        [
            jnp.einsum("td,tf->df", normed_two, part, preferred_element_type=jnp.float32)
            for part in (delta_gate, delta_up)
        ]
    )
    delta_normed = matmul(delta_gate, shared_in_full[0].T) + matmul(
        delta_up, shared_in_full[1].T
    )
    delta_gates = jnp.sum(delta_out[:, None, :] * picked, axis=-1)
    delta_normed = delta_normed + jnp.sum(
        jnp.take(delta_returned, slot_of, axis=0).reshape(tok_rows, TOPK, D).astype(jnp.float32),
        axis=1,
    )
    match_float = expert_match.reshape(tok_rows, TOPK, experts_all).astype(jnp.float32)
    delta_probs = jnp.einsum("tk,tke->te", delta_gates, match_float)
    delta_logits = (
        route_probs * (delta_probs - jnp.sum(route_probs * delta_probs, axis=-1, keepdims=True))
    ).astype(jnp.bfloat16)
    delta_router = jnp.einsum(
        "td,te->de", normed_two, delta_logits, preferred_element_type=jnp.float32
    )
    delta_normed = delta_normed + jnp.einsum(
        "te,de->td", delta_logits, router_full, preferred_element_type=jnp.float32
    )
    unused_second, second_back = jax.vjp(norm_rows, residual, gain_two_float)
    delta_residual_norm, delta_gain_two = second_back(delta_normed)
    delta_residual = delta_out + delta_residual_norm
    inner_grad_blocks = jnp.transpose(
        delta_shared_inner.reshape(
            (shared_inner.shape[0], experts_all, shard_count) + shared_inner.shape[1:]
        ),
        (1, 2, 0, 3, 4),
    ).reshape((experts_all, shard_count, -1, shared_inner.shape[-1]))
    outer_grad_blocks = delta_shared_outer_t.reshape(
        (experts_all, shard_count, -1, delta_shared_outer_t.shape[-1])
    )
    ffn_total = jnp.concatenate(
        [pair_total(inner_grad_blocks), pair_total(outer_grad_blocks)], axis=1
    )
    ffn_local = reduce_over_expert(ffn_total, by_exchange=True)
    delta_shared_inner_local = ffn_local[:inner_rows].reshape(shared_inner.shape)
    delta_shared_outer_local = ffn_local[inner_rows:].T

    delta_attention = delta_residual.astype(jnp.bfloat16)
    delta_output_t = jnp.einsum(
        "td,tc->dc", delta_attention, mixed_heads, preferred_element_type=jnp.float32
    )
    delta_output_local = scatter_rows(delta_output_t, experts_all).T
    delta_mixed = (
        jnp.einsum("td,dc->tc", delta_attention, output_t_full, preferred_element_type=jnp.float32)
        .astype(jnp.bfloat16)
        .reshape(tok_rows, H, DV)
    )
    delta_weights = jnp.einsum(
        "qhd,khd->hqk", delta_mixed, key_rows[..., DN:], preferred_element_type=jnp.float32
    )
    delta_scores = (
        weights_float
        * (delta_weights - jnp.sum(weights_float * delta_weights, axis=-1, keepdims=True))
    ).astype(jnp.bfloat16)
    delta_values = jnp.einsum(
        "hqk,qhd->khd", weights_low, delta_mixed, preferred_element_type=jnp.float32
    )
    delta_query_plain = (
        jnp.einsum(
            "hqk,khd->qhd", delta_scores, key_rows[..., :DN], preferred_element_type=jnp.float32
        )
        * factor
    )
    delta_query_rotary = (
        jnp.einsum("hqk,kr->qhr", delta_scores, rotary_rows, preferred_element_type=jnp.float32)
        * factor
    )
    delta_key_plain = (
        jnp.einsum(
            "hqk,qhd->khd", delta_scores, queries[..., :DN], preferred_element_type=jnp.float32
        )
        * factor
    )
    delta_key_rotary = (
        jnp.einsum(
            "hqk,qhr->kr", delta_scores, queries[..., DN:], preferred_element_type=jnp.float32
        )
        * factor
    )
    delta_key_rows = jnp.concatenate([delta_key_plain, delta_values], axis=-1)
    back_local = jnp.concatenate(
        [delta_key_rows[:tok_rows].reshape(tok_rows, -1), delta_key_rotary[:tok_rows]], axis=1
    ).astype(jnp.bfloat16)
    back_remote = passed_along(back_local, "shard", -1).astype(jnp.float32)
    back_rows = back_remote[:, : H * (DN + DV)].reshape(tok_rows, H, DN + DV)
    back_rotary = back_remote[:, H * (DN + DV) :]
    delta_expanded = (
        (delta_key_rows[tok_rows:] + back_rows)
        .astype(jnp.bfloat16)
        .reshape(tok_rows, H * (DN + DV))
    )
    delta_rotary_total = delta_key_rotary[tok_rows:] + back_rotary
    delta_latent_up = jnp.einsum(
        "tl,tc->lc", latents, delta_expanded, preferred_element_type=jnp.float32
    )
    delta_latent_up_local = scatter_rows(delta_latent_up, experts_all)
    delta_latents = jnp.einsum(
        "tc,lc->tl", delta_expanded, up_full, preferred_element_type=jnp.float32
    )
    unused_latent, latent_back = jax.vjp(norm_rows, latent_raw, gain_latent_float)
    delta_latent_raw, delta_gain_latent = latent_back(delta_latents)
    delta_down_out = jnp.concatenate(
        [delta_latent_raw, rotate(delta_rotary_total, cosine_table, -sine_table)], axis=-1
    ).astype(jnp.bfloat16)
    delta_latent_down = jnp.einsum(
        "td,tc->dc", normed_one, delta_down_out, preferred_element_type=jnp.float32
    )
    delta_query_raw = (
        jnp.concatenate(
            [
                delta_query_plain,
                rotate(delta_query_rotary, cosine_table[:, None, :], -sine_table[:, None, :]),
            ],
            axis=-1,
        )
        .astype(jnp.bfloat16)
        .reshape(tok_rows, H * (DN + DR))
    )
    delta_query_weight = jnp.einsum(
        "td,tc->dc", normed_one, delta_query_raw, preferred_element_type=jnp.float32
    )
    delta_query_local = scatter_rows(delta_query_weight, experts_all, by_exchange=True)
    delta_normed_one = jnp.einsum(
        "tc,dc->td", delta_query_raw, query_full, preferred_element_type=jnp.float32
    ) + jnp.einsum("tc,dc->td", delta_down_out, down_full, preferred_element_type=jnp.float32)
    unused_first, first_back = jax.vjp(norm_rows, tokens_float, gain_one_float)
    delta_tokens_norm, delta_gain_one = first_back(delta_normed_one)
    input_gradient = (delta_residual + delta_tokens_norm).astype(jnp.bfloat16)

    small_parts = [
        delta_gain_one.reshape(devices, -1),
        delta_gain_latent.reshape(devices, -1),
        delta_gain_two.reshape(devices, -1),
        delta_router.reshape(devices, -1),
        jnp.broadcast_to(square_sums[None], (devices, 3)),
    ]
    small_packed = jnp.concatenate(small_parts, axis=1)
    grad_rows = down_rows + -(-small_packed.shape[1] // width)
    grad_rows = grad_rows + (-grad_rows) % 8
    small_packed = jnp.concatenate(
        [
            small_packed,
            jnp.zeros(
                (devices, (grad_rows - down_rows) * width - small_packed.shape[1]), jnp.float32
            ),
        ],
        axis=1,
    ).reshape(devices, grad_rows - down_rows, width)
    down_blocks = jnp.concatenate(
        [delta_latent_down.reshape(devices, down_rows, width), small_packed], axis=1
    ).reshape(experts_all, shard_count, grad_rows, width)
    down_local = reduce_over_expert(pair_total(down_blocks))
    delta_latent_down_local = down_local[:down_rows]
    small_sum = down_local[down_rows:].reshape(-1)
    small_cuts = [0]
    for part in small_parts:
        small_cuts.append(small_cuts[-1] + part.shape[1])
    small_pieces = [small_sum[small_cuts[i] : small_cuts[i + 1]] for i in range(len(small_parts))]
    statistics = jnp.sqrt(small_pieces[4] / (tok_rows * D * devices))
    return (
        layer_output,
        input_gradient,
        small_pieces[0],
        delta_query_local,
        delta_latent_down_local,
        small_pieces[1],
        delta_latent_up_local,
        delta_output_local,
        small_pieces[2],
        small_pieces[3].reshape(router_weight.shape),
        delta_shared_inner_local,
        delta_shared_outer_local,
        delta_expert_inner[None],
        delta_expert_outer[None],
        statistics,
    )


def solution(mesh):
    return jax.shard_map(
        shards,
        mesh=mesh,
        in_specs=(
            P(ALL, None),
            P(ALL, None),
            P(ALL, None),
            P(ALL),
            P(ALL, None),
            P(ALL, None),
            P(ALL),
            P(ALL, None),
            P(None, ALL),
            P(ALL),
            P(ALL, None),
            P(None, ALL, None),
            P(None, ALL),
            P("expert", None, None, "shard"),
            P("expert", "shard", None),
        ),
        out_specs=(
            P(ALL, None),
            P(ALL, None),
            P(ALL),
            P(ALL, None),
            P(ALL, None),
            P(ALL),
            P(ALL, None),
            P(None, ALL),
            P(ALL),
            P(ALL, None),
            P(None, ALL, None),
            P(None, ALL),
            P("expert", None, None, "shard"),
            P("expert", "shard", None),
            P(),
        ),
        check_vma=False,
    )
```

```python
import jax
import jax.numpy as jnp
from jax import lax
from jax.sharding import PartitionSpec as P

D = 2048
H = 16
DN = 128
DR = 64
DV = 128
KVR = 512
TOPK = 6
CL = 64

ALL = ("expert", "shard")
EPSILON = 1e-06
THETA = 10000.0


def passed_along(value, axis, steps):
    count = lax.axis_size(axis)
    first, last = (max(0, -steps), min(count, count - steps))
    return lax.ppermute(value, axis, [(source, source + steps) for source in range(first, last)])


def matmul(left_side, right_side):
    return jnp.dot(left_side, right_side, preferred_element_type=jnp.float32)


def norm_rows(values, gain_vector):
    return (
        values
        * lax.rsqrt(jnp.mean(values * values, axis=-1, keepdims=True) + EPSILON)
        * gain_vector
    )


def rotate(values, cosine_table, sine_table):
    middle = values.shape[-1] // 2
    first_half = values[..., :middle]
    second_half = values[..., middle:]
    return jnp.concatenate(
        [
            first_half * cosine_table - second_half * sine_table,
            second_half * cosine_table + first_half * sine_table,
        ],
        axis=-1,
    )


def angles(positions):
    inverse = THETA ** (-jnp.arange(DR // 2, dtype=jnp.float32) * 2.0 / DR)
    phases = positions.astype(jnp.float32)[:, None] * inverse[None, :]
    return (jnp.cos(phases), jnp.sin(phases))


def gated(inner_out):
    return jax.nn.silu(inner_out[..., 0, :]) * inner_out[..., 1, :]


def masked_scores(queries, key_rows, rotary_rows, visible):
    factor = (DN + DR) ** (-0.5)
    plain_part = jnp.einsum(
        "qhd,khd->hqk", queries[..., :DN], key_rows[..., :DN], preferred_element_type=jnp.float32
    )
    rotary_part = jnp.einsum(
        "qhr,kr->hqk", queries[..., DN:], rotary_rows, preferred_element_type=jnp.float32
    )
    return jnp.where(visible[None], (plain_part + rotary_part) * factor, -1e30)


def swap_shard(value):
    return lax.ppermute(value, "shard", [(0, 1), (1, 0)])


def pair_total(blocks):
    side = lax.axis_index("shard")
    mine = lax.dynamic_index_in_dim(blocks, side, axis=1, keepdims=False)
    theirs = lax.dynamic_index_in_dim(blocks, 1 - side, axis=1, keepdims=False)
    arrived = swap_shard(theirs.astype(jnp.bfloat16))
    return (mine + arrived.astype(jnp.float32)).astype(jnp.bfloat16)


def reduce_over_expert(total, by_exchange=False):
    if by_exchange:
        got = lax.all_to_all(total, "expert", split_axis=0, concat_axis=0, tiled=True)
        return jnp.sum(got.astype(jnp.float32), axis=0)
    rows = total.reshape((-1,) + total.shape[2:])
    return lax.psum_scatter(rows, "expert", scatter_dimension=0, tiled=True).astype(jnp.float32)


def scatter_rows(full, experts, by_exchange=False):
    blocks = full.reshape((experts, 2, -1) + full.shape[1:])
    return reduce_over_expert(pair_total(blocks), by_exchange)


def gated_pair(gate_part, up_part):
    return jax.nn.silu(gate_part) * up_part


def shards(
    tokens_in,
    cotangent,
    expert_ids,
    attention_gain,
    query_weight,
    latent_down,
    latent_gain,
    latent_up,
    output_weight,
    feedforward_gain,
    router_weight,
    shared_inner,
    shared_outer,
    expert_inner,
    expert_outer,
):
    tok_rows = tokens_in.shape[0]
    experts_all = lax.axis_size("expert")
    shard_count = lax.axis_size("shard")
    devices = experts_all * shard_count
    slot_cap = tok_rows * TOPK * 4 // (3 * experts_all)
    factor = (DN + DR) ** (-0.5)
    side_index = lax.axis_index("shard")
    ordinal = jnp.arange(tok_rows, dtype=jnp.int32)
    positions = jnp.where(side_index == 0, ordinal, tok_rows + ordinal % CL)
    cosine_table, sine_table = angles(positions)
    query_place = ordinal[:, None]
    key_place = ordinal[None, :]
    causal = key_place <= query_place
    same_block = query_place // CL == key_place // CL
    local_mask = jnp.where(side_index == 0, causal, causal & same_block)
    remote_mask = jnp.broadcast_to(side_index == 1, (tok_rows, tok_rows))
    visible = jnp.concatenate([remote_mask, local_mask], axis=1)

    small_sizes = [
        attention_gain.shape[0],
        latent_gain.shape[0],
        feedforward_gain.shape[0],
        router_weight.size,
    ]
    small_local = jnp.concatenate(
        [attention_gain, latent_gain, feedforward_gain, router_weight.reshape(-1)]
    )
    width = latent_down.shape[1]
    small_rows = -(-small_local.shape[0] // width)
    small_local = jnp.concatenate(
        [small_local, jnp.zeros((small_rows * width - small_local.shape[0],), jnp.bfloat16)]
    ).reshape(small_rows, width)
    down_rows = latent_down.shape[0]
    down_all = lax.all_gather(
        jnp.concatenate([latent_down, small_local], axis=0), ALL, axis=0, tiled=False
    )
    down_full = down_all[:, :down_rows].reshape(-1, width)
    small_all = down_all[:, down_rows:].reshape(devices, -1)
    cuts = [0]
    for size in small_sizes:
        cuts.append(cuts[-1] + size)
    gain_one_float = small_all[:, cuts[0] : cuts[1]].reshape(-1).astype(jnp.float32)
    gain_latent_float = small_all[:, cuts[1] : cuts[2]].reshape(-1).astype(jnp.float32)
    gain_two_float = small_all[:, cuts[2] : cuts[3]].reshape(-1).astype(jnp.float32)
    router_full = small_all[:, cuts[3] : cuts[4]].reshape(-1, router_weight.shape[1])

    query_width = query_weight.shape[1]
    query_output_full = lax.all_gather(
        jnp.concatenate([query_weight, output_weight.T], axis=1), ALL, axis=0, tiled=True
    )
    query_full = query_output_full[:, :query_width]
    output_t_full = query_output_full[:, query_width:]
    up_full = lax.all_gather(latent_up, ALL, axis=0, tiled=True)
    inner_rows = shared_inner.shape[0] * shared_inner.shape[1]
    ffn_all = lax.all_gather(
        jnp.concatenate(
            [shared_inner.reshape(inner_rows, shared_inner.shape[-1]), shared_outer.T], axis=0
        ),
        ALL,
        axis=0,
        tiled=False,
    )
    shared_in_full = [
        ffn_all[:, g * shared_inner.shape[1] : (g + 1) * shared_inner.shape[1]].reshape(
            -1, shared_inner.shape[-1]
        )
        for g in range(shared_inner.shape[0])
    ]
    shared_out_t_full = ffn_all[:, inner_rows:].reshape(-1, shared_inner.shape[-1])

    inner_halves = (expert_inner[0], swap_shard(expert_inner[0]))
    outer_halves = (expert_outer[0], swap_shard(expert_outer[0]))

    tokens_float = tokens_in.astype(jnp.float32)
    normed_one = norm_rows(tokens_float, gain_one_float).astype(jnp.bfloat16)
    query_raw = matmul(normed_one, query_full).reshape(tok_rows, H, DN + DR)
    queries = jnp.concatenate(
        [
            query_raw[..., :DN],
            rotate(query_raw[..., DN:], cosine_table[:, None, :], sine_table[:, None, :]),
        ],
        axis=-1,
    ).astype(jnp.bfloat16)
    down_out = matmul(normed_one, down_full)
    latent_raw = down_out[:, :KVR]
    latents = norm_rows(latent_raw, gain_latent_float).astype(jnp.bfloat16)
    key_rotary = rotate(down_out[:, KVR:], cosine_table, sine_table).astype(jnp.bfloat16)
    expanded = matmul(latents, up_full).astype(jnp.bfloat16).reshape(tok_rows, H, DN + DV)
    kv_local = jnp.concatenate([expanded.reshape(tok_rows, -1), key_rotary], axis=1)
    kv_remote = passed_along(kv_local, "shard", 1)
    remote_expanded = kv_remote[:, : H * (DN + DV)].reshape(tok_rows, H, DN + DV)
    remote_rotary = kv_remote[:, H * (DN + DV) :]
    key_rows = jnp.concatenate([remote_expanded, expanded], axis=0)
    rotary_rows = jnp.concatenate([remote_rotary, key_rotary], axis=0)
    scores = masked_scores(queries, key_rows, rotary_rows, visible)
    score_max = jnp.max(scores, axis=-1, keepdims=True)
    log_total = score_max + jnp.log(jnp.sum(jnp.exp(scores - score_max), axis=-1, keepdims=True))
    weights_float = jnp.exp(scores - log_total)
    weights_low = weights_float.astype(jnp.bfloat16)
    mixed_heads = (
        jnp.einsum(
            "hqk,khd->qhd", weights_low, key_rows[..., DN:], preferred_element_type=jnp.float32
        )
        .astype(jnp.bfloat16)
        .reshape(tok_rows, H * DV)
    )
    attention_out = jnp.einsum(
        "tc,dc->td", mixed_heads, output_t_full, preferred_element_type=jnp.float32
    )
    residual = tokens_float + attention_out
    normed_two = norm_rows(residual, gain_two_float).astype(jnp.bfloat16)
    logits = matmul(normed_two, router_full)
    route_probs = jax.nn.softmax(logits, axis=-1)
    gate_values = jnp.take_along_axis(route_probs, expert_ids, axis=1)
    flat_experts = expert_ids.reshape(-1)
    expert_match = (
        flat_experts[:, None] == jnp.arange(experts_all, dtype=jnp.int32)[None, :]
    ).astype(jnp.int32)
    slot_rank = jnp.sum((jnp.cumsum(expert_match, axis=0) - expert_match) * expert_match, axis=1)
    pair_count = tok_rows * TOPK
    slot_of = flat_experts * slot_cap + slot_rank
    slot_pair = (
        jnp.full((experts_all * slot_cap,), pair_count, jnp.int32)
        .at[slot_of]
        .set(jnp.arange(pair_count, dtype=jnp.int32))
    )
    slot_token = slot_pair // TOPK
    delta_out = cotangent.astype(jnp.float32)
    padded_rows = jnp.concatenate([normed_two, jnp.zeros((1, D), jnp.bfloat16)], axis=0)
    send_rows = jnp.take(padded_rows, slot_token, axis=0)
    padded_gates = jnp.concatenate([gate_values.reshape(-1), jnp.zeros((1,), jnp.float32)])
    slot_gate = jnp.take(padded_gates, slot_pair, axis=0)
    padded_delta = jnp.concatenate([delta_out, jnp.zeros((1, D), jnp.float32)], axis=0)
    send_delta = (jnp.take(padded_delta, slot_token, axis=0) * slot_gate[:, None]).astype(
        jnp.bfloat16
    )
    outgoing = jnp.stack(
        [send_rows.reshape(experts_all, slot_cap, D), send_delta.reshape(experts_all, slot_cap, D)],
        axis=1,
    )
    incoming = lax.all_to_all(outgoing, "expert", split_axis=0, concat_axis=0, tiled=True)
    arrived = incoming[:, 0].reshape(-1, D)
    delta_arrived = incoming[:, 1].reshape(-1, D)

    expert_pre = [
        jnp.einsum("rd,gdf->rgf", arrived, weight, preferred_element_type=jnp.float32)
        for weight in inner_halves
    ]
    expert_hidden = [gated(pre).astype(jnp.bfloat16) for pre in expert_pre]
    expert_result = sum(
        matmul(hidden, weight) for hidden, weight in zip(expert_hidden, outer_halves)
    ).astype(jnp.bfloat16)
    delta_outer_halves = [
        jnp.einsum("rf,rd->fd", hidden, delta_arrived, preferred_element_type=jnp.float32)
        for hidden in expert_hidden
    ]
    delta_pre_halves = []
    for pre, weight in zip(expert_pre, outer_halves):
        delta_hidden = jnp.einsum(
            "rd,fd->rf", delta_arrived, weight, preferred_element_type=jnp.float32
        )
        unused_expert, expert_back = jax.vjp(gated, pre)
        delta_pre_halves.append(expert_back(delta_hidden)[0].astype(jnp.bfloat16))
    delta_inner_halves = [
        jnp.einsum("rd,rgf->gdf", arrived, delta_pre, preferred_element_type=jnp.float32)
        for delta_pre in delta_pre_halves
    ]
    delta_rows = sum(
        jnp.einsum("rgf,gdf->rd", delta_pre, weight, preferred_element_type=jnp.float32)
        for delta_pre, weight in zip(delta_pre_halves, inner_halves)
    ).astype(jnp.bfloat16)
    going_back = jnp.stack(
        [
            expert_result.reshape(experts_all, slot_cap, D),
            delta_rows.reshape(experts_all, slot_cap, D),
        ],
        axis=1,
    )
    coming_back = lax.all_to_all(going_back, "expert", split_axis=0, concat_axis=0, tiled=True)
    returned = coming_back[:, 0].reshape(-1, D)
    delta_returned = coming_back[:, 1].reshape(-1, D)
    inner_from_partner = swap_shard(delta_inner_halves[1].astype(jnp.bfloat16))
    outer_from_partner = swap_shard(delta_outer_halves[1].astype(jnp.bfloat16))
    delta_expert_inner = delta_inner_halves[0] + inner_from_partner.astype(jnp.float32)
    delta_expert_outer = delta_outer_halves[0] + outer_from_partner.astype(jnp.float32)

    picked = jnp.take(returned, slot_of, axis=0).reshape(tok_rows, TOPK, D).astype(jnp.float32)
    routed = jnp.sum(gate_values[..., None] * picked, axis=1)
    shared_gate = matmul(normed_two, shared_in_full[0])
    shared_up = matmul(normed_two, shared_in_full[1])
    shared_hidden = gated_pair(shared_gate, shared_up).astype(jnp.bfloat16)
    shared_result = jnp.einsum(
        "tf,df->td", shared_hidden, shared_out_t_full, preferred_element_type=jnp.float32
    )
    feedforward = routed + shared_result
    layer_output = (residual + feedforward).astype(jnp.bfloat16)
    square_sums = jnp.stack(
        [
            jnp.sum(residual * residual),
            jnp.sum(attention_out * attention_out),
            jnp.sum(feedforward * feedforward),
        ]
    )

    delta_shared_outer_t = jnp.einsum(
        "td,tf->df", cotangent, shared_hidden, preferred_element_type=jnp.float32
    )
    delta_shared_hidden = jnp.einsum(
        "td,df->tf", cotangent, shared_out_t_full, preferred_element_type=jnp.float32
    )
    unused_shared, shared_back = jax.vjp(gated_pair, shared_gate, shared_up)
    delta_gate, delta_up = [
        part.astype(jnp.bfloat16) for part in shared_back(delta_shared_hidden)
    ]
    delta_shared_inner = jnp.stack(
        [
            jnp.einsum("td,tf->df", normed_two, part, preferred_element_type=jnp.float32)
            for part in (delta_gate, delta_up)
        ]
    )
    delta_normed = matmul(delta_gate, shared_in_full[0].T) + matmul(
        delta_up, shared_in_full[1].T
    )
    delta_gates = jnp.sum(delta_out[:, None, :] * picked, axis=-1)
    delta_normed = delta_normed + jnp.sum(
        jnp.take(delta_returned, slot_of, axis=0).reshape(tok_rows, TOPK, D).astype(jnp.float32),
        axis=1,
    )
    match_float = expert_match.reshape(tok_rows, TOPK, experts_all).astype(jnp.float32)
    delta_probs = jnp.einsum("tk,tke->te", delta_gates, match_float)
    delta_logits = (
        route_probs * (delta_probs - jnp.sum(route_probs * delta_probs, axis=-1, keepdims=True))
    ).astype(jnp.bfloat16)
    delta_router = jnp.einsum(
        "td,te->de", normed_two, delta_logits, preferred_element_type=jnp.float32
    )
    delta_normed = delta_normed + jnp.einsum(
        "te,de->td", delta_logits, router_full, preferred_element_type=jnp.float32
    )
    unused_second, second_back = jax.vjp(norm_rows, residual, gain_two_float)
    delta_residual_norm, delta_gain_two = second_back(delta_normed)
    delta_residual = delta_out + delta_residual_norm
    inner_grad_blocks = jnp.transpose(
        delta_shared_inner.reshape(
            (shared_inner.shape[0], experts_all, shard_count) + shared_inner.shape[1:]
        ),
        (1, 2, 0, 3, 4),
    ).reshape((experts_all, shard_count, -1, shared_inner.shape[-1]))
    outer_grad_blocks = delta_shared_outer_t.reshape(
        (experts_all, shard_count, -1, delta_shared_outer_t.shape[-1])
    )
    ffn_total = jnp.concatenate(
        [pair_total(inner_grad_blocks), pair_total(outer_grad_blocks)], axis=1
    )
    ffn_local = reduce_over_expert(ffn_total, by_exchange=True)
    delta_shared_inner_local = ffn_local[:inner_rows].reshape(shared_inner.shape)
    delta_shared_outer_local = ffn_local[inner_rows:].T

    delta_attention = delta_residual.astype(jnp.bfloat16)
    delta_output_t = jnp.einsum(
        "td,tc->dc", delta_attention, mixed_heads, preferred_element_type=jnp.float32
    )
    delta_output_local = scatter_rows(delta_output_t, experts_all).T
    delta_mixed = (
        jnp.einsum("td,dc->tc", delta_attention, output_t_full, preferred_element_type=jnp.float32)
        .astype(jnp.bfloat16)
        .reshape(tok_rows, H, DV)
    )
    delta_weights = jnp.einsum(
        "qhd,khd->hqk", delta_mixed, key_rows[..., DN:], preferred_element_type=jnp.float32
    )
    delta_scores = (
        weights_float
        * (delta_weights - jnp.sum(weights_float * delta_weights, axis=-1, keepdims=True))
    ).astype(jnp.bfloat16)
    delta_values = jnp.einsum(
        "hqk,qhd->khd", weights_low, delta_mixed, preferred_element_type=jnp.float32
    )
    delta_query_plain = (
        jnp.einsum(
            "hqk,khd->qhd", delta_scores, key_rows[..., :DN], preferred_element_type=jnp.float32
        )
        * factor
    )
    delta_query_rotary = (
        jnp.einsum("hqk,kr->qhr", delta_scores, rotary_rows, preferred_element_type=jnp.float32)
        * factor
    )
    delta_key_plain = (
        jnp.einsum(
            "hqk,qhd->khd", delta_scores, queries[..., :DN], preferred_element_type=jnp.float32
        )
        * factor
    )
    delta_key_rotary = (
        jnp.einsum(
            "hqk,qhr->kr", delta_scores, queries[..., DN:], preferred_element_type=jnp.float32
        )
        * factor
    )
    delta_key_rows = jnp.concatenate([delta_key_plain, delta_values], axis=-1)
    back_local = jnp.concatenate(
        [delta_key_rows[:tok_rows].reshape(tok_rows, -1), delta_key_rotary[:tok_rows]], axis=1
    ).astype(jnp.bfloat16)
    back_remote = passed_along(back_local, "shard", -1).astype(jnp.float32)
    back_rows = back_remote[:, : H * (DN + DV)].reshape(tok_rows, H, DN + DV)
    back_rotary = back_remote[:, H * (DN + DV) :]
    delta_expanded = (
        (delta_key_rows[tok_rows:] + back_rows)
        .astype(jnp.bfloat16)
        .reshape(tok_rows, H * (DN + DV))
    )
    delta_rotary_total = delta_key_rotary[tok_rows:] + back_rotary
    delta_latent_up = jnp.einsum(
        "tl,tc->lc", latents, delta_expanded, preferred_element_type=jnp.float32
    )
    delta_latent_up_local = scatter_rows(delta_latent_up, experts_all)
    delta_latents = jnp.einsum(
        "tc,lc->tl", delta_expanded, up_full, preferred_element_type=jnp.float32
    )
    unused_latent, latent_back = jax.vjp(norm_rows, latent_raw, gain_latent_float)
    delta_latent_raw, delta_gain_latent = latent_back(delta_latents)
    delta_down_out = jnp.concatenate(
        [delta_latent_raw, rotate(delta_rotary_total, cosine_table, -sine_table)], axis=-1
    ).astype(jnp.bfloat16)
    delta_latent_down = jnp.einsum(
        "td,tc->dc", normed_one, delta_down_out, preferred_element_type=jnp.float32
    )
    delta_query_raw = (
        jnp.concatenate(
            [
                delta_query_plain,
                rotate(delta_query_rotary, cosine_table[:, None, :], -sine_table[:, None, :]),
            ],
            axis=-1,
        )
        .astype(jnp.bfloat16)
        .reshape(tok_rows, H * (DN + DR))
    )
    delta_query_weight = jnp.einsum(
        "td,tc->dc", normed_one, delta_query_raw, preferred_element_type=jnp.float32
    )
    delta_query_local = scatter_rows(delta_query_weight, experts_all)
    delta_normed_one = jnp.einsum(
        "tc,dc->td", delta_query_raw, query_full, preferred_element_type=jnp.float32
    ) + jnp.einsum("tc,dc->td", delta_down_out, down_full, preferred_element_type=jnp.float32)
    unused_first, first_back = jax.vjp(norm_rows, tokens_float, gain_one_float)
    delta_tokens_norm, delta_gain_one = first_back(delta_normed_one)
    input_gradient = (delta_residual + delta_tokens_norm).astype(jnp.bfloat16)

    small_parts = [
        delta_gain_one.reshape(devices, -1),
        delta_gain_latent.reshape(devices, -1),
        delta_gain_two.reshape(devices, -1),
        delta_router.reshape(devices, -1),
        jnp.broadcast_to(square_sums[None], (devices, 3)),
    ]
    small_packed = jnp.concatenate(small_parts, axis=1)
    grad_rows = down_rows + -(-small_packed.shape[1] // width)
    grad_rows = grad_rows + (-grad_rows) % 8
    small_packed = jnp.concatenate(
        [
            small_packed,
            jnp.zeros(
                (devices, (grad_rows - down_rows) * width - small_packed.shape[1]), jnp.float32
            ),
        ],
        axis=1,
    ).reshape(devices, grad_rows - down_rows, width)
    down_blocks = jnp.concatenate(
        [delta_latent_down.reshape(devices, down_rows, width), small_packed], axis=1
    ).reshape(experts_all, shard_count, grad_rows, width)
    down_local = reduce_over_expert(pair_total(down_blocks))
    delta_latent_down_local = down_local[:down_rows]
    small_sum = down_local[down_rows:].reshape(-1)
    small_cuts = [0]
    for part in small_parts:
        small_cuts.append(small_cuts[-1] + part.shape[1])
    small_pieces = [small_sum[small_cuts[i] : small_cuts[i + 1]] for i in range(len(small_parts))]
    statistics = jnp.sqrt(small_pieces[4] / (tok_rows * D * devices))
    return (
        layer_output,
        input_gradient,
        small_pieces[0],
        delta_query_local,
        delta_latent_down_local,
        small_pieces[1],
        delta_latent_up_local,
        delta_output_local,
        small_pieces[2],
        small_pieces[3].reshape(router_weight.shape),
        delta_shared_inner_local,
        delta_shared_outer_local,
        delta_expert_inner[None],
        delta_expert_outer[None],
        statistics,
    )


def solution(mesh):
    return jax.shard_map(
        shards,
        mesh=mesh,
        in_specs=(
            P(ALL, None),
            P(ALL, None),
            P(ALL, None),
            P(ALL),
            P(ALL, None),
            P(ALL, None),
            P(ALL),
            P(ALL, None),
            P(None, ALL),
            P(ALL),
            P(ALL, None),
            P(None, ALL, None),
            P(None, ALL),
            P("expert", None, None, "shard"),
            P("expert", "shard", None),
        ),
        out_specs=(
            P(ALL, None),
            P(ALL, None),
            P(ALL),
            P(ALL, None),
            P(ALL, None),
            P(ALL),
            P(ALL, None),
            P(None, ALL),
            P(ALL),
            P(ALL, None),
            P(None, ALL, None),
            P(None, ALL),
            P("expert", None, None, "shard"),
            P("expert", "shard", None),
            P(),
        ),
        check_vma=False,
    )
```

```python
import jax
import jax.numpy as jnp
from jax import lax
from jax.sharding import PartitionSpec as P


D = 2048
H = 16
DN = 128
DR = 64
DV = 128
KVR = 512
TOPK = 6
CL = 64

ALL = ("expert", "shard")
EPSILON = 1e-06
THETA = 10000.0


def passed_along(value, axis, steps):
    count = lax.axis_size(axis)
    first, last = (max(0, -steps), min(count, count - steps))
    return lax.ppermute(value, axis, [(source, source + steps) for source in range(first, last)])


def matmul(left_side, right_side):
    return jnp.dot(left_side, right_side, preferred_element_type=jnp.float32)


def norm_rows(values, gain_vector):
    return (
        values
        * lax.rsqrt(jnp.mean(values * values, axis=-1, keepdims=True) + EPSILON)
        * gain_vector
    )


def rotate(values, cosine_table, sine_table):
    middle = values.shape[-1] // 2
    first_half = values[..., :middle]
    second_half = values[..., middle:]
    return jnp.concatenate(
        [
            first_half * cosine_table - second_half * sine_table,
            second_half * cosine_table + first_half * sine_table,
        ],
        axis=-1,
    )


def angles(positions):
    inverse = THETA ** (-jnp.arange(DR // 2, dtype=jnp.float32) * 2.0 / DR)
    phases = positions.astype(jnp.float32)[:, None] * inverse[None, :]
    return (jnp.cos(phases), jnp.sin(phases))


def gated(inner_out):
    return jax.nn.silu(inner_out[..., 0, :]) * inner_out[..., 1, :]


def masked_scores(queries, key_rows, rotary_rows, visible):
    factor = (DN + DR) ** (-0.5)
    plain_part = jnp.einsum(
        "qhd,khd->hqk", queries[..., :DN], key_rows[..., :DN], preferred_element_type=jnp.float32
    )
    rotary_part = jnp.einsum(
        "qhr,kr->hqk", queries[..., DN:], rotary_rows, preferred_element_type=jnp.float32
    )
    return jnp.where(visible[None], (plain_part + rotary_part) * factor, -1e30)


def swap_shard(value):
    return lax.ppermute(value, "shard", [(0, 1), (1, 0)])


def pair_total(blocks):
    side = lax.axis_index("shard")
    mine = lax.dynamic_index_in_dim(blocks, side, axis=1, keepdims=False)
    theirs = lax.dynamic_index_in_dim(blocks, 1 - side, axis=1, keepdims=False)
    arrived = swap_shard(theirs.astype(jnp.bfloat16))
    return (mine + arrived.astype(jnp.float32)).astype(jnp.bfloat16)


def reduce_over_expert(total):
    rows = total.reshape((-1,) + total.shape[2:])
    summed = lax.psum_scatter(rows, "expert", scatter_dimension=0, tiled=True)
    return summed.astype(jnp.float32)


def scatter_rows(full, experts):
    blocks = full.reshape((experts, 2, -1) + full.shape[1:])
    return reduce_over_expert(pair_total(blocks))


def gated_pair(gate_part, up_part):
    return jax.nn.silu(gate_part) * up_part


def shards(
    tokens_in,
    cotangent,
    expert_ids,
    attention_gain,
    query_weight,
    latent_down,
    latent_gain,
    latent_up,
    output_weight,
    feedforward_gain,
    router_weight,
    shared_inner,
    shared_outer,
    expert_inner,
    expert_outer,
):
    tok_rows = tokens_in.shape[0]
    experts_all = lax.axis_size("expert")
    shard_count = lax.axis_size("shard")
    devices = experts_all * shard_count
    slot_cap = tok_rows * TOPK * 4 // (3 * experts_all)
    factor = (DN + DR) ** (-0.5)
    side_index = lax.axis_index("shard")
    ordinal = jnp.arange(tok_rows, dtype=jnp.int32)
    positions = jnp.where(side_index == 0, ordinal, tok_rows + ordinal % CL)
    cosine_table, sine_table = angles(positions)
    query_place = ordinal[:, None]
    key_place = ordinal[None, :]
    causal = key_place <= query_place
    same_block = query_place // CL == key_place // CL
    local_mask = jnp.where(side_index == 0, causal, causal & same_block)
    remote_mask = jnp.broadcast_to(side_index == 1, (tok_rows, tok_rows))
    visible = jnp.concatenate([remote_mask, local_mask], axis=1)

    small_sizes = [
        attention_gain.shape[0],
        latent_gain.shape[0],
        feedforward_gain.shape[0],
        router_weight.size,
    ]
    small_local = jnp.concatenate(
        [attention_gain, latent_gain, feedforward_gain, router_weight.reshape(-1)]
    )
    width = latent_down.shape[1]
    small_rows = -(-small_local.shape[0] // width)
    small_local = jnp.concatenate(
        [small_local, jnp.zeros((small_rows * width - small_local.shape[0],), jnp.bfloat16)]
    ).reshape(small_rows, width)
    down_rows = latent_down.shape[0]
    down_all = lax.all_gather(
        jnp.concatenate([latent_down, small_local], axis=0), ALL, axis=0, tiled=False
    )
    down_full = down_all[:, :down_rows].reshape(-1, width)
    small_all = down_all[:, down_rows:].reshape(devices, -1)
    cuts = [0]
    for size in small_sizes:
        cuts.append(cuts[-1] + size)
    gain_one_float = small_all[:, cuts[0] : cuts[1]].reshape(-1).astype(jnp.float32)
    gain_latent_float = small_all[:, cuts[1] : cuts[2]].reshape(-1).astype(jnp.float32)
    gain_two_float = small_all[:, cuts[2] : cuts[3]].reshape(-1).astype(jnp.float32)
    router_full = small_all[:, cuts[3] : cuts[4]].reshape(-1, router_weight.shape[1])

    query_width = query_weight.shape[1]
    query_output_full = lax.all_gather(
        jnp.concatenate([query_weight, output_weight.T], axis=1), ALL, axis=0, tiled=True
    )
    query_full = query_output_full[:, :query_width]
    output_t_full = query_output_full[:, query_width:]
    up_full = lax.all_gather(latent_up, ALL, axis=0, tiled=True)
    inner_rows = shared_inner.shape[0] * shared_inner.shape[1]
    ffn_all = lax.all_gather(
        jnp.concatenate(
            [shared_inner.reshape(inner_rows, shared_inner.shape[-1]), shared_outer.T], axis=0
        ),
        ALL,
        axis=0,
        tiled=False,
    )
    shared_in_full = [
        ffn_all[:, g * shared_inner.shape[1] : (g + 1) * shared_inner.shape[1]].reshape(
            -1, shared_inner.shape[-1]
        )
        for g in range(shared_inner.shape[0])
    ]
    shared_out_t_full = ffn_all[:, inner_rows:].reshape(-1, shared_inner.shape[-1])

    inner_halves = (expert_inner[0], swap_shard(expert_inner[0]))
    outer_halves = (expert_outer[0], swap_shard(expert_outer[0]))

    tokens_float = tokens_in.astype(jnp.float32)
    normed_one = norm_rows(tokens_float, gain_one_float).astype(jnp.bfloat16)
    query_raw = matmul(normed_one, query_full).reshape(tok_rows, H, DN + DR)
    queries = jnp.concatenate(
        [
            query_raw[..., :DN],
            rotate(query_raw[..., DN:], cosine_table[:, None, :], sine_table[:, None, :]),
        ],
        axis=-1,
    ).astype(jnp.bfloat16)
    down_out = matmul(normed_one, down_full)
    latent_raw = down_out[:, :KVR]
    latents = norm_rows(latent_raw, gain_latent_float).astype(jnp.bfloat16)
    key_rotary = rotate(down_out[:, KVR:], cosine_table, sine_table).astype(jnp.bfloat16)
    expanded = matmul(latents, up_full).astype(jnp.bfloat16).reshape(tok_rows, H, DN + DV)
    kv_local = jnp.concatenate([expanded.reshape(tok_rows, -1), key_rotary], axis=1)
    kv_remote = passed_along(kv_local, "shard", 1)
    remote_expanded = kv_remote[:, : H * (DN + DV)].reshape(tok_rows, H, DN + DV)
    remote_rotary = kv_remote[:, H * (DN + DV) :]
    key_rows = jnp.concatenate([remote_expanded, expanded], axis=0)
    rotary_rows = jnp.concatenate([remote_rotary, key_rotary], axis=0)
    scores = masked_scores(queries, key_rows, rotary_rows, visible)
    score_max = jnp.max(scores, axis=-1, keepdims=True)
    log_total = score_max + jnp.log(jnp.sum(jnp.exp(scores - score_max), axis=-1, keepdims=True))
    weights_float = jnp.exp(scores - log_total)
    weights_low = weights_float.astype(jnp.bfloat16)
    mixed_heads = (
        jnp.einsum(
            "hqk,khd->qhd", weights_low, key_rows[..., DN:], preferred_element_type=jnp.float32
        )
        .astype(jnp.bfloat16)
        .reshape(tok_rows, H * DV)
    )
    attention_out = jnp.einsum(
        "tc,dc->td", mixed_heads, output_t_full, preferred_element_type=jnp.float32
    )
    residual = tokens_float + attention_out
    normed_two = norm_rows(residual, gain_two_float).astype(jnp.bfloat16)
    logits = matmul(normed_two, router_full)
    route_probs = jax.nn.softmax(logits, axis=-1)
    gate_values = jnp.take_along_axis(route_probs, expert_ids, axis=1)
    flat_experts = expert_ids.reshape(-1)
    expert_match = (
        flat_experts[:, None] == jnp.arange(experts_all, dtype=jnp.int32)[None, :]
    ).astype(jnp.int32)
    slot_rank = jnp.sum((jnp.cumsum(expert_match, axis=0) - expert_match) * expert_match, axis=1)
    pair_count = tok_rows * TOPK
    slot_of = flat_experts * slot_cap + slot_rank
    slot_pair = (
        jnp.full((experts_all * slot_cap,), pair_count, jnp.int32)
        .at[slot_of]
        .set(jnp.arange(pair_count, dtype=jnp.int32))
    )
    slot_token = slot_pair // TOPK
    delta_out = cotangent.astype(jnp.float32)
    padded_rows = jnp.concatenate([normed_two, jnp.zeros((1, D), jnp.bfloat16)], axis=0)
    send_rows = jnp.take(padded_rows, slot_token, axis=0)
    padded_gates = jnp.concatenate([gate_values.reshape(-1), jnp.zeros((1,), jnp.float32)])
    slot_gate = jnp.take(padded_gates, slot_pair, axis=0)
    padded_delta = jnp.concatenate([delta_out, jnp.zeros((1, D), jnp.float32)], axis=0)
    send_delta = (jnp.take(padded_delta, slot_token, axis=0) * slot_gate[:, None]).astype(
        jnp.bfloat16
    )
    outgoing = jnp.stack(
        [send_rows.reshape(experts_all, slot_cap, D), send_delta.reshape(experts_all, slot_cap, D)],
        axis=1,
    )
    incoming = lax.all_to_all(outgoing, "expert", split_axis=0, concat_axis=0, tiled=True)

    shared_gate = matmul(normed_two, shared_in_full[0])
    shared_up = matmul(normed_two, shared_in_full[1])
    shared_hidden = gated_pair(shared_gate, shared_up).astype(jnp.bfloat16)
    shared_result = jnp.einsum(
        "tf,df->td", shared_hidden, shared_out_t_full, preferred_element_type=jnp.float32
    )
    delta_shared_outer_t = jnp.einsum(
        "td,tf->df", cotangent, shared_hidden, preferred_element_type=jnp.float32
    )
    delta_shared_hidden = jnp.einsum(
        "td,df->tf", cotangent, shared_out_t_full, preferred_element_type=jnp.float32
    )
    _, shared_back = jax.vjp(gated_pair, shared_gate, shared_up)
    delta_gate, delta_up = [
        part.astype(jnp.bfloat16) for part in shared_back(delta_shared_hidden)
    ]
    delta_shared_inner = jnp.stack(
        [
            jnp.einsum("td,tf->df", normed_two, part, preferred_element_type=jnp.float32)
            for part in (delta_gate, delta_up)
        ]
    )
    delta_normed = matmul(delta_gate, shared_in_full[0].T) + matmul(
        delta_up, shared_in_full[1].T
    )
    inner_grad_blocks = jnp.transpose(
        delta_shared_inner.reshape(
            (shared_inner.shape[0], experts_all, shard_count) + shared_inner.shape[1:]
        ),
        (1, 2, 0, 3, 4),
    ).reshape((experts_all, shard_count, -1, shared_inner.shape[-1]))
    outer_grad_blocks = delta_shared_outer_t.reshape(
        (experts_all, shard_count, -1, delta_shared_outer_t.shape[-1])
    )
    ffn_total = jnp.concatenate(
        [pair_total(inner_grad_blocks), pair_total(outer_grad_blocks)], axis=1
    )
    incoming, ffn_total = lax.optimization_barrier((incoming, ffn_total))
    arrived = incoming[:, 0].reshape(-1, D)
    delta_arrived = incoming[:, 1].reshape(-1, D)

    expert_pre = [
        jnp.einsum("rd,gdf->rgf", arrived, weight, preferred_element_type=jnp.float32)
        for weight in inner_halves
    ]
    expert_hidden = [gated(pre).astype(jnp.bfloat16) for pre in expert_pre]
    expert_result = sum(
        matmul(hidden, weight) for hidden, weight in zip(expert_hidden, outer_halves)
    ).astype(jnp.bfloat16)
    delta_outer_halves = [
        jnp.einsum("rf,rd->fd", hidden, delta_arrived, preferred_element_type=jnp.float32)
        for hidden in expert_hidden
    ]
    delta_pre_halves = []
    for pre, weight in zip(expert_pre, outer_halves):
        delta_hidden = jnp.einsum(
            "rd,fd->rf", delta_arrived, weight, preferred_element_type=jnp.float32
        )
        _, expert_back = jax.vjp(gated, pre)
        delta_pre_halves.append(expert_back(delta_hidden)[0].astype(jnp.bfloat16))
    delta_inner_halves = [
        jnp.einsum("rd,rgf->gdf", arrived, delta_pre, preferred_element_type=jnp.float32)
        for delta_pre in delta_pre_halves
    ]
    delta_rows = sum(
        jnp.einsum("rgf,gdf->rd", delta_pre, weight, preferred_element_type=jnp.float32)
        for delta_pre, weight in zip(delta_pre_halves, inner_halves)
    ).astype(jnp.bfloat16)
    going_back = jnp.stack(
        [
            expert_result.reshape(experts_all, slot_cap, D),
            delta_rows.reshape(experts_all, slot_cap, D),
        ],
        axis=1,
    )
    coming_back = lax.all_to_all(going_back, "expert", split_axis=0, concat_axis=0, tiled=True)
    returned = coming_back[:, 0].reshape(-1, D)
    delta_returned = coming_back[:, 1].reshape(-1, D)
    inner_from_partner = swap_shard(delta_inner_halves[1].astype(jnp.bfloat16))
    outer_from_partner = swap_shard(delta_outer_halves[1].astype(jnp.bfloat16))
    delta_expert_inner = delta_inner_halves[0] + inner_from_partner.astype(jnp.float32)
    delta_expert_outer = delta_outer_halves[0] + outer_from_partner.astype(jnp.float32)

    picked = jnp.take(returned, slot_of, axis=0).reshape(tok_rows, TOPK, D).astype(jnp.float32)
    routed = jnp.sum(gate_values[..., None] * picked, axis=1)
    feedforward = routed + shared_result
    layer_output = (residual + feedforward).astype(jnp.bfloat16)
    square_sums = jnp.stack(
        [
            jnp.sum(residual * residual),
            jnp.sum(attention_out * attention_out),
            jnp.sum(feedforward * feedforward),
        ]
    )

    delta_gates = jnp.sum(delta_out[:, None, :] * picked, axis=-1)
    delta_normed = delta_normed + jnp.sum(
        jnp.take(delta_returned, slot_of, axis=0).reshape(tok_rows, TOPK, D).astype(jnp.float32),
        axis=1,
    )
    match_float = expert_match.reshape(tok_rows, TOPK, experts_all).astype(jnp.float32)
    delta_probs = jnp.einsum("tk,tke->te", delta_gates, match_float)
    delta_logits = (
        route_probs * (delta_probs - jnp.sum(route_probs * delta_probs, axis=-1, keepdims=True))
    ).astype(jnp.bfloat16)
    delta_router = jnp.einsum(
        "td,te->de", normed_two, delta_logits, preferred_element_type=jnp.float32
    )
    delta_normed = delta_normed + jnp.einsum(
        "te,de->td", delta_logits, router_full, preferred_element_type=jnp.float32
    )
    _, second_back = jax.vjp(norm_rows, residual, gain_two_float)
    delta_residual_norm, delta_gain_two = second_back(delta_normed)
    delta_residual = delta_out + delta_residual_norm
    ffn_local = reduce_over_expert(ffn_total)
    delta_shared_inner_local = ffn_local[:inner_rows].reshape(shared_inner.shape)
    delta_shared_outer_local = ffn_local[inner_rows:].T

    delta_attention = delta_residual.astype(jnp.bfloat16)
    delta_output_t = jnp.einsum(
        "td,tc->dc", delta_attention, mixed_heads, preferred_element_type=jnp.float32
    )
    delta_output_local = scatter_rows(delta_output_t, experts_all).T
    delta_mixed = jnp.einsum(
        "td,dc->tc", delta_attention, output_t_full, preferred_element_type=jnp.float32
    )
    delta_mixed = delta_mixed.astype(jnp.bfloat16).reshape(tok_rows, H, DV)
    delta_weights = jnp.einsum(
        "qhd,khd->hqk", delta_mixed, key_rows[..., DN:], preferred_element_type=jnp.float32
    )
    delta_scores = (
        weights_float
        * (delta_weights - jnp.sum(weights_float * delta_weights, axis=-1, keepdims=True))
    ).astype(jnp.bfloat16)
    delta_values = jnp.einsum(
        "hqk,qhd->khd", weights_low, delta_mixed, preferred_element_type=jnp.float32
    )
    delta_query_plain = (
        jnp.einsum(
            "hqk,khd->qhd", delta_scores, key_rows[..., :DN], preferred_element_type=jnp.float32
        )
        * factor
    )
    delta_query_rotary = (
        jnp.einsum("hqk,kr->qhr", delta_scores, rotary_rows, preferred_element_type=jnp.float32)
        * factor
    )
    delta_key_plain = (
        jnp.einsum(
            "hqk,qhd->khd", delta_scores, queries[..., :DN], preferred_element_type=jnp.float32
        )
        * factor
    )
    delta_key_rotary = (
        jnp.einsum(
            "hqk,qhr->kr", delta_scores, queries[..., DN:], preferred_element_type=jnp.float32
        )
        * factor
    )
    delta_key_rows = jnp.concatenate([delta_key_plain, delta_values], axis=-1)
    back_local = jnp.concatenate(
        [delta_key_rows[:tok_rows].reshape(tok_rows, -1), delta_key_rotary[:tok_rows]], axis=1
    ).astype(jnp.bfloat16)
    back_remote = passed_along(back_local, "shard", -1).astype(jnp.float32)
    back_rows = back_remote[:, : H * (DN + DV)].reshape(tok_rows, H, DN + DV)
    back_rotary = back_remote[:, H * (DN + DV) :]
    delta_expanded = (
        (delta_key_rows[tok_rows:] + back_rows)
        .astype(jnp.bfloat16)
        .reshape(tok_rows, H * (DN + DV))
    )
    delta_rotary_total = delta_key_rotary[tok_rows:] + back_rotary
    delta_latent_up = jnp.einsum(
        "tl,tc->lc", latents, delta_expanded, preferred_element_type=jnp.float32
    )
    delta_latent_up_local = scatter_rows(delta_latent_up, experts_all)
    delta_latents = jnp.einsum(
        "tc,lc->tl", delta_expanded, up_full, preferred_element_type=jnp.float32
    )
    _, latent_back = jax.vjp(norm_rows, latent_raw, gain_latent_float)
    delta_latent_raw, delta_gain_latent = latent_back(delta_latents)
    delta_down_out = jnp.concatenate(
        [delta_latent_raw, rotate(delta_rotary_total, cosine_table, -sine_table)], axis=-1
    ).astype(jnp.bfloat16)
    delta_latent_down = jnp.einsum(
        "td,tc->dc", normed_one, delta_down_out, preferred_element_type=jnp.float32
    )
    delta_query_raw = (
        jnp.concatenate(
            [
                delta_query_plain,
                rotate(delta_query_rotary, cosine_table[:, None, :], -sine_table[:, None, :]),
            ],
            axis=-1,
        )
        .astype(jnp.bfloat16)
        .reshape(tok_rows, H * (DN + DR))
    )
    delta_query_weight = jnp.einsum(
        "td,tc->dc", normed_one, delta_query_raw, preferred_element_type=jnp.float32
    )
    delta_query_local = scatter_rows(delta_query_weight, experts_all)
    delta_normed_one = jnp.einsum(
        "tc,dc->td", delta_query_raw, query_full, preferred_element_type=jnp.float32
    ) + jnp.einsum("tc,dc->td", delta_down_out, down_full, preferred_element_type=jnp.float32)
    _, first_back = jax.vjp(norm_rows, tokens_float, gain_one_float)
    delta_tokens_norm, delta_gain_one = first_back(delta_normed_one)
    input_gradient = (delta_residual + delta_tokens_norm).astype(jnp.bfloat16)

    small_parts = [
        delta_gain_one.reshape(devices, -1),
        delta_gain_latent.reshape(devices, -1),
        delta_gain_two.reshape(devices, -1),
        delta_router.reshape(devices, -1),
        jnp.broadcast_to(square_sums[None], (devices, 3)),
    ]
    small_packed = jnp.concatenate(small_parts, axis=1)
    grad_rows = down_rows + -(-small_packed.shape[1] // width)
    grad_rows = grad_rows + (-grad_rows) % 8
    small_packed = jnp.concatenate(
        [
            small_packed,
            jnp.zeros(
                (devices, (grad_rows - down_rows) * width - small_packed.shape[1]), jnp.float32
            ),
        ],
        axis=1,
    ).reshape(devices, grad_rows - down_rows, width)
    down_blocks = jnp.concatenate(
        [delta_latent_down.reshape(devices, down_rows, width), small_packed], axis=1
    ).reshape(experts_all, shard_count, grad_rows, width)
    down_local = reduce_over_expert(pair_total(down_blocks))
    delta_latent_down_local = down_local[:down_rows]
    small_sum = down_local[down_rows:].reshape(-1)
    small_cuts = [0]
    for part in small_parts:
        small_cuts.append(small_cuts[-1] + part.shape[1])
    small_pieces = [small_sum[small_cuts[i] : small_cuts[i + 1]] for i in range(len(small_parts))]
    statistics = jnp.sqrt(small_pieces[4] / (tok_rows * D * devices))
    return (
        layer_output,
        input_gradient,
        small_pieces[0],
        delta_query_local,
        delta_latent_down_local,
        small_pieces[1],
        delta_latent_up_local,
        delta_output_local,
        small_pieces[2],
        small_pieces[3].reshape(router_weight.shape),
        delta_shared_inner_local,
        delta_shared_outer_local,
        delta_expert_inner[None],
        delta_expert_outer[None],
        statistics,
    )


def solution(mesh):
    return jax.shard_map(
        shards,
        mesh=mesh,
        in_specs=(
            P(ALL, None),
            P(ALL, None),
            P(ALL, None),
            P(ALL),
            P(ALL, None),
            P(ALL, None),
            P(ALL),
            P(ALL, None),
            P(None, ALL),
            P(ALL),
            P(ALL, None),
            P(None, ALL, None),
            P(None, ALL),
            P("expert", None, None, "shard"),
            P("expert", "shard", None),
        ),
        out_specs=(
            P(ALL, None),
            P(ALL, None),
            P(ALL),
            P(ALL, None),
            P(ALL, None),
            P(ALL),
            P(ALL, None),
            P(None, ALL),
            P(ALL),
            P(ALL, None),
            P(None, ALL, None),
            P(None, ALL),
            P("expert", None, None, "shard"),
            P("expert", "shard", None),
            P(),
        ),
        check_vma=False,
    )
```

```python
import jax
import jax.numpy as jnp
from jax import lax
from jax.sharding import PartitionSpec as P


D = 2048
H = 16
DN = 128
DR = 64
DV = 128
KVR = 512
TOPK = 6
CL = 64

ALL = ("expert", "shard")
EPSILON = 1e-06
THETA = 10000.0


def passed_along(value, axis, steps):
    count = lax.axis_size(axis)
    first, last = (max(0, -steps), min(count, count - steps))
    return lax.ppermute(value, axis, [(source, source + steps) for source in range(first, last)])


def matmul(left_side, right_side):
    return jnp.dot(left_side, right_side, preferred_element_type=jnp.float32)


def norm_rows(values, gain_vector):
    return (
        values
        * lax.rsqrt(jnp.mean(values * values, axis=-1, keepdims=True) + EPSILON)
        * gain_vector
    )


def rotate(values, cosine_table, sine_table):
    middle = values.shape[-1] // 2
    first_half = values[..., :middle]
    second_half = values[..., middle:]
    return jnp.concatenate(
        [
            first_half * cosine_table - second_half * sine_table,
            second_half * cosine_table + first_half * sine_table,
        ],
        axis=-1,
    )


def angles(positions):
    inverse = THETA ** (-jnp.arange(DR // 2, dtype=jnp.float32) * 2.0 / DR)
    phases = positions.astype(jnp.float32)[:, None] * inverse[None, :]
    return (jnp.cos(phases), jnp.sin(phases))


def gated(inner_out):
    return jax.nn.silu(inner_out[..., 0, :]) * inner_out[..., 1, :]


def masked_scores(queries, key_rows, rotary_rows, visible):
    factor = (DN + DR) ** (-0.5)
    plain_part = jnp.einsum(
        "qhd,khd->hqk", queries[..., :DN], key_rows[..., :DN], preferred_element_type=jnp.float32
    )
    rotary_part = jnp.einsum(
        "qhr,kr->hqk", queries[..., DN:], rotary_rows, preferred_element_type=jnp.float32
    )
    return jnp.where(visible[None], (plain_part + rotary_part) * factor, -1e30)


def swap_shard(value):
    return lax.ppermute(value, "shard", [(0, 1), (1, 0)])


def pair_total(blocks):
    side = lax.axis_index("shard")
    mine = lax.dynamic_index_in_dim(blocks, side, axis=1, keepdims=False)
    theirs = lax.dynamic_index_in_dim(blocks, 1 - side, axis=1, keepdims=False)
    arrived = swap_shard(theirs.astype(jnp.bfloat16))
    return (mine + arrived.astype(jnp.float32)).astype(jnp.bfloat16)


def reduce_over_expert(total):
    rows = total.reshape((-1,) + total.shape[2:])
    summed = lax.psum_scatter(rows, "expert", scatter_dimension=0, tiled=True)
    return summed.astype(jnp.float32)


def scatter_rows(full, experts):
    blocks = full.reshape((experts, 2, -1) + full.shape[1:])
    return reduce_over_expert(pair_total(blocks))


def gated_pair(gate_part, up_part):
    return jax.nn.silu(gate_part) * up_part


def shards(
    tokens_in,
    cotangent,
    expert_ids,
    attention_gain,
    query_weight,
    latent_down,
    latent_gain,
    latent_up,
    output_weight,
    feedforward_gain,
    router_weight,
    shared_inner,
    shared_outer,
    expert_inner,
    expert_outer,
):
    tok_rows = tokens_in.shape[0]
    experts_all = lax.axis_size("expert")
    shard_count = lax.axis_size("shard")
    devices = experts_all * shard_count
    slot_cap = tok_rows * TOPK * 4 // (3 * experts_all)
    factor = (DN + DR) ** (-0.5)
    side_index = lax.axis_index("shard")
    ordinal = jnp.arange(tok_rows, dtype=jnp.int32)
    positions = jnp.where(side_index == 0, ordinal, tok_rows + ordinal % CL)
    cosine_table, sine_table = angles(positions)
    query_place = ordinal[:, None]
    key_place = ordinal[None, :]
    causal = key_place <= query_place
    same_block = query_place // CL == key_place // CL
    local_mask = jnp.where(side_index == 0, causal, causal & same_block)
    remote_mask = jnp.broadcast_to(side_index == 1, (tok_rows, tok_rows))
    visible = jnp.concatenate([remote_mask, local_mask], axis=1)

    small_sizes = [
        attention_gain.shape[0],
        latent_gain.shape[0],
        feedforward_gain.shape[0],
        router_weight.size,
    ]
    small_local = jnp.concatenate(
        [attention_gain, latent_gain, feedforward_gain, router_weight.reshape(-1)]
    )
    width = latent_down.shape[1]
    small_rows = -(-small_local.shape[0] // width)
    small_local = jnp.concatenate(
        [small_local, jnp.zeros((small_rows * width - small_local.shape[0],), jnp.bfloat16)]
    ).reshape(small_rows, width)
    down_rows = latent_down.shape[0]
    down_all = lax.all_gather(
        jnp.concatenate([latent_down, small_local], axis=0), ALL, axis=0, tiled=False
    )
    down_full = down_all[:, :down_rows].reshape(-1, width)
    small_all = down_all[:, down_rows:].reshape(devices, -1)
    cuts = [0]
    for size in small_sizes:
        cuts.append(cuts[-1] + size)
    gain_one_float = small_all[:, cuts[0] : cuts[1]].reshape(-1).astype(jnp.float32)
    gain_latent_float = small_all[:, cuts[1] : cuts[2]].reshape(-1).astype(jnp.float32)
    gain_two_float = small_all[:, cuts[2] : cuts[3]].reshape(-1).astype(jnp.float32)
    router_full = small_all[:, cuts[3] : cuts[4]].reshape(-1, router_weight.shape[1])

    query_width = query_weight.shape[1]
    query_output_full = lax.all_gather(
        jnp.concatenate([query_weight, output_weight.T], axis=1), ALL, axis=0, tiled=True
    )
    query_full = query_output_full[:, :query_width]
    output_t_full = query_output_full[:, query_width:]
    up_full = lax.all_gather(latent_up, ALL, axis=0, tiled=True)
    inner_rows = shared_inner.shape[0] * shared_inner.shape[1]
    ffn_all = lax.all_gather(
        jnp.concatenate(
            [shared_inner.reshape(inner_rows, shared_inner.shape[-1]), shared_outer.T], axis=0
        ),
        ALL,
        axis=0,
        tiled=False,
    )
    shared_in_full = [
        ffn_all[:, g * shared_inner.shape[1] : (g + 1) * shared_inner.shape[1]].reshape(
            -1, shared_inner.shape[-1]
        )
        for g in range(shared_inner.shape[0])
    ]
    shared_out_t_full = ffn_all[:, inner_rows:].reshape(-1, shared_inner.shape[-1])

    inner_halves = (expert_inner[0], swap_shard(expert_inner[0]))
    outer_halves = (expert_outer[0], swap_shard(expert_outer[0]))

    tokens_float = tokens_in.astype(jnp.float32)
    normed_one = norm_rows(tokens_float, gain_one_float).astype(jnp.bfloat16)
    query_raw = matmul(normed_one, query_full).reshape(tok_rows, H, DN + DR)
    queries = jnp.concatenate(
        [
            query_raw[..., :DN],
            rotate(query_raw[..., DN:], cosine_table[:, None, :], sine_table[:, None, :]),
        ],
        axis=-1,
    ).astype(jnp.bfloat16)
    down_out = matmul(normed_one, down_full)
    latent_raw = down_out[:, :KVR]
    latents = norm_rows(latent_raw, gain_latent_float).astype(jnp.bfloat16)
    key_rotary = rotate(down_out[:, KVR:], cosine_table, sine_table).astype(jnp.bfloat16)
    expanded = matmul(latents, up_full).astype(jnp.bfloat16).reshape(tok_rows, H, DN + DV)
    kv_local = jnp.concatenate([expanded.reshape(tok_rows, -1), key_rotary], axis=1)
    kv_remote = passed_along(kv_local, "shard", 1)
    remote_expanded = kv_remote[:, : H * (DN + DV)].reshape(tok_rows, H, DN + DV)
    remote_rotary = kv_remote[:, H * (DN + DV) :]
    key_rows = jnp.concatenate([remote_expanded, expanded], axis=0)
    rotary_rows = jnp.concatenate([remote_rotary, key_rotary], axis=0)
    scores = masked_scores(queries, key_rows, rotary_rows, visible)
    score_max = jnp.max(scores, axis=-1, keepdims=True)
    log_total = score_max + jnp.log(jnp.sum(jnp.exp(scores - score_max), axis=-1, keepdims=True))
    weights_float = jnp.exp(scores - log_total)
    weights_low = weights_float.astype(jnp.bfloat16)
    mixed_heads = (
        jnp.einsum(
            "hqk,khd->qhd", weights_low, key_rows[..., DN:], preferred_element_type=jnp.float32
        )
        .astype(jnp.bfloat16)
        .reshape(tok_rows, H * DV)
    )
    attention_out = jnp.einsum(
        "tc,dc->td", mixed_heads, output_t_full, preferred_element_type=jnp.float32
    )
    residual = tokens_float + attention_out
    normed_two = norm_rows(residual, gain_two_float).astype(jnp.bfloat16)
    logits = matmul(normed_two, router_full)
    route_probs = jax.nn.softmax(logits, axis=-1)
    gate_values = jnp.take_along_axis(route_probs, expert_ids, axis=1)
    flat_experts = expert_ids.reshape(-1)
    expert_match = (
        flat_experts[:, None] == jnp.arange(experts_all, dtype=jnp.int32)[None, :]
    ).astype(jnp.int32)
    slot_rank = jnp.sum((jnp.cumsum(expert_match, axis=0) - expert_match) * expert_match, axis=1)
    pair_count = tok_rows * TOPK
    slot_of = flat_experts * slot_cap + slot_rank
    slot_pair = (
        jnp.full((experts_all * slot_cap,), pair_count, jnp.int32)
        .at[slot_of]
        .set(jnp.arange(pair_count, dtype=jnp.int32))
    )
    slot_token = slot_pair // TOPK
    delta_out = cotangent.astype(jnp.float32)
    padded_rows = jnp.concatenate([normed_two, jnp.zeros((1, D), jnp.bfloat16)], axis=0)
    send_rows = jnp.take(padded_rows, slot_token, axis=0)
    padded_gates = jnp.concatenate([gate_values.reshape(-1), jnp.zeros((1,), jnp.float32)])
    slot_gate = jnp.take(padded_gates, slot_pair, axis=0)
    padded_delta = jnp.concatenate([delta_out, jnp.zeros((1, D), jnp.float32)], axis=0)
    send_delta = (jnp.take(padded_delta, slot_token, axis=0) * slot_gate[:, None]).astype(
        jnp.bfloat16
    )
    outgoing = jnp.stack(
        [send_rows.reshape(experts_all, slot_cap, D), send_delta.reshape(experts_all, slot_cap, D)],
        axis=1,
    )
    incoming = lax.all_to_all(outgoing, "expert", split_axis=0, concat_axis=0, tiled=True)

    shared_gate = matmul(normed_two, shared_in_full[0])
    shared_up = matmul(normed_two, shared_in_full[1])
    shared_hidden = gated_pair(shared_gate, shared_up).astype(jnp.bfloat16)
    shared_result = jnp.einsum(
        "tf,df->td", shared_hidden, shared_out_t_full, preferred_element_type=jnp.float32
    )
    delta_shared_outer_t = jnp.einsum(
        "td,tf->df", cotangent, shared_hidden, preferred_element_type=jnp.bfloat16
    )
    delta_shared_hidden = jnp.einsum(
        "td,df->tf", cotangent, shared_out_t_full, preferred_element_type=jnp.float32
    )
    _, shared_back = jax.vjp(gated_pair, shared_gate, shared_up)
    delta_gate, delta_up = [
        part.astype(jnp.bfloat16) for part in shared_back(delta_shared_hidden)
    ]
    delta_shared_inner = jnp.stack(
        [
            jnp.einsum("td,tf->df", normed_two, part, preferred_element_type=jnp.bfloat16)
            for part in (delta_gate, delta_up)
        ]
    )
    delta_normed = matmul(delta_gate, shared_in_full[0].T) + matmul(
        delta_up, shared_in_full[1].T
    )
    inner_grad_blocks = jnp.transpose(
        delta_shared_inner.reshape(
            (shared_inner.shape[0], experts_all, shard_count) + shared_inner.shape[1:]
        ),
        (1, 2, 0, 3, 4),
    ).reshape((experts_all, shard_count, -1, shared_inner.shape[-1]))
    outer_grad_blocks = delta_shared_outer_t.reshape(
        (experts_all, shard_count, -1, delta_shared_outer_t.shape[-1])
    )
    ffn_total = jnp.concatenate(
        [pair_total(inner_grad_blocks), pair_total(outer_grad_blocks)], axis=1
    )
    incoming, ffn_total = lax.optimization_barrier((incoming, ffn_total))
    arrived = incoming[:, 0].reshape(-1, D)
    delta_arrived = incoming[:, 1].reshape(-1, D)

    expert_pre = [
        jnp.einsum("rd,gdf->rgf", arrived, weight, preferred_element_type=jnp.float32)
        for weight in inner_halves
    ]
    expert_hidden = [gated(pre).astype(jnp.bfloat16) for pre in expert_pre]
    expert_result = sum(
        matmul(hidden, weight) for hidden, weight in zip(expert_hidden, outer_halves)
    ).astype(jnp.bfloat16)
    delta_outer_halves = [
        jnp.einsum("rf,rd->fd", hidden, delta_arrived, preferred_element_type=jnp.float32)
        for hidden in expert_hidden
    ]
    delta_pre_halves = []
    for pre, weight in zip(expert_pre, outer_halves):
        delta_hidden = jnp.einsum(
            "rd,fd->rf", delta_arrived, weight, preferred_element_type=jnp.float32
        )
        _, expert_back = jax.vjp(gated, pre)
        delta_pre_halves.append(expert_back(delta_hidden)[0].astype(jnp.bfloat16))
    delta_inner_halves = [
        jnp.einsum("rd,rgf->gdf", arrived, delta_pre, preferred_element_type=jnp.float32)
        for delta_pre in delta_pre_halves
    ]
    delta_rows = sum(
        jnp.einsum("rgf,gdf->rd", delta_pre, weight, preferred_element_type=jnp.float32)
        for delta_pre, weight in zip(delta_pre_halves, inner_halves)
    ).astype(jnp.bfloat16)
    going_back = jnp.stack(
        [
            expert_result.reshape(experts_all, slot_cap, D),
            delta_rows.reshape(experts_all, slot_cap, D),
        ],
        axis=1,
    )
    coming_back = lax.all_to_all(going_back, "expert", split_axis=0, concat_axis=0, tiled=True)
    returned = coming_back[:, 0].reshape(-1, D)
    delta_returned = coming_back[:, 1].reshape(-1, D)
    inner_from_partner = swap_shard(delta_inner_halves[1].astype(jnp.bfloat16))
    outer_from_partner = swap_shard(delta_outer_halves[1].astype(jnp.bfloat16))
    delta_expert_inner = delta_inner_halves[0] + inner_from_partner.astype(jnp.float32)
    delta_expert_outer = delta_outer_halves[0] + outer_from_partner.astype(jnp.float32)

    picked = jnp.take(returned, slot_of, axis=0).reshape(tok_rows, TOPK, D).astype(jnp.float32)
    routed = jnp.sum(gate_values[..., None] * picked, axis=1)
    feedforward = routed + shared_result
    layer_output = (residual + feedforward).astype(jnp.bfloat16)
    square_sums = jnp.stack(
        [
            jnp.sum(residual * residual),
            jnp.sum(attention_out * attention_out),
            jnp.sum(feedforward * feedforward),
        ]
    )

    delta_gates = jnp.sum(delta_out[:, None, :] * picked, axis=-1)
    delta_normed = delta_normed + jnp.sum(
        jnp.take(delta_returned, slot_of, axis=0).reshape(tok_rows, TOPK, D).astype(jnp.float32),
        axis=1,
    )
    match_float = expert_match.reshape(tok_rows, TOPK, experts_all).astype(jnp.float32)
    delta_probs = jnp.einsum("tk,tke->te", delta_gates, match_float)
    delta_logits = (
        route_probs * (delta_probs - jnp.sum(route_probs * delta_probs, axis=-1, keepdims=True))
    ).astype(jnp.bfloat16)
    delta_router = jnp.einsum(
        "td,te->de", normed_two, delta_logits, preferred_element_type=jnp.float32
    )
    delta_normed = delta_normed + jnp.einsum(
        "te,de->td", delta_logits, router_full, preferred_element_type=jnp.float32
    )
    _, second_back = jax.vjp(norm_rows, residual, gain_two_float)
    delta_residual_norm, delta_gain_two = second_back(delta_normed)
    delta_residual = delta_out + delta_residual_norm
    ffn_local = reduce_over_expert(ffn_total)
    delta_shared_inner_local = ffn_local[:inner_rows].reshape(shared_inner.shape)
    delta_shared_outer_local = ffn_local[inner_rows:].T

    delta_attention = delta_residual.astype(jnp.bfloat16)
    delta_output_t = jnp.einsum(
        "td,tc->dc", delta_attention, mixed_heads, preferred_element_type=jnp.float32
    )
    delta_output_local = scatter_rows(delta_output_t, experts_all).T
    delta_mixed = jnp.einsum(
        "td,dc->tc", delta_attention, output_t_full, preferred_element_type=jnp.float32
    )
    delta_mixed = delta_mixed.astype(jnp.bfloat16).reshape(tok_rows, H, DV)
    delta_weights = jnp.einsum(
        "qhd,khd->hqk", delta_mixed, key_rows[..., DN:], preferred_element_type=jnp.float32
    )
    delta_scores = (
        weights_float
        * (delta_weights - jnp.sum(weights_float * delta_weights, axis=-1, keepdims=True))
    ).astype(jnp.bfloat16)
    delta_values = jnp.einsum(
        "hqk,qhd->khd", weights_low, delta_mixed, preferred_element_type=jnp.float32
    )
    delta_query_plain = (
        jnp.einsum(
            "hqk,khd->qhd", delta_scores, key_rows[..., :DN], preferred_element_type=jnp.float32
        )
        * factor
    )
    delta_query_rotary = (
        jnp.einsum("hqk,kr->qhr", delta_scores, rotary_rows, preferred_element_type=jnp.float32)
        * factor
    )
    delta_key_plain = (
        jnp.einsum(
            "hqk,qhd->khd", delta_scores, queries[..., :DN], preferred_element_type=jnp.float32
        )
        * factor
    )
    delta_key_rotary = (
        jnp.einsum(
            "hqk,qhr->kr", delta_scores, queries[..., DN:], preferred_element_type=jnp.float32
        )
        * factor
    )
    delta_key_rows = jnp.concatenate([delta_key_plain, delta_values], axis=-1)
    back_local = jnp.concatenate(
        [delta_key_rows[:tok_rows].reshape(tok_rows, -1), delta_key_rotary[:tok_rows]], axis=1
    ).astype(jnp.bfloat16)
    back_remote = passed_along(back_local, "shard", -1).astype(jnp.float32)
    back_rows = back_remote[:, : H * (DN + DV)].reshape(tok_rows, H, DN + DV)
    back_rotary = back_remote[:, H * (DN + DV) :]
    delta_expanded = (
        (delta_key_rows[tok_rows:] + back_rows)
        .astype(jnp.bfloat16)
        .reshape(tok_rows, H * (DN + DV))
    )
    delta_rotary_total = delta_key_rotary[tok_rows:] + back_rotary
    delta_latent_up = jnp.einsum(
        "tl,tc->lc", latents, delta_expanded, preferred_element_type=jnp.float32
    )
    delta_latent_up_local = scatter_rows(delta_latent_up, experts_all)
    delta_latents = jnp.einsum(
        "tc,lc->tl", delta_expanded, up_full, preferred_element_type=jnp.float32
    )
    _, latent_back = jax.vjp(norm_rows, latent_raw, gain_latent_float)
    delta_latent_raw, delta_gain_latent = latent_back(delta_latents)
    delta_down_out = jnp.concatenate(
        [delta_latent_raw, rotate(delta_rotary_total, cosine_table, -sine_table)], axis=-1
    ).astype(jnp.bfloat16)
    delta_latent_down = jnp.einsum(
        "td,tc->dc", normed_one, delta_down_out, preferred_element_type=jnp.float32
    )
    delta_query_raw = (
        jnp.concatenate(
            [
                delta_query_plain,
                rotate(delta_query_rotary, cosine_table[:, None, :], -sine_table[:, None, :]),
            ],
            axis=-1,
        )
        .astype(jnp.bfloat16)
        .reshape(tok_rows, H * (DN + DR))
    )
    delta_query_weight = jnp.einsum(
        "td,tc->dc", normed_one, delta_query_raw, preferred_element_type=jnp.float32
    )
    delta_normed_one = jnp.einsum(
        "tc,dc->td", delta_query_raw, query_full, preferred_element_type=jnp.float32
    ) + jnp.einsum("tc,dc->td", delta_down_out, down_full, preferred_element_type=jnp.float32)
    _, first_back = jax.vjp(norm_rows, tokens_float, gain_one_float)
    delta_tokens_norm, delta_gain_one = first_back(delta_normed_one)
    input_gradient = (delta_residual + delta_tokens_norm).astype(jnp.bfloat16)

    small_parts = [
        delta_gain_one.reshape(devices, -1),
        delta_gain_latent.reshape(devices, -1),
        delta_gain_two.reshape(devices, -1),
        delta_router.reshape(devices, -1),
        jnp.broadcast_to(square_sums[None], (devices, 3)),
    ]
    small_packed = jnp.concatenate(small_parts, axis=1)
    query_rows = query_weight.shape[0]
    down_size = latent_down.size
    extra = jnp.concatenate([delta_latent_down.reshape(devices, -1), small_packed], axis=1)
    total_rows = query_rows + -(-extra.shape[1] // query_width)
    total_rows = total_rows + (-total_rows) % 8
    extra = jnp.concatenate(
        [
            extra,
            jnp.zeros(
                (devices, (total_rows - query_rows) * query_width - extra.shape[1]), jnp.float32
            ),
        ],
        axis=1,
    ).reshape(devices, total_rows - query_rows, query_width)
    query_blocks = jnp.concatenate(
        [delta_query_weight.reshape(devices, query_rows, query_width), extra], axis=1
    ).reshape(experts_all, shard_count, total_rows, query_width)
    query_out = reduce_over_expert(pair_total(query_blocks))
    delta_query_local = query_out[:query_rows]
    rest = query_out[query_rows:].reshape(-1)
    delta_latent_down_local = rest[:down_size].reshape(latent_down.shape)
    small_sum = rest[down_size:]
    small_cuts = [0]
    for part in small_parts:
        small_cuts.append(small_cuts[-1] + part.shape[1])
    small_pieces = [small_sum[small_cuts[i] : small_cuts[i + 1]] for i in range(len(small_parts))]
    statistics = jnp.sqrt(small_pieces[4] / (tok_rows * D * devices))
    return (
        layer_output,
        input_gradient,
        small_pieces[0],
        delta_query_local,
        delta_latent_down_local,
        small_pieces[1],
        delta_latent_up_local,
        delta_output_local,
        small_pieces[2],
        small_pieces[3].reshape(router_weight.shape),
        delta_shared_inner_local,
        delta_shared_outer_local,
        delta_expert_inner[None],
        delta_expert_outer[None],
        statistics,
    )


def solution(mesh):
    return jax.shard_map(
        shards,
        mesh=mesh,
        in_specs=(
            P(ALL, None),
            P(ALL, None),
            P(ALL, None),
            P(ALL),
            P(ALL, None),
            P(ALL, None),
            P(ALL),
            P(ALL, None),
            P(None, ALL),
            P(ALL),
            P(ALL, None),
            P(None, ALL, None),
            P(None, ALL),
            P("expert", None, None, "shard"),
            P("expert", "shard", None),
        ),
        out_specs=(
            P(ALL, None),
            P(ALL, None),
            P(ALL),
            P(ALL, None),
            P(ALL, None),
            P(ALL),
            P(ALL, None),
            P(None, ALL),
            P(ALL),
            P(ALL, None),
            P(None, ALL, None),
            P(None, ALL),
            P("expert", None, None, "shard"),
            P("expert", "shard", None),
            P(),
        ),
        check_vma=False,
    )
```

```python
import jax
import jax.numpy as jnp
from jax import lax
from jax.sharding import PartitionSpec as P


D = 2048
H = 16
DN = 128
DR = 64
DV = 128
KVR = 512
TOPK = 6
CL = 64

ALL = ("expert", "shard")
EPSILON = 1e-06
THETA = 10000.0


def passed_along(value, axis, steps):
    count = lax.axis_size(axis)
    first, last = (max(0, -steps), min(count, count - steps))
    return lax.ppermute(value, axis, [(source, source + steps) for source in range(first, last)])


def matmul(left_side, right_side):
    return jnp.dot(left_side, right_side, preferred_element_type=jnp.float32)


def norm_rows(values, gain_vector):
    return (
        values
        * lax.rsqrt(jnp.mean(values * values, axis=-1, keepdims=True) + EPSILON)
        * gain_vector
    )


def rotate(values, cosine_table, sine_table):
    middle = values.shape[-1] // 2
    first_half = values[..., :middle]
    second_half = values[..., middle:]
    return jnp.concatenate(
        [
            first_half * cosine_table - second_half * sine_table,
            second_half * cosine_table + first_half * sine_table,
        ],
        axis=-1,
    )


def angles(positions):
    inverse = THETA ** (-jnp.arange(DR // 2, dtype=jnp.float32) * 2.0 / DR)
    phases = positions.astype(jnp.float32)[:, None] * inverse[None, :]
    return (jnp.cos(phases), jnp.sin(phases))


def gated(inner_out):
    return jax.nn.silu(inner_out[..., 0, :]) * inner_out[..., 1, :]


def masked_scores(queries, key_rows, rotary_rows, visible):
    factor = (DN + DR) ** (-0.5)
    plain_part = jnp.einsum(
        "qhd,khd->hqk", queries[..., :DN], key_rows[..., :DN], preferred_element_type=jnp.float32
    )
    rotary_part = jnp.einsum(
        "qhr,kr->hqk", queries[..., DN:], rotary_rows, preferred_element_type=jnp.float32
    )
    return jnp.where(visible[None], (plain_part + rotary_part) * factor, -1e30)


def swap_shard(value):
    return lax.ppermute(value, "shard", [(0, 1), (1, 0)])


def pair_total(blocks):
    side = lax.axis_index("shard")
    mine = lax.dynamic_index_in_dim(blocks, side, axis=1, keepdims=False)
    theirs = lax.dynamic_index_in_dim(blocks, 1 - side, axis=1, keepdims=False)
    arrived = swap_shard(theirs.astype(jnp.bfloat16))
    return (mine + arrived.astype(jnp.float32)).astype(jnp.bfloat16)


def reduce_over_expert(total):
    rows = total.reshape((-1,) + total.shape[2:])
    summed = lax.psum_scatter(rows, "expert", scatter_dimension=0, tiled=True)
    return summed.astype(jnp.float32)


def scatter_rows(full, experts):
    blocks = full.reshape((experts, 2, -1) + full.shape[1:])
    return reduce_over_expert(pair_total(blocks))


def gated_pair(gate_part, up_part):
    return jax.nn.silu(gate_part) * up_part


def shards(
    tokens_in,
    cotangent,
    expert_ids,
    attention_gain,
    query_weight,
    latent_down,
    latent_gain,
    latent_up,
    output_weight,
    feedforward_gain,
    router_weight,
    shared_inner,
    shared_outer,
    expert_inner,
    expert_outer,
):
    tok_rows = tokens_in.shape[0]
    experts_all = lax.axis_size("expert")
    shard_count = lax.axis_size("shard")
    devices = experts_all * shard_count
    slot_cap = tok_rows * TOPK * 4 // (3 * experts_all)
    factor = (DN + DR) ** (-0.5)
    side_index = lax.axis_index("shard")
    ordinal = jnp.arange(tok_rows, dtype=jnp.int32)
    positions = jnp.where(side_index == 0, ordinal, tok_rows + ordinal % CL)
    cosine_table, sine_table = angles(positions)
    query_place = ordinal[:, None]
    key_place = ordinal[None, :]
    causal = key_place <= query_place
    same_block = query_place // CL == key_place // CL
    local_mask = jnp.where(side_index == 0, causal, causal & same_block)
    remote_mask = jnp.broadcast_to(side_index == 1, (tok_rows, tok_rows))
    visible = jnp.concatenate([remote_mask, local_mask], axis=1)

    small_sizes = [
        attention_gain.shape[0],
        latent_gain.shape[0],
        feedforward_gain.shape[0],
        router_weight.size,
    ]
    small_local = jnp.concatenate(
        [attention_gain, latent_gain, feedforward_gain, router_weight.reshape(-1)]
    )
    width = latent_down.shape[1]
    small_rows = -(-small_local.shape[0] // width)
    small_local = jnp.concatenate(
        [small_local, jnp.zeros((small_rows * width - small_local.shape[0],), jnp.bfloat16)]
    ).reshape(small_rows, width)
    down_rows = latent_down.shape[0]
    down_all = lax.all_gather(
        jnp.concatenate([latent_down, small_local], axis=0), ALL, axis=0, tiled=False
    )
    down_full = down_all[:, :down_rows].reshape(-1, width)
    small_all = down_all[:, down_rows:].reshape(devices, -1)
    cuts = [0]
    for size in small_sizes:
        cuts.append(cuts[-1] + size)
    gain_one_float = small_all[:, cuts[0] : cuts[1]].reshape(-1).astype(jnp.float32)
    gain_latent_float = small_all[:, cuts[1] : cuts[2]].reshape(-1).astype(jnp.float32)
    gain_two_float = small_all[:, cuts[2] : cuts[3]].reshape(-1).astype(jnp.float32)
    router_full = small_all[:, cuts[3] : cuts[4]].reshape(-1, router_weight.shape[1])

    query_width = query_weight.shape[1]
    query_output_full = lax.all_gather(
        jnp.concatenate([query_weight, output_weight.T], axis=1), ALL, axis=0, tiled=True
    )
    query_full = query_output_full[:, :query_width]
    output_t_full = query_output_full[:, query_width:]
    up_full = lax.all_gather(latent_up, ALL, axis=0, tiled=True)
    inner_rows = shared_inner.shape[0] * shared_inner.shape[1]
    ffn_all = lax.all_gather(
        jnp.concatenate(
            [shared_inner.reshape(inner_rows, shared_inner.shape[-1]), shared_outer.T], axis=0
        ),
        ALL,
        axis=0,
        tiled=False,
    )
    shared_in_full = [
        ffn_all[:, g * shared_inner.shape[1] : (g + 1) * shared_inner.shape[1]].reshape(
            -1, shared_inner.shape[-1]
        )
        for g in range(shared_inner.shape[0])
    ]
    shared_out_t_full = ffn_all[:, inner_rows:].reshape(-1, shared_inner.shape[-1])

    inner_halves = (expert_inner[0], swap_shard(expert_inner[0]))
    outer_halves = (expert_outer[0], swap_shard(expert_outer[0]))

    tokens_float = tokens_in.astype(jnp.float32)
    normed_one = norm_rows(tokens_float, gain_one_float).astype(jnp.bfloat16)
    query_raw = matmul(normed_one, query_full).reshape(tok_rows, H, DN + DR)
    queries = jnp.concatenate(
        [
            query_raw[..., :DN],
            rotate(query_raw[..., DN:], cosine_table[:, None, :], sine_table[:, None, :]),
        ],
        axis=-1,
    ).astype(jnp.bfloat16)
    down_out = matmul(normed_one, down_full)
    latent_raw = down_out[:, :KVR]
    latents = norm_rows(latent_raw, gain_latent_float).astype(jnp.bfloat16)
    key_rotary = rotate(down_out[:, KVR:], cosine_table, sine_table).astype(jnp.bfloat16)
    expanded = matmul(latents, up_full).astype(jnp.bfloat16).reshape(tok_rows, H, DN + DV)
    kv_local = jnp.concatenate([expanded.reshape(tok_rows, -1), key_rotary], axis=1)
    kv_remote = passed_along(kv_local, "shard", 1)
    remote_expanded = kv_remote[:, : H * (DN + DV)].reshape(tok_rows, H, DN + DV)
    remote_rotary = kv_remote[:, H * (DN + DV) :]
    key_rows = jnp.concatenate([remote_expanded, expanded], axis=0)
    rotary_rows = jnp.concatenate([remote_rotary, key_rotary], axis=0)
    scores = masked_scores(queries, key_rows, rotary_rows, visible)
    score_max = jnp.max(scores, axis=-1, keepdims=True)
    log_total = score_max + jnp.log(jnp.sum(jnp.exp(scores - score_max), axis=-1, keepdims=True))
    weights_float = jnp.exp(scores - log_total)
    weights_low = weights_float.astype(jnp.bfloat16)
    mixed_heads = (
        jnp.einsum(
            "hqk,khd->qhd", weights_low, key_rows[..., DN:], preferred_element_type=jnp.float32
        )
        .astype(jnp.bfloat16)
        .reshape(tok_rows, H * DV)
    )
    attention_out = jnp.einsum(
        "tc,dc->td", mixed_heads, output_t_full, preferred_element_type=jnp.float32
    )
    residual = tokens_float + attention_out
    normed_two = norm_rows(residual, gain_two_float).astype(jnp.bfloat16)
    logits = matmul(normed_two, router_full)
    route_probs = jax.nn.softmax(logits, axis=-1)
    gate_values = jnp.take_along_axis(route_probs, expert_ids, axis=1)
    flat_experts = expert_ids.reshape(-1)
    expert_match = (
        flat_experts[:, None] == jnp.arange(experts_all, dtype=jnp.int32)[None, :]
    ).astype(jnp.int32)
    slot_rank = jnp.sum((jnp.cumsum(expert_match, axis=0) - expert_match) * expert_match, axis=1)
    pair_count = tok_rows * TOPK
    slot_of = flat_experts * slot_cap + slot_rank
    slot_pair = (
        jnp.full((experts_all * slot_cap,), pair_count, jnp.int32)
        .at[slot_of]
        .set(jnp.arange(pair_count, dtype=jnp.int32))
    )
    slot_token = slot_pair // TOPK
    delta_out = cotangent.astype(jnp.float32)
    padded_rows = jnp.concatenate([normed_two, jnp.zeros((1, D), jnp.bfloat16)], axis=0)
    send_rows = jnp.take(padded_rows, slot_token, axis=0)
    padded_gates = jnp.concatenate([gate_values.reshape(-1), jnp.zeros((1,), jnp.float32)])
    slot_gate = jnp.take(padded_gates, slot_pair, axis=0)
    padded_delta = jnp.concatenate([delta_out, jnp.zeros((1, D), jnp.float32)], axis=0)
    send_delta = (jnp.take(padded_delta, slot_token, axis=0) * slot_gate[:, None]).astype(
        jnp.bfloat16
    )
    outgoing = jnp.stack(
        [send_rows.reshape(experts_all, slot_cap, D), send_delta.reshape(experts_all, slot_cap, D)],
        axis=1,
    )
    incoming = lax.all_to_all(outgoing, "expert", split_axis=0, concat_axis=0, tiled=True)

    shared_gate = matmul(normed_two, shared_in_full[0])
    shared_up = matmul(normed_two, shared_in_full[1])
    shared_hidden = gated_pair(shared_gate, shared_up).astype(jnp.bfloat16)
    shared_result = jnp.einsum(
        "tf,df->td", shared_hidden, shared_out_t_full, preferred_element_type=jnp.float32
    )
    delta_shared_outer_t = jnp.einsum(
        "td,tf->df", cotangent, shared_hidden, preferred_element_type=jnp.bfloat16
    )
    delta_shared_hidden = jnp.einsum(
        "td,df->tf", cotangent, shared_out_t_full, preferred_element_type=jnp.float32
    )
    _, shared_back = jax.vjp(gated_pair, shared_gate, shared_up)
    delta_gate, delta_up = [
        part.astype(jnp.bfloat16) for part in shared_back(delta_shared_hidden)
    ]
    delta_shared_inner = jnp.stack(
        [
            jnp.einsum("td,tf->df", normed_two, part, preferred_element_type=jnp.bfloat16)
            for part in (delta_gate, delta_up)
        ]
    )
    delta_normed = matmul(delta_gate, shared_in_full[0].T) + matmul(
        delta_up, shared_in_full[1].T
    )
    inner_grad_blocks = jnp.transpose(
        delta_shared_inner.reshape(
            (shared_inner.shape[0], experts_all, shard_count) + shared_inner.shape[1:]
        ),
        (1, 2, 0, 3, 4),
    ).reshape((experts_all, shard_count, -1, shared_inner.shape[-1]))
    outer_grad_blocks = delta_shared_outer_t.reshape(
        (experts_all, shard_count, -1, delta_shared_outer_t.shape[-1])
    )
    ffn_total = jnp.concatenate(
        [
            inner_grad_blocks.reshape((devices, -1) + inner_grad_blocks.shape[3:]),
            outer_grad_blocks.reshape((devices, -1) + outer_grad_blocks.shape[3:]),
        ],
        axis=1,
    ).astype(jnp.bfloat16)
    incoming, ffn_total = lax.optimization_barrier((incoming, ffn_total))
    arrived = incoming[:, 0].reshape(-1, D)
    delta_arrived = incoming[:, 1].reshape(-1, D)

    expert_pre = [
        jnp.einsum("rd,gdf->rgf", arrived, weight, preferred_element_type=jnp.float32)
        for weight in inner_halves
    ]
    expert_hidden = [gated(pre).astype(jnp.bfloat16) for pre in expert_pre]
    expert_result = sum(
        matmul(hidden, weight) for hidden, weight in zip(expert_hidden, outer_halves)
    ).astype(jnp.bfloat16)
    delta_outer_halves = [
        jnp.einsum("rf,rd->fd", hidden, delta_arrived, preferred_element_type=jnp.float32)
        for hidden in expert_hidden
    ]
    delta_pre_halves = []
    for pre, weight in zip(expert_pre, outer_halves):
        delta_hidden = jnp.einsum(
            "rd,fd->rf", delta_arrived, weight, preferred_element_type=jnp.float32
        )
        _, expert_back = jax.vjp(gated, pre)
        delta_pre_halves.append(expert_back(delta_hidden)[0].astype(jnp.bfloat16))
    delta_inner_halves = [
        jnp.einsum("rd,rgf->gdf", arrived, delta_pre, preferred_element_type=jnp.float32)
        for delta_pre in delta_pre_halves
    ]
    delta_rows = sum(
        jnp.einsum("rgf,gdf->rd", delta_pre, weight, preferred_element_type=jnp.float32)
        for delta_pre, weight in zip(delta_pre_halves, inner_halves)
    ).astype(jnp.bfloat16)
    going_back = jnp.stack(
        [
            expert_result.reshape(experts_all, slot_cap, D),
            delta_rows.reshape(experts_all, slot_cap, D),
        ],
        axis=1,
    )
    coming_back = lax.all_to_all(going_back, "expert", split_axis=0, concat_axis=0, tiled=True)
    returned = coming_back[:, 0].reshape(-1, D)
    delta_returned = coming_back[:, 1].reshape(-1, D)
    inner_from_partner = swap_shard(delta_inner_halves[1].astype(jnp.bfloat16))
    outer_from_partner = swap_shard(delta_outer_halves[1].astype(jnp.bfloat16))
    delta_expert_inner = delta_inner_halves[0] + inner_from_partner.astype(jnp.float32)
    delta_expert_outer = delta_outer_halves[0] + outer_from_partner.astype(jnp.float32)

    picked = jnp.take(returned, slot_of, axis=0).reshape(tok_rows, TOPK, D).astype(jnp.float32)
    routed = jnp.sum(gate_values[..., None] * picked, axis=1)
    feedforward = routed + shared_result
    layer_output = (residual + feedforward).astype(jnp.bfloat16)
    square_sums = jnp.stack(
        [
            jnp.sum(residual * residual),
            jnp.sum(attention_out * attention_out),
            jnp.sum(feedforward * feedforward),
        ]
    )

    delta_gates = jnp.sum(delta_out[:, None, :] * picked, axis=-1)
    delta_normed = delta_normed + jnp.sum(
        jnp.take(delta_returned, slot_of, axis=0).reshape(tok_rows, TOPK, D).astype(jnp.float32),
        axis=1,
    )
    match_float = expert_match.reshape(tok_rows, TOPK, experts_all).astype(jnp.float32)
    delta_probs = jnp.einsum("tk,tke->te", delta_gates, match_float)
    delta_logits = (
        route_probs * (delta_probs - jnp.sum(route_probs * delta_probs, axis=-1, keepdims=True))
    ).astype(jnp.bfloat16)
    delta_router = jnp.einsum(
        "td,te->de", normed_two, delta_logits, preferred_element_type=jnp.float32
    )
    delta_normed = delta_normed + jnp.einsum(
        "te,de->td", delta_logits, router_full, preferred_element_type=jnp.float32
    )
    _, second_back = jax.vjp(norm_rows, residual, gain_two_float)
    delta_residual_norm, delta_gain_two = second_back(delta_normed)
    delta_residual = delta_out + delta_residual_norm
    ffn_local = lax.psum_scatter(
        ffn_total.reshape((-1,) + ffn_total.shape[2:]), ALL, scatter_dimension=0, tiled=True
    )
    ffn_local = ffn_local.astype(jnp.float32)
    delta_shared_inner_local = ffn_local[:inner_rows].reshape(shared_inner.shape)
    delta_shared_outer_local = ffn_local[inner_rows:].T

    delta_attention = delta_residual.astype(jnp.bfloat16)
    delta_output_t = jnp.einsum(
        "td,tc->dc", delta_attention, mixed_heads, preferred_element_type=jnp.float32
    )
    delta_output_local = scatter_rows(delta_output_t, experts_all).T
    delta_mixed = jnp.einsum(
        "td,dc->tc", delta_attention, output_t_full, preferred_element_type=jnp.float32
    )
    delta_mixed = delta_mixed.astype(jnp.bfloat16).reshape(tok_rows, H, DV)
    delta_weights = jnp.einsum(
        "qhd,khd->hqk", delta_mixed, key_rows[..., DN:], preferred_element_type=jnp.float32
    )
    delta_scores = (
        weights_float
        * (delta_weights - jnp.sum(weights_float * delta_weights, axis=-1, keepdims=True))
    ).astype(jnp.bfloat16)
    delta_values = jnp.einsum(
        "hqk,qhd->khd", weights_low, delta_mixed, preferred_element_type=jnp.float32
    )
    delta_query_plain = (
        jnp.einsum(
            "hqk,khd->qhd", delta_scores, key_rows[..., :DN], preferred_element_type=jnp.float32
        )
        * factor
    )
    delta_query_rotary = (
        jnp.einsum("hqk,kr->qhr", delta_scores, rotary_rows, preferred_element_type=jnp.float32)
        * factor
    )
    delta_key_plain = (
        jnp.einsum(
            "hqk,qhd->khd", delta_scores, queries[..., :DN], preferred_element_type=jnp.float32
        )
        * factor
    )
    delta_key_rotary = (
        jnp.einsum(
            "hqk,qhr->kr", delta_scores, queries[..., DN:], preferred_element_type=jnp.float32
        )
        * factor
    )
    delta_key_rows = jnp.concatenate([delta_key_plain, delta_values], axis=-1)
    back_local = jnp.concatenate(
        [delta_key_rows[:tok_rows].reshape(tok_rows, -1), delta_key_rotary[:tok_rows]], axis=1
    ).astype(jnp.bfloat16)
    back_remote = passed_along(back_local, "shard", -1).astype(jnp.float32)
    back_rows = back_remote[:, : H * (DN + DV)].reshape(tok_rows, H, DN + DV)
    back_rotary = back_remote[:, H * (DN + DV) :]
    delta_expanded = (
        (delta_key_rows[tok_rows:] + back_rows)
        .astype(jnp.bfloat16)
        .reshape(tok_rows, H * (DN + DV))
    )
    delta_rotary_total = delta_key_rotary[tok_rows:] + back_rotary
    delta_latent_up = jnp.einsum(
        "tl,tc->lc", latents, delta_expanded, preferred_element_type=jnp.float32
    )
    delta_latent_up_local = scatter_rows(delta_latent_up, experts_all)
    delta_latents = jnp.einsum(
        "tc,lc->tl", delta_expanded, up_full, preferred_element_type=jnp.float32
    )
    _, latent_back = jax.vjp(norm_rows, latent_raw, gain_latent_float)
    delta_latent_raw, delta_gain_latent = latent_back(delta_latents)
    delta_down_out = jnp.concatenate(
        [delta_latent_raw, rotate(delta_rotary_total, cosine_table, -sine_table)], axis=-1
    ).astype(jnp.bfloat16)
    delta_latent_down = jnp.einsum(
        "td,tc->dc", normed_one, delta_down_out, preferred_element_type=jnp.float32
    )
    delta_query_raw = (
        jnp.concatenate(
            [
                delta_query_plain,
                rotate(delta_query_rotary, cosine_table[:, None, :], -sine_table[:, None, :]),
            ],
            axis=-1,
        )
        .astype(jnp.bfloat16)
        .reshape(tok_rows, H * (DN + DR))
    )
    delta_query_weight = jnp.einsum(
        "td,tc->dc", normed_one, delta_query_raw, preferred_element_type=jnp.float32
    )
    delta_normed_one = jnp.einsum(
        "tc,dc->td", delta_query_raw, query_full, preferred_element_type=jnp.float32
    ) + jnp.einsum("tc,dc->td", delta_down_out, down_full, preferred_element_type=jnp.float32)
    _, first_back = jax.vjp(norm_rows, tokens_float, gain_one_float)
    delta_tokens_norm, delta_gain_one = first_back(delta_normed_one)
    input_gradient = (delta_residual + delta_tokens_norm).astype(jnp.bfloat16)

    small_parts = [
        delta_gain_one.reshape(devices, -1),
        delta_gain_latent.reshape(devices, -1),
        delta_gain_two.reshape(devices, -1),
        delta_router.reshape(devices, -1),
        jnp.broadcast_to(square_sums[None], (devices, 3)),
    ]
    small_packed = jnp.concatenate(small_parts, axis=1)
    query_rows = query_weight.shape[0]
    down_size = latent_down.size
    extra = jnp.concatenate([delta_latent_down.reshape(devices, -1), small_packed], axis=1)
    total_rows = query_rows + -(-extra.shape[1] // query_width)
    total_rows = total_rows + (-total_rows) % 8
    extra = jnp.concatenate(
        [
            extra,
            jnp.zeros(
                (devices, (total_rows - query_rows) * query_width - extra.shape[1]), jnp.float32
            ),
        ],
        axis=1,
    ).reshape(devices, total_rows - query_rows, query_width)
    query_blocks = jnp.concatenate(
        [delta_query_weight.reshape(devices, query_rows, query_width), extra], axis=1
    ).reshape(experts_all, shard_count, total_rows, query_width)
    query_out = reduce_over_expert(pair_total(query_blocks))
    delta_query_local = query_out[:query_rows]
    rest = query_out[query_rows:].reshape(-1)
    delta_latent_down_local = rest[:down_size].reshape(latent_down.shape)
    small_sum = rest[down_size:]
    small_cuts = [0]
    for part in small_parts:
        small_cuts.append(small_cuts[-1] + part.shape[1])
    small_pieces = [small_sum[small_cuts[i] : small_cuts[i + 1]] for i in range(len(small_parts))]
    statistics = jnp.sqrt(small_pieces[4] / (tok_rows * D * devices))
    return (
        layer_output,
        input_gradient,
        small_pieces[0],
        delta_query_local,
        delta_latent_down_local,
        small_pieces[1],
        delta_latent_up_local,
        delta_output_local,
        small_pieces[2],
        small_pieces[3].reshape(router_weight.shape),
        delta_shared_inner_local,
        delta_shared_outer_local,
        delta_expert_inner[None],
        delta_expert_outer[None],
        statistics,
    )


def solution(mesh):
    return jax.shard_map(
        shards,
        mesh=mesh,
        in_specs=(
            P(ALL, None),
            P(ALL, None),
            P(ALL, None),
            P(ALL),
            P(ALL, None),
            P(ALL, None),
            P(ALL),
            P(ALL, None),
            P(None, ALL),
            P(ALL),
            P(ALL, None),
            P(None, ALL, None),
            P(None, ALL),
            P("expert", None, None, "shard"),
            P("expert", "shard", None),
        ),
        out_specs=(
            P(ALL, None),
            P(ALL, None),
            P(ALL),
            P(ALL, None),
            P(ALL, None),
            P(ALL),
            P(ALL, None),
            P(None, ALL),
            P(ALL),
            P(ALL, None),
            P(None, ALL, None),
            P(None, ALL),
            P("expert", None, None, "shard"),
            P("expert", "shard", None),
            P(),
        ),
        check_vma=False,
    )
```
